32 devices in a mesh: req: 8 (over z, x), grp: 4 (over y, core).
Axes of the slice: x: 2, y: 2, z: 4, core: 2. Of those that a mesh axis runs over, the one named last changes fastest.
Arguments:
- residual: bfloat16 [8192, 2048], P('req', 'grp'), may hold values from -6 to 6
- queries: bfloat16 [8192, 2048], P('req', 'grp'), may hold values from -26 to 26
- new_keys: bfloat16 [8192, 512], P('req', 'grp'), may hold values from -26 to 26
- new_values: bfloat16 [8192, 512], P('req', 'grp'), may hold values from -6 to 6
- pool_keys: bfloat16 [36864, 512], P('req', 'grp'), may hold values from -6 to 6
- pool_values: bfloat16 [36864, 512], P('req', 'grp'), may hold values from -6 to 6
- cache_len: int32 [64], P('req'), may hold values from 1 to 512, as said below
- prefix_group: int32 [64], P('req'), may hold values from 0 to 7, as said below
- prefix_len: int32 [64], P('req'), may hold values from 0 to 512, as said below
- span_rows: int32 [8], replicated, may hold values from 0 to 1008, as said below
- span_offset: int32 [8], P('req'), may hold values from 0 to 512
- out_weight: bfloat16 [2048, 2048], P('grp'), may hold values from -0.125 to 0.125
- norm_gain: float32 [2048], replicated, may hold values from 0.1 to 1.9
- gate_weight: bfloat16 [2048, 4096], P(None, 'grp'), may hold values from -0.125 to 0.125
- up_weight: bfloat16 [2048, 4096], P(None, 'grp'), may hold values from -0.125 to 0.125
- down_weight: bfloat16 [4096, 2048], P('grp'), may hold values from -0.09375 to 0.09375
Outputs:
- layer_out: bfloat16 [8192, 2048], P('req', 'grp')
The draws below stay inside these ranges and needn't reach their ends.
Inputs may be any that keep to these rules, and one draw needn't show every extreme that they name: `cache_len`: the first decode request of every req index has a cache of 512 positions. `prefix_group`: the slot, within its req index, of the first request of the group; at or before the request's own slot; a group's requests stand in consecutive slots. `prefix_len`: equal within a group and at most the cache length of each of its requests; some request shares 512 positions. `span_rows`: exactly 4 req indices hold a span of 1008 rows, the others none.
All inputs are finite; a program needn't handle non-finite values.
Results may differ from the reference program's by a relative error of at most 0.014.
Values may be sent and summed in bfloat16 or wider, within the bound.
No kernel may reach another device: no remote copies, remote signals or barrier semaphores. Data moves between devices by JAX's collectives and lax.ppermute only.
A program may use at most 128 MiB of HBM per device.

```python
import jax
import jax.numpy as jnp
from jax import lax

D = 2048
HEADS = 32
KV_HEADS = 8
HEAD_DIM = 64
FF = 4096
DEC = 8
REG = 512
CAP = 1024
SPAN = 1008
POOL = 4608
ROWS = 8192
N_REQ = 8
N_GRP = 4


def span_plan(key):
    order = jax.random.permutation(jax.random.fold_in(key, 11), N_REQ)
    counts = jnp.where(order < N_REQ // 2, SPAN, 0).astype(jnp.int32)
    picked = jax.random.randint(jax.random.fold_in(key, 12), (N_REQ,), 0, REG + 1)
    starts = jnp.where(order == 0, REG, picked).astype(jnp.int32)
    return (counts, starts)


def decode_plan(key):
    lengths = jax.random.randint(jax.random.fold_in(key, 21), (N_REQ, DEC), 1, REG + 1)
    lengths = lengths.at[:, 0].set(REG)
    slots = jnp.arange(DEC, dtype=jnp.int32)
    flips = jax.random.randint(jax.random.fold_in(key, 22), (N_REQ, DEC), 0, 2)
    heads_of = (slots[None, :] == 0) | (flips == 1)
    heads_of = heads_of.at[0, DEC - 1].set(True)
    heads_of = heads_of.at[0, 1].set(True)
    leaders = lax.cummax(jnp.where(heads_of, slots[None, :], 0), axis=1).astype(jnp.int32)
    same = leaders[:, :, None] == leaders[:, None, :]
    shortest = jnp.min(jnp.where(same, lengths[:, None, :], REG + 1), axis=2)
    wanted = jax.random.randint(jax.random.fold_in(key, 23), (N_REQ, DEC), 0, REG + 1)
    wanted = wanted.at[0, 0].set(REG)
    lead_want = jnp.take_along_axis(wanted, leaders, axis=1)
    shared = jnp.minimum(lead_want, shortest)
    return (lengths.reshape(-1).astype(jnp.int32), leaders.reshape(-1), shared.reshape(-1).astype(jnp.int32))


def attention_draw(key):
    kv_width = KV_HEADS * HEAD_DIM
    base_q = jax.random.truncated_normal(jax.random.fold_in(key, 31), -4.0, 4.0, (ROWS, D), jnp.float32)
    base_k = jax.random.truncated_normal(jax.random.fold_in(key, 32), -4.0, 4.0, (ROWS, kv_width), jnp.float32)
    keys_out = base_k
    queries_out = base_q
    return (queries_out, keys_out)


def draw_queries(key, part):
    return attention_draw(key)[0].astype(jnp.bfloat16)


def draw_new_keys(key, part):
    return attention_draw(key)[1].astype(jnp.bfloat16)


def draw_cache_len(key, part):
    return decode_plan(key)[0]


def draw_prefix_group(key, part):
    return decode_plan(key)[1]


def draw_prefix_len(key, part):
    return decode_plan(key)[2]


def draw_span_rows(key, part):
    return span_plan(key)[0]


def draw_span_offset(key, part):
    return span_plan(key)[1]


def shard_levels(own_key, extent, pieces, smallest, largest):
    def one(dim, parts):
        heights = jax.random.uniform(jax.random.fold_in(jax.random.fold_in(own_key, 6), dim), (parts,), jnp.float32, smallest / len(pieces), largest / len(pieces))
        return jnp.repeat(jnp.exp(heights), extent[dim] // parts).reshape((-1,) + (1,) * (len(extent) - dim - 1))

    gain = one(*pieces[0])
    for cut in pieces[1:]:
        gain = gain * one(*cut)
    return gain


def bell_draw(rng, shape, spread, reach, shards=(), held_as=jnp.bfloat16):
    gain = shard_levels(rng, shape, shards, -0.22, 0.18) if shards else 1.0
    drawn = jax.random.normal(rng, shape, jnp.float32) * spread * gain
    return jnp.minimum(jnp.maximum(drawn, -reach), reach).astype(held_as)


def setup_inputs(seed: int = 0) -> dict:
    arg_keys = jax.random.split(jax.random.key(seed), 17)
    return {
        "residual": bell_draw(arg_keys[0], (ROWS, D), 1.0, 6.0, ((0, 8), (1, 4))),
        "queries": draw_queries(jax.random.fold_in(arg_keys[16], 71), 0),
        "new_keys": draw_new_keys(jax.random.fold_in(arg_keys[16], 71), 0),
        "new_values": bell_draw(arg_keys[3], (ROWS, KV_HEADS * HEAD_DIM), 1.0, 6.0, ((0, 8), (1, 4))),
        "pool_keys": bell_draw(arg_keys[4], (N_REQ * POOL, KV_HEADS * HEAD_DIM), 1.0, 6.0, ((0, 8), (1, 4))),
        "pool_values": bell_draw(arg_keys[5], (N_REQ * POOL, KV_HEADS * HEAD_DIM), 1.0, 6.0, ((0, 8), (1, 4))),
        "cache_len": draw_cache_len(jax.random.fold_in(arg_keys[16], 71), 0),
        "prefix_group": draw_prefix_group(jax.random.fold_in(arg_keys[16], 71), 0),
        "prefix_len": draw_prefix_len(jax.random.fold_in(arg_keys[16], 71), 0),
        "span_rows": draw_span_rows(jax.random.fold_in(arg_keys[16], 71), 0),
        "span_offset": draw_span_offset(jax.random.fold_in(arg_keys[16], 71), 0),
        "out_weight": bell_draw(arg_keys[11], (D, D), D ** -0.5, 0.125, ((0, 4),)),
        "norm_gain": jnp.clip(1.0 + 0.18 * jax.random.normal(arg_keys[12], (D,), jnp.float32), 0.1, 1.9),
        "gate_weight": bell_draw(arg_keys[13], (D, FF), D ** -0.5, 0.125, ((1, 4),)),
        "up_weight": bell_draw(arg_keys[14], (D, FF), D ** -0.5, 0.125, ((1, 4),)),
        "down_weight": bell_draw(arg_keys[15], (FF, D), FF ** -0.5, 0.09375, ((0, 4),)),
    }


MASKED_SCORE = -1e+30

def attend(query_rows, key_rows, value_rows, allowed):
    scores = jnp.dot(query_rows, key_rows.T, preferred_element_type=jnp.float32) * query_rows.shape[1] ** (-0.5)
    scores = jnp.where(allowed, scores, MASKED_SCORE)
    highest = lax.optimization_barrier(jnp.max(scores, axis=1, keepdims=True))
    expval = jnp.exp(scores - highest)
    totals = lax.optimization_barrier(jnp.sum(expval, axis=1, keepdims=True))
    probs = (expval / totals).astype(jnp.bfloat16)
    return jnp.dot(probs, value_rows, preferred_element_type=jnp.float32).astype(jnp.bfloat16)

def build_masks(cache_len, prefix_group, prefix_len, span_count, span_start, total_rows):
    position = jnp.arange(DEC * REG, dtype=jnp.int32)
    region = position // REG
    offset = position % REG
    request = jnp.arange(DEC, dtype=jnp.int32)
    shared = (region[None, :] == prefix_group[:, None]) & (offset[None, :] < prefix_len[:, None])
    owned = (region[None, :] == request[:, None]) & (offset[None, :] >= prefix_len[:, None]) & (offset[None, :] < cache_len[:, None])
    decode_mask = jnp.concatenate([shared | owned, jnp.eye(DEC, dtype=jnp.bool_)], axis=1)
    span_total = total_rows - DEC
    within = jnp.arange(span_total, dtype=jnp.int32)
    in_span = within < span_count
    earlier = jnp.arange(REG, dtype=jnp.int32)
    prior = (earlier[None, :] < span_start) & in_span[:, None]
    lowest = jnp.where(in_span, 0, within)
    causal = (within[None, :] >= lowest[:, None]) & (within[None, :] <= within[:, None])
    span_mask = jnp.concatenate([prior, causal], axis=1)
    return (decode_mask, span_mask)

def attention(queries, new_keys, new_values, pool_keys, pool_values, decode_mask, span_mask):
    head_count = queries.shape[1] // HEAD_DIM
    per_kv = HEADS // KV_HEADS
    split_at = DEC * REG

    def one_head(head):
        query_rows = lax.dynamic_slice_in_dim(queries, head * HEAD_DIM, HEAD_DIM, 1)
        column = head // per_kv * HEAD_DIM
        fresh_keys = lax.dynamic_slice_in_dim(new_keys, column, HEAD_DIM, 1)
        fresh_values = lax.dynamic_slice_in_dim(new_values, column, HEAD_DIM, 1)
        cached_keys = lax.dynamic_slice_in_dim(pool_keys, column, HEAD_DIM, 1)
        cached_values = lax.dynamic_slice_in_dim(pool_values, column, HEAD_DIM, 1)
        decode_out = attend(query_rows[:DEC], jnp.concatenate([cached_keys[:split_at], fresh_keys[:DEC]], axis=0), jnp.concatenate([cached_values[:split_at], fresh_values[:DEC]], axis=0), decode_mask)
        span_out = attend(query_rows[DEC:], jnp.concatenate([cached_keys[split_at:], fresh_keys[DEC:]], axis=0), jnp.concatenate([cached_values[split_at:], fresh_values[DEC:]], axis=0), span_mask)
        return jnp.concatenate([decode_out, span_out], axis=0)
    outputs = lax.map(one_head, jnp.arange(head_count, dtype=jnp.int32))
    return jnp.transpose(outputs, (1, 0, 2)).reshape(queries.shape[0], head_count * HEAD_DIM)

def grouped_sum(left, right):
    width = left.shape[1] // N_GRP
    total = jnp.zeros((left.shape[0], right.shape[1]), jnp.float32)
    for group in range(N_GRP):
        part = jnp.dot(left[:, group * width:(group + 1) * width], right[group * width:(group + 1) * width], preferred_element_type=jnp.float32).astype(jnp.bfloat16)
        total = total + lax.optimization_barrier(part).astype(jnp.float32)
    return total

def reference(residual, queries, new_keys, new_values, pool_keys, pool_values, cache_len, prefix_group, prefix_len, span_rows, span_offset, out_weight, norm_gain, gate_weight, up_weight, down_weight):

    def per_device(items):
        resid, query_block, key_block, value_block, cached_k, cached_v, lengths, groups, shared_len, span_count, span_start = items
        decode_mask, span_mask = build_masks(lengths, groups, shared_len, span_count, span_start, CAP)
        attn = attention(query_block, key_block, value_block, cached_k, cached_v, decode_mask, span_mask)
        hidden_state = (resid.astype(jnp.float32) + grouped_sum(attn, out_weight)).astype(jnp.bfloat16)
        state32 = hidden_state.astype(jnp.float32)
        normed = (state32 * lax.rsqrt(lax.optimization_barrier(jnp.mean(state32 * state32, axis=1, keepdims=True)) + 1e-05) * norm_gain).astype(jnp.bfloat16)
        gate = jnp.dot(normed, gate_weight, preferred_element_type=jnp.float32)
        upval = jnp.dot(normed, up_weight, preferred_element_type=jnp.float32)
        inner = (jax.nn.silu(gate) * upval).astype(jnp.bfloat16)
        result = (state32 + grouped_sum(inner, down_weight)).astype(jnp.bfloat16)
        is_live = jnp.arange(CAP, dtype=jnp.int32) < DEC + span_count
        return jnp.where(is_live[:, None], result, jnp.zeros((), jnp.bfloat16))
    kv_width = KV_HEADS * HEAD_DIM
    stacked = lax.map(per_device, (residual.reshape(N_REQ, CAP, D), queries.reshape(N_REQ, CAP, D), new_keys.reshape(N_REQ, CAP, kv_width), new_values.reshape(N_REQ, CAP, kv_width), pool_keys.reshape(N_REQ, POOL, kv_width), pool_values.reshape(N_REQ, POOL, kv_width), cache_len.reshape(N_REQ, DEC), prefix_group.reshape(N_REQ, DEC), prefix_len.reshape(N_REQ, DEC), span_rows, span_offset))
    return stacked.reshape(ROWS, D)
```

```python
import jax
import jax.numpy as jnp
from jax import lax
from jax.experimental import pallas as pl
from jax.experimental.pallas import tpu as pltpu
from jax.sharding import PartitionSpec as P

HEADS = 32
KV_HEADS = 8
HEAD_DIM = 64
DEC = 8
BAL = 512
REG = 512


MASKED_SCORE = -1e30


SCALE = HEAD_DIM ** (-0.5)
QBLK = 256


def span_kernel(start_ref, q_ref, kp_ref, vp_ref, kf_ref, vf_ref, o_ref):
    span_start = start_ref[0]
    q_all = q_ref[0]
    kp = kp_ref[0]
    vp = vp_ref[0]
    rows = q_all.shape[0]
    prior = kp.shape[0]
    for blk in range(rows // QBLK):
        lo = blk * QBLK
        hi = lo + QBLK
        q = q_all[lo:hi]
        kf = kf_ref[0, 0:hi]
        vf = vf_ref[0, 0:hi]
        s_p = lax.dot_general(
            q, kp, (((1,), (1,)), ((), ())), preferred_element_type=jnp.float32
        ) * SCALE
        s_f = lax.dot_general(
            q, kf, (((1,), (1,)), ((), ())), preferred_element_type=jnp.float32
        ) * SCALE
        t_p = lax.broadcasted_iota(jnp.int32, (QBLK, prior), 1)
        s_p = jnp.where(t_p < span_start, s_p, MASKED_SCORE)
        q_pos = lax.broadcasted_iota(jnp.int32, (QBLK, hi), 0) + lo
        k_pos = lax.broadcasted_iota(jnp.int32, (QBLK, hi), 1)
        seen = (k_pos >= DEC) & (k_pos <= q_pos)
        s_f = jnp.where(seen, s_f, MASKED_SCORE)
        highest = jnp.maximum(
            jnp.max(s_p, axis=1, keepdims=True), jnp.max(s_f, axis=1, keepdims=True)
        )
        e_p = jnp.exp(s_p - highest)
        e_f = jnp.exp(s_f - highest)
        totals = jnp.sum(e_p, axis=1, keepdims=True) + jnp.sum(e_f, axis=1, keepdims=True)
        p_p = (e_p / totals).astype(jnp.bfloat16)
        p_f = (e_f / totals).astype(jnp.bfloat16)
        out = jnp.dot(p_p, vp, preferred_element_type=jnp.float32) + jnp.dot(
            p_f, vf, preferred_element_type=jnp.float32
        )
        o_ref[0, lo:hi, :] = out.astype(o_ref.dtype)


def span_attention(q_heads, kp_heads, vp_heads, kf_heads, vf_heads, span_start):
    heads, rows, dim = q_heads.shape
    prior = kp_heads.shape[1]
    per_kv = heads // kp_heads.shape[0]
    q_spec = pl.BlockSpec((1, rows, dim), lambda h, s: (h, 0, 0))
    p_spec = pl.BlockSpec((1, prior, dim), lambda h, s: (h // per_kv, 0, 0))
    f_spec = pl.BlockSpec((1, rows, dim), lambda h, s: (h // per_kv, 0, 0))
    flops = 4 * heads * rows * (prior + rows // 2) * dim
    cost = pl.CostEstimate(
        flops=flops,
        transcendentals=heads * rows * (prior + rows // 2),
        bytes_accessed=2 * (2 * heads * rows * dim + 4 * (prior + rows) * dim),
    )
    return pl.pallas_call(
        span_kernel,
        out_shape=jax.ShapeDtypeStruct((heads, rows, dim), jnp.bfloat16),
        grid_spec=pltpu.PrefetchScalarGridSpec(
            num_scalar_prefetch=1,
            grid=(heads,),
            in_specs=[q_spec, p_spec, p_spec, f_spec, f_spec],
            out_specs=q_spec,
        ),
        cost_estimate=cost,
    )(span_start.reshape(1).astype(jnp.int32), q_heads, kp_heads, vp_heads, kf_heads, vf_heads)


def decode_attention(queries, new_keys, new_values, pool_keys, pool_values, decode_mask):
    kv = new_keys.shape[1] // HEAD_DIM
    per_kv = queries.shape[1] // HEAD_DIM // kv
    cached = DEC * REG
    q = queries[:DEC].reshape(DEC, kv, per_kv, HEAD_DIM)
    kc = pool_keys[:cached].reshape(cached, kv, HEAD_DIM)
    vc = pool_values[:cached].reshape(cached, kv, HEAD_DIM)
    kn = new_keys[:DEC].reshape(DEC, kv, HEAD_DIM)
    vn = new_values[:DEC].reshape(DEC, kv, HEAD_DIM)
    s_c = jnp.einsum("rjhd,tjd->rjht", q, kc, preferred_element_type=jnp.float32) * SCALE
    s_n = jnp.einsum("rjhd,tjd->rjht", q, kn, preferred_element_type=jnp.float32) * SCALE
    s_c = jnp.where(decode_mask[:, None, None, :cached], s_c, MASKED_SCORE)
    s_n = jnp.where(decode_mask[:, None, None, cached:], s_n, MASKED_SCORE)
    highest = jnp.maximum(
        jnp.max(s_c, axis=3, keepdims=True), jnp.max(s_n, axis=3, keepdims=True)
    )
    e_c = jnp.exp(s_c - highest)
    e_n = jnp.exp(s_n - highest)
    totals = jnp.sum(e_c, axis=3, keepdims=True) + jnp.sum(e_n, axis=3, keepdims=True)
    p_c = (e_c / totals).astype(jnp.bfloat16)
    p_n = (e_n / totals).astype(jnp.bfloat16)
    out = jnp.einsum("rjht,tjd->rjhd", p_c, vc, preferred_element_type=jnp.float32) + jnp.einsum(
        "rjht,tjd->rjhd", p_n, vn, preferred_element_type=jnp.float32
    )
    return out.astype(jnp.bfloat16).reshape(DEC, kv * per_kv * HEAD_DIM)


def build_decode_mask(cache_len, prefix_group, prefix_len):
    position = jnp.arange(DEC * REG, dtype=jnp.int32)
    region = position // REG
    offset = position % REG
    request = jnp.arange(DEC, dtype=jnp.int32)
    shared = (region[None, :] == prefix_group[:, None]) & (offset[None, :] < prefix_len[:, None])
    owned = (
        (region[None, :] == request[:, None])
        & (offset[None, :] >= prefix_len[:, None])
        & (offset[None, :] < cache_len[:, None])
    )
    return jnp.concatenate([shared | owned, jnp.eye(DEC, dtype=jnp.bool_)], axis=1)


def attention(queries, new_keys, new_values, pool_keys, pool_values, decode_mask, span_start):
    rows = queries.shape[0]
    heads = queries.shape[1] // HEAD_DIM
    kv = new_keys.shape[1] // HEAD_DIM
    cached = DEC * REG

    def head_major(x, n):
        return jnp.transpose(x.reshape(x.shape[0], n, HEAD_DIM), (1, 0, 2))

    span_heads = span_attention(
        head_major(queries, heads),
        head_major(pool_keys[cached:], kv),
        head_major(pool_values[cached:], kv),
        head_major(new_keys, kv),
        head_major(new_values, kv),
        span_start,
    )
    span_rows = jnp.transpose(span_heads, (1, 0, 2)).reshape(rows, heads * HEAD_DIM)
    decode_rows = decode_attention(
        queries, new_keys, new_values, pool_keys, pool_values, decode_mask
    )
    return jnp.concatenate([decode_rows, span_rows[DEC:]], axis=0)


def finish(attn_rows, resid_rows, out_weight, norm_gain, gate_weight, up_weight, down_weight):
    partial_value = jnp.dot(attn_rows, out_weight, preferred_element_type=jnp.float32)
    proj_cols = lax.psum_scatter(
        partial_value.astype(jnp.bfloat16), "grp", scatter_dimension=1, tiled=True
    ).astype(jnp.float32)
    state_cols = (resid_rows.astype(jnp.float32) + proj_cols).astype(jnp.bfloat16)
    state_full = lax.all_gather(state_cols, "grp", axis=1, tiled=True)
    state32 = state_full.astype(jnp.float32)
    normed = (
        state32 * lax.rsqrt(jnp.mean(state32 * state32, axis=1, keepdims=True) + 1e-05) * norm_gain
    ).astype(jnp.bfloat16)
    gate = jnp.dot(normed, gate_weight, preferred_element_type=jnp.float32)
    upval = jnp.dot(normed, up_weight, preferred_element_type=jnp.float32)
    inner = (jax.nn.silu(gate) * upval).astype(jnp.bfloat16)
    down_cols = lax.psum_scatter(
        jnp.dot(inner, down_weight, preferred_element_type=jnp.float32).astype(jnp.bfloat16),
        "grp",
        scatter_dimension=1,
        tiled=True,
    ).astype(jnp.float32)
    return (state_cols.astype(jnp.float32) + down_cols).astype(jnp.bfloat16)


def shards(
    residual,
    queries,
    new_keys,
    new_values,
    pool_keys,
    pool_values,
    cache_len,
    prefix_group,
    prefix_len,
    span_rows,
    span_offset,
    out_weight,
    norm_gain,
    gate_weight,
    up_weight,
    down_weight,
):
    total_rows = residual.shape[0]
    width = residual.shape[1]
    device = lax.axis_index("req")
    devices = lax.axis_size("req")
    own_span = span_rows[device]
    decode_mask = build_decode_mask(cache_len, prefix_group, prefix_len)
    attn = attention(
        queries, new_keys, new_values, pool_keys, pool_values, decode_mask, span_offset[0]
    )
    row_index = jnp.arange(total_rows, dtype=jnp.int32)
    is_live = row_index < DEC + own_span
    zero_value = jnp.zeros((), jnp.bfloat16)
    counts = DEC + span_rows
    first = jnp.sum(jnp.where(jnp.arange(devices, dtype=jnp.int32) < device, counts, 0))
    target = jnp.where(is_live, first + row_index, -1)
    bucket = (total_rows - DEC + devices - 1) // devices
    owner_dev = jnp.where(is_live, target % devices, devices)
    bucket_pos = jnp.where(is_live, row_index // devices, 0)
    send_attn = (
        jnp.zeros((devices, bucket, width), jnp.bfloat16)
        .at[owner_dev, bucket_pos]
        .set(attn, mode="drop")
    )
    send_resid = (
        jnp.zeros((devices, bucket, width), jnp.bfloat16)
        .at[owner_dev, bucket_pos]
        .set(residual, mode="drop")
    )
    send_target = (
        jnp.full((devices, bucket), -1, jnp.int32)
        .at[owner_dev, bucket_pos]
        .set(target, mode="drop")
    )
    got_attn, got_resid, got_target = (
        lax.all_to_all(send_attn, "req", split_axis=0, concat_axis=0, tiled=True),
        lax.all_to_all(send_resid, "req", split_axis=0, concat_axis=0, tiled=True),
        lax.all_to_all(send_target, "req", split_axis=0, concat_axis=0, tiled=True),
    )
    flat_target = got_target.reshape(-1)
    has_row = flat_target >= 0
    bal_slot = jnp.where(has_row, flat_target // devices, BAL)
    dense_attn = (
        jnp.zeros((BAL, width), jnp.bfloat16)
        .at[bal_slot]
        .set(got_attn.reshape(-1, width), mode="drop")
    )
    dense_resid = (
        jnp.zeros((BAL, width), jnp.bfloat16)
        .at[bal_slot]
        .set(got_resid.reshape(-1, width), mode="drop")
    )
    mixed = finish(
        dense_attn, dense_resid, out_weight, norm_gain, gate_weight, up_weight, down_weight
    )
    picked = jnp.where(has_row[:, None], mixed[jnp.minimum(bal_slot, BAL - 1)], zero_value)
    returned = lax.all_to_all(
        picked.reshape(devices, bucket, width), "req", split_axis=0, concat_axis=0, tiled=True
    )
    layer_out = jnp.where(
        is_live[:, None], returned[jnp.minimum(owner_dev, devices - 1), bucket_pos], zero_value
    )
    return layer_out


def solution(mesh):
    placed = (
        P("req", "grp"),
        P("req", "grp"),
        P("req", "grp"),
        P("req", "grp"),
        P("req", "grp"),
        P("req", "grp"),
        P("req"),
        P("req"),
        P("req"),
        P(),
        P("req"),
        P("grp", None),
        P(),
        P(None, "grp"),
        P(None, "grp"),
        P("grp", None),
    )
    return jax.shard_map(
        shards, mesh=mesh, in_specs=placed, out_specs=P("req", "grp"), check_vma=False
    )
```

```python
import jax
import jax.numpy as jnp
from jax import lax
from jax.experimental import pallas as pl
from jax.experimental.pallas import tpu as pltpu
from jax.sharding import PartitionSpec as P

HEADS = 32
KV_HEADS = 8
HEAD_DIM = 64
DEC = 8
REG = 512


MASKED_SCORE = -1e30


SCALE = HEAD_DIM ** (-0.5)
QBLK = 256


def span_kernel(start_ref, q_ref, kp_ref, vp_ref, kf_ref, vf_ref, o_ref):
    span_start = start_ref[0]
    first_kv = (pl.program_id(0) * 2 // (HEADS // KV_HEADS)) % 2 == 0
    half = HEAD_DIM

    def pick(ref, lo, hi):
        return jnp.where(first_kv, ref[lo:hi, 0:half], ref[lo:hi, half : 2 * half])

    rows = q_ref.shape[0]
    prior = kp_ref.shape[0]
    kp = pick(kp_ref, 0, prior)
    vp = pick(vp_ref, 0, prior)
    for blk in range(rows // QBLK):
        lo = blk * QBLK
        hi = lo + QBLK
        kf = pick(kf_ref, 0, hi)
        vf = pick(vf_ref, 0, hi)
        t_p = lax.broadcasted_iota(jnp.int32, (QBLK, prior), 1)
        prior_seen = t_p < span_start
        q_pos = lax.broadcasted_iota(jnp.int32, (QBLK, hi), 0) + lo
        k_pos = lax.broadcasted_iota(jnp.int32, (QBLK, hi), 1)
        seen = (k_pos >= DEC) & (k_pos <= q_pos)
        for hh in range(2):
            q = q_ref[lo:hi, hh * half : (hh + 1) * half]
            s_p = lax.dot_general(
                q, kp, (((1,), (1,)), ((), ())), preferred_element_type=jnp.float32
            ) * SCALE
            s_f = lax.dot_general(
                q, kf, (((1,), (1,)), ((), ())), preferred_element_type=jnp.float32
            ) * SCALE
            s_p = jnp.where(prior_seen, s_p, MASKED_SCORE)
            s_f = jnp.where(seen, s_f, MASKED_SCORE)
            highest = jnp.maximum(
                jnp.max(s_p, axis=1, keepdims=True), jnp.max(s_f, axis=1, keepdims=True)
            )
            e_p = jnp.exp(s_p - highest)
            e_f = jnp.exp(s_f - highest)
            totals = jnp.sum(e_p, axis=1, keepdims=True) + jnp.sum(e_f, axis=1, keepdims=True)
            p_p = (e_p / totals).astype(jnp.bfloat16)
            p_f = (e_f / totals).astype(jnp.bfloat16)
            out = jnp.dot(p_p, vp, preferred_element_type=jnp.float32) + jnp.dot(
                p_f, vf, preferred_element_type=jnp.float32
            )
            o_ref[lo:hi, hh * half : (hh + 1) * half] = out.astype(o_ref.dtype)


def span_attention(queries, pool_keys, pool_values, new_keys, new_values, span_start, cached):
    rows, width = queries.shape
    kv_width = new_keys.shape[1]
    prior = REG
    lanes = 2 * HEAD_DIM
    heads = width // HEAD_DIM
    q_spec = pl.BlockSpec((rows, lanes), lambda c, s: (0, c))
    p_spec = pl.BlockSpec((prior, kv_width), lambda c, s: (cached // prior, 0))
    f_spec = pl.BlockSpec((rows, kv_width), lambda c, s: (0, 0))
    flops = 4 * heads * rows * (prior + rows // 2) * HEAD_DIM
    cost = pl.CostEstimate(
        flops=flops,
        transcendentals=heads * rows * (prior + rows // 2),
        bytes_accessed=2 * (2 * rows * width + 2 * (prior + rows) * kv_width),
    )
    return pl.pallas_call(
        span_kernel,
        out_shape=jax.ShapeDtypeStruct((rows, width), jnp.bfloat16),
        grid_spec=pltpu.PrefetchScalarGridSpec(
            num_scalar_prefetch=1,
            grid=(width // lanes,),
            in_specs=[q_spec, p_spec, p_spec, f_spec, f_spec],
            out_specs=q_spec,
        ),
        cost_estimate=cost,
    )(span_start.reshape(1).astype(jnp.int32), queries, pool_keys, pool_values, new_keys, new_values)


def decode_attention(queries, new_keys, new_values, pool_keys, pool_values, decode_mask):
    kv = new_keys.shape[1] // HEAD_DIM
    per_kv = queries.shape[1] // HEAD_DIM // kv
    cached = DEC * REG
    q = queries[:DEC].reshape(DEC, kv, per_kv, HEAD_DIM)
    kc = pool_keys[:cached].reshape(cached, kv, HEAD_DIM)
    vc = pool_values[:cached].reshape(cached, kv, HEAD_DIM)
    kn = new_keys[:DEC].reshape(DEC, kv, HEAD_DIM)
    vn = new_values[:DEC].reshape(DEC, kv, HEAD_DIM)
    s_c = jnp.einsum("rjhd,tjd->rjht", q, kc, preferred_element_type=jnp.float32) * SCALE
    s_n = jnp.einsum("rjhd,tjd->rjht", q, kn, preferred_element_type=jnp.float32) * SCALE
    s_c = jnp.where(decode_mask[:, None, None, :cached], s_c, MASKED_SCORE)
    s_n = jnp.where(decode_mask[:, None, None, cached:], s_n, MASKED_SCORE)
    highest = jnp.maximum(
        jnp.max(s_c, axis=3, keepdims=True), jnp.max(s_n, axis=3, keepdims=True)
    )
    e_c = jnp.exp(s_c - highest)
    e_n = jnp.exp(s_n - highest)
    totals = jnp.sum(e_c, axis=3, keepdims=True) + jnp.sum(e_n, axis=3, keepdims=True)
    p_c = (e_c / totals).astype(jnp.bfloat16)
    p_n = (e_n / totals).astype(jnp.bfloat16)
    out = jnp.einsum("rjht,tjd->rjhd", p_c, vc, preferred_element_type=jnp.float32) + jnp.einsum(
        "rjht,tjd->rjhd", p_n, vn, preferred_element_type=jnp.float32
    )
    return out.astype(jnp.bfloat16).reshape(DEC, kv * per_kv * HEAD_DIM)


def build_decode_mask(cache_len, prefix_group, prefix_len):
    position = jnp.arange(DEC * REG, dtype=jnp.int32)
    region = position // REG
    offset = position % REG
    request = jnp.arange(DEC, dtype=jnp.int32)
    shared = (region[None, :] == prefix_group[:, None]) & (offset[None, :] < prefix_len[:, None])
    owned = (
        (region[None, :] == request[:, None])
        & (offset[None, :] >= prefix_len[:, None])
        & (offset[None, :] < cache_len[:, None])
    )
    return jnp.concatenate([shared | owned, jnp.eye(DEC, dtype=jnp.bool_)], axis=1)


def attention(queries, new_keys, new_values, pool_keys, pool_values, decode_mask, span_start):
    cached = DEC * REG
    span_rows = span_attention(
        queries, pool_keys, pool_values, new_keys, new_values, span_start, cached
    )
    decode_rows = decode_attention(
        queries, new_keys, new_values, pool_keys, pool_values, decode_mask
    )
    return lax.dynamic_update_slice(span_rows, decode_rows, (0, 0))


def finish(attn_rows, resid_rows, out_weight, norm_gain, gate_weight, up_weight, down_weight):
    partial_value = jnp.dot(attn_rows, out_weight, preferred_element_type=jnp.float32)
    proj_cols = lax.psum_scatter(
        partial_value.astype(jnp.bfloat16), "grp", scatter_dimension=1, tiled=True
    ).astype(jnp.float32)
    state_cols = (resid_rows.astype(jnp.float32) + proj_cols).astype(jnp.bfloat16)
    state_full = lax.all_gather(state_cols, "grp", axis=1, tiled=True)
    state32 = state_full.astype(jnp.float32)
    normed = (
        state32 * lax.rsqrt(jnp.mean(state32 * state32, axis=1, keepdims=True) + 1e-05) * norm_gain
    ).astype(jnp.bfloat16)
    gate = jnp.dot(normed, gate_weight, preferred_element_type=jnp.float32)
    upval = jnp.dot(normed, up_weight, preferred_element_type=jnp.float32)
    inner = (jax.nn.silu(gate) * upval).astype(jnp.bfloat16)
    down_cols = lax.psum_scatter(
        jnp.dot(inner, down_weight, preferred_element_type=jnp.float32).astype(jnp.bfloat16),
        "grp",
        scatter_dimension=1,
        tiled=True,
    ).astype(jnp.float32)
    return (state_cols.astype(jnp.float32) + down_cols).astype(jnp.bfloat16)


def shards(
    residual,
    queries,
    new_keys,
    new_values,
    pool_keys,
    pool_values,
    cache_len,
    prefix_group,
    prefix_len,
    span_rows,
    span_offset,
    out_weight,
    norm_gain,
    gate_weight,
    up_weight,
    down_weight,
):
    total_rows = residual.shape[0]
    width = residual.shape[1]
    device = lax.axis_index("req")
    devices = lax.axis_size("req")
    bucket = (total_rows - DEC + devices - 1) // devices
    spread = bucket * devices
    bal = total_rows // 2
    counts = DEC + span_rows
    ends = jnp.cumsum(counts)
    firsts = ends - counts
    first = firsts[device]
    own_count = counts[device]
    shift = first % devices

    def outbound(rows):
        grid = rows[:spread].reshape(bucket, devices, rows.shape[1])
        return jnp.transpose(jnp.roll(grid, shift, axis=1), (1, 0, 2))

    send_resid = outbound(residual)
    got_resid = lax.all_to_all(send_resid, "req", split_axis=0, concat_axis=0, tiled=True)
    decode_mask = build_decode_mask(cache_len, prefix_group, prefix_len)
    attn = attention(
        queries, new_keys, new_values, pool_keys, pool_values, decode_mask, span_offset[0]
    )
    got_attn = lax.all_to_all(outbound(attn), "req", split_axis=0, concat_axis=0, tiled=True)

    slots = jnp.arange(bal, dtype=jnp.int32)
    wanted = slots * devices + device
    src_dev = jnp.sum((ends[None, :] <= wanted[:, None]).astype(jnp.int32), axis=1)
    src_dev = jnp.minimum(src_dev, devices - 1)
    src_pos = jnp.clip((wanted - firsts[src_dev]) // devices, 0, bucket - 1)
    flat_idx = src_dev * bucket + src_pos
    dense_attn = got_attn.reshape(spread, width)[flat_idx]
    dense_resid = got_resid.reshape(spread, width)[flat_idx]
    mixed = finish(
        dense_attn, dense_resid, out_weight, norm_gain, gate_weight, up_weight, down_weight
    )
    lane = (device - firsts) % devices
    row_of = jnp.arange(bucket, dtype=jnp.int32)[None, :] * devices + lane[:, None]
    back_valid = row_of < counts[:, None]
    back_slot = jnp.clip((firsts[:, None] + row_of) // devices, 0, bal - 1)
    picked = jnp.where(
        back_valid[:, :, None], mixed[back_slot.reshape(-1)].reshape(devices, bucket, width), 0
    ).astype(jnp.bfloat16)
    returned = lax.all_to_all(picked, "req", split_axis=0, concat_axis=0, tiled=True)
    restored = jnp.roll(jnp.transpose(returned, (1, 0, 2)), -shift, axis=1).reshape(spread, width)
    if spread < total_rows:
        restored = jnp.concatenate(
            [restored, jnp.zeros((total_rows - spread, width), restored.dtype)], axis=0
        )
    is_live = jnp.arange(total_rows, dtype=jnp.int32) < own_count
    return jnp.where(is_live[:, None], restored, jnp.zeros((), jnp.bfloat16))


def solution(mesh):
    placed = (
        P("req", "grp"),
        P("req", "grp"),
        P("req", "grp"),
        P("req", "grp"),
        P("req", "grp"),
        P("req", "grp"),
        P("req"),
        P("req"),
        P("req"),
        P(),
        P("req"),
        P("grp", None),
        P(),
        P(None, "grp"),
        P(None, "grp"),
        P("grp", None),
    )
    return jax.shard_map(
        shards, mesh=mesh, in_specs=placed, out_specs=P("req", "grp"), check_vma=False
    )
```

```python
import jax
import jax.numpy as jnp
from jax import lax
from jax.experimental import pallas as pl
from jax.experimental.pallas import tpu as pltpu
from jax.sharding import PartitionSpec as P

HEADS = 32
KV_HEADS = 8
HEAD_DIM = 64
DEC = 8
REG = 512


MASKED_SCORE = -1e30


SCALE = HEAD_DIM ** (-0.5)
QBLK = 256


def span_kernel(start_ref, q_ref, kp_ref, vp_ref, kf_ref, vf_ref, o_ref):
    span_start = start_ref[0]
    first_kv = (pl.program_id(0) * 2 // (HEADS // KV_HEADS)) % 2 == 0
    half = HEAD_DIM

    def pick(ref, lo, hi):
        return jnp.where(first_kv, ref[lo:hi, 0:half], ref[lo:hi, half : 2 * half])

    rows = q_ref.shape[0]
    prior = kp_ref.shape[0]
    kp = pick(kp_ref, 0, prior)
    vp = pick(vp_ref, 0, prior)
    for blk in range(rows // QBLK):
        lo = blk * QBLK
        hi = lo + QBLK
        kf = pick(kf_ref, 0, hi)
        vf = pick(vf_ref, 0, hi)
        t_p = lax.broadcasted_iota(jnp.int32, (QBLK, prior), 1)
        prior_seen = t_p < span_start
        q_pos = lax.broadcasted_iota(jnp.int32, (QBLK, hi), 0) + lo
        k_pos = lax.broadcasted_iota(jnp.int32, (QBLK, hi), 1)
        seen = (k_pos >= DEC) & (k_pos <= q_pos)
        for hh in range(2):
            q = q_ref[lo:hi, hh * half : (hh + 1) * half]
            s_p = lax.dot_general(
                q, kp, (((1,), (1,)), ((), ())), preferred_element_type=jnp.float32
            ) * SCALE
            s_f = lax.dot_general(
                q, kf, (((1,), (1,)), ((), ())), preferred_element_type=jnp.float32
            ) * SCALE
            s_p = jnp.where(prior_seen, s_p, MASKED_SCORE)
            s_f = jnp.where(seen, s_f, MASKED_SCORE)
            highest = jnp.maximum(
                jnp.max(s_p, axis=1, keepdims=True), jnp.max(s_f, axis=1, keepdims=True)
            )
            e_p = jnp.exp(s_p - highest)
            e_f = jnp.exp(s_f - highest)
            totals = jnp.sum(e_p, axis=1, keepdims=True) + jnp.sum(e_f, axis=1, keepdims=True)
            p_p = (e_p / totals).astype(jnp.bfloat16)
            p_f = (e_f / totals).astype(jnp.bfloat16)
            out = jnp.dot(p_p, vp, preferred_element_type=jnp.float32) + jnp.dot(
                p_f, vf, preferred_element_type=jnp.float32
            )
            o_ref[lo:hi, hh * half : (hh + 1) * half] = out.astype(o_ref.dtype)


def span_attention(queries, pool_keys, pool_values, new_keys, new_values, span_start, cached):
    rows, width = queries.shape
    kv_width = new_keys.shape[1]
    prior = REG
    lanes = 2 * HEAD_DIM
    heads = width // HEAD_DIM
    q_spec = pl.BlockSpec((rows, lanes), lambda c, s: (0, c))
    p_spec = pl.BlockSpec((prior, kv_width), lambda c, s: (cached // prior, 0))
    f_spec = pl.BlockSpec((rows, kv_width), lambda c, s: (0, 0))
    flops = 4 * heads * rows * (prior + rows // 2) * HEAD_DIM
    cost = pl.CostEstimate(
        flops=flops,
        transcendentals=heads * rows * (prior + rows // 2),
        bytes_accessed=2 * (2 * rows * width + 2 * (prior + rows) * kv_width),
    )
    return pl.pallas_call(
        span_kernel,
        out_shape=jax.ShapeDtypeStruct((rows, width), jnp.bfloat16),
        grid_spec=pltpu.PrefetchScalarGridSpec(
            num_scalar_prefetch=1,
            grid=(width // lanes,),
            in_specs=[q_spec, p_spec, p_spec, f_spec, f_spec],
            out_specs=q_spec,
        ),
        cost_estimate=cost,
    )(span_start.reshape(1).astype(jnp.int32), queries, pool_keys, pool_values, new_keys, new_values)


def decode_attention(queries, new_keys, new_values, pool_keys, pool_values, decode_mask):
    kv = new_keys.shape[1] // HEAD_DIM
    per_kv = queries.shape[1] // HEAD_DIM // kv
    cached = DEC * REG
    q = queries[:DEC].reshape(DEC, kv, per_kv, HEAD_DIM)
    kc = pool_keys[:cached].reshape(cached, kv, HEAD_DIM)
    vc = pool_values[:cached].reshape(cached, kv, HEAD_DIM)
    kn = new_keys[:DEC].reshape(DEC, kv, HEAD_DIM)
    vn = new_values[:DEC].reshape(DEC, kv, HEAD_DIM)
    s_c = jnp.einsum("rjhd,tjd->rjht", q, kc, preferred_element_type=jnp.float32) * SCALE
    s_n = jnp.einsum("rjhd,tjd->rjht", q, kn, preferred_element_type=jnp.float32) * SCALE
    s_c = jnp.where(decode_mask[:, None, None, :cached], s_c, MASKED_SCORE)
    s_n = jnp.where(decode_mask[:, None, None, cached:], s_n, MASKED_SCORE)
    highest = jnp.maximum(
        jnp.max(s_c, axis=3, keepdims=True), jnp.max(s_n, axis=3, keepdims=True)
    )
    e_c = jnp.exp(s_c - highest)
    e_n = jnp.exp(s_n - highest)
    totals = jnp.sum(e_c, axis=3, keepdims=True) + jnp.sum(e_n, axis=3, keepdims=True)
    p_c = (e_c / totals).astype(jnp.bfloat16)
    p_n = (e_n / totals).astype(jnp.bfloat16)
    out = jnp.einsum("rjht,tjd->rjhd", p_c, vc, preferred_element_type=jnp.float32) + jnp.einsum(
        "rjht,tjd->rjhd", p_n, vn, preferred_element_type=jnp.float32
    )
    return out.astype(jnp.bfloat16).reshape(DEC, kv * per_kv * HEAD_DIM)


def build_decode_mask(cache_len, prefix_group, prefix_len):
    position = jnp.arange(DEC * REG, dtype=jnp.int32)
    region = position // REG
    offset = position % REG
    request = jnp.arange(DEC, dtype=jnp.int32)
    shared = (region[None, :] == prefix_group[:, None]) & (offset[None, :] < prefix_len[:, None])
    owned = (
        (region[None, :] == request[:, None])
        & (offset[None, :] >= prefix_len[:, None])
        & (offset[None, :] < cache_len[:, None])
    )
    return jnp.concatenate([shared | owned, jnp.eye(DEC, dtype=jnp.bool_)], axis=1)


def attention(queries, new_keys, new_values, pool_keys, pool_values, decode_mask, span_start):
    cached = DEC * REG
    span_rows = span_attention(
        queries, pool_keys, pool_values, new_keys, new_values, span_start, cached
    )
    decode_rows = decode_attention(
        queries, new_keys, new_values, pool_keys, pool_values, decode_mask
    )
    return lax.dynamic_update_slice(span_rows, decode_rows, (0, 0))


def grp_block(x, index, width):
    return lax.dynamic_slice_in_dim(x, index * width, width, 1)


def grp_reduce_scatter(partial):
    parts = lax.axis_size("grp")
    width = partial.shape[1] // parts
    if parts != 4:
        return lax.psum_scatter(partial, "grp", scatter_dimension=1, tiled=True).astype(
            jnp.float32
        )
    me = lax.axis_index("grp")
    near = [(i, i ^ 1) for i in range(parts)]
    far = [(i, i ^ 2) for i in range(parts)]
    outgoing = jnp.stack([grp_block(partial, me ^ 1, width), grp_block(partial, me ^ 3, width)])
    incoming = lax.ppermute(outgoing, "grp", near)
    own = grp_block(partial, me, width).astype(jnp.float32) + incoming[0].astype(jnp.float32)
    other = grp_block(partial, me ^ 2, width).astype(jnp.float32) + incoming[1].astype(
        jnp.float32
    )
    arrived = lax.ppermute(other.astype(jnp.bfloat16), "grp", far)
    return own + arrived.astype(jnp.float32)


def grp_all_gather(block):
    parts = lax.axis_size("grp")
    if parts != 4:
        return lax.all_gather(block, "grp", axis=1, tiled=True)
    me = lax.axis_index("grp")
    near = [(i, i ^ 1) for i in range(parts)]
    far = [(i, i ^ 2) for i in range(parts)]
    across = lax.ppermute(block, "grp", far)
    pair = lax.ppermute(jnp.stack([block, across]), "grp", near)
    held = jnp.stack([block, pair[0], across, pair[1]])
    pieces = [lax.dynamic_index_in_dim(held, k ^ me, 0, keepdims=False) for k in range(parts)]
    return jnp.concatenate(pieces, axis=1)


def finish(attn_rows, resid_rows, out_weight, norm_gain, gate_weight, up_weight, down_weight):
    partial_value = jnp.dot(attn_rows, out_weight, preferred_element_type=jnp.float32)
    proj_cols = grp_reduce_scatter(partial_value.astype(jnp.bfloat16))
    state_cols = (resid_rows.astype(jnp.float32) + proj_cols).astype(jnp.bfloat16)
    state_full = grp_all_gather(state_cols)
    state32 = state_full.astype(jnp.float32)
    normed = (
        state32 * lax.rsqrt(jnp.mean(state32 * state32, axis=1, keepdims=True) + 1e-05) * norm_gain
    ).astype(jnp.bfloat16)
    gate = jnp.dot(normed, gate_weight, preferred_element_type=jnp.float32)
    upval = jnp.dot(normed, up_weight, preferred_element_type=jnp.float32)
    inner = (jax.nn.silu(gate) * upval).astype(jnp.bfloat16)
    down_cols = grp_reduce_scatter(
        jnp.dot(inner, down_weight, preferred_element_type=jnp.float32).astype(jnp.bfloat16)
    )
    return (state_cols.astype(jnp.float32) + down_cols).astype(jnp.bfloat16)


def shards(
    residual,
    queries,
    new_keys,
    new_values,
    pool_keys,
    pool_values,
    cache_len,
    prefix_group,
    prefix_len,
    span_rows,
    span_offset,
    out_weight,
    norm_gain,
    gate_weight,
    up_weight,
    down_weight,
):
    total_rows = residual.shape[0]
    width = residual.shape[1]
    device = lax.axis_index("req")
    devices = lax.axis_size("req")
    bucket = (total_rows - DEC + devices - 1) // devices
    spread = bucket * devices
    bal = total_rows // 2
    counts = DEC + span_rows
    ends = jnp.cumsum(counts)
    firsts = ends - counts
    first = firsts[device]
    own_count = counts[device]
    shift = first % devices

    def outbound(rows):
        grid = rows[:spread].reshape(bucket, devices, rows.shape[1])
        return jnp.transpose(jnp.roll(grid, shift, axis=1), (1, 0, 2))

    send_resid = outbound(residual)
    got_resid = lax.all_to_all(send_resid, "req", split_axis=0, concat_axis=0, tiled=True)
    decode_mask = build_decode_mask(cache_len, prefix_group, prefix_len)
    attn = attention(
        queries, new_keys, new_values, pool_keys, pool_values, decode_mask, span_offset[0]
    )
    got_attn = lax.all_to_all(outbound(attn), "req", split_axis=0, concat_axis=0, tiled=True)

    slots = jnp.arange(bal, dtype=jnp.int32)
    wanted = slots * devices + device
    src_dev = jnp.sum((ends[None, :] <= wanted[:, None]).astype(jnp.int32), axis=1)
    src_dev = jnp.minimum(src_dev, devices - 1)
    src_pos = jnp.clip((wanted - firsts[src_dev]) // devices, 0, bucket - 1)
    flat_idx = src_dev * bucket + src_pos
    dense_attn = got_attn.reshape(spread, width)[flat_idx]
    dense_resid = got_resid.reshape(spread, width)[flat_idx]
    mixed = finish(
        dense_attn, dense_resid, out_weight, norm_gain, gate_weight, up_weight, down_weight
    )
    lane = (device - firsts) % devices
    row_of = jnp.arange(bucket, dtype=jnp.int32)[None, :] * devices + lane[:, None]
    back_valid = row_of < counts[:, None]
    back_slot = jnp.clip((firsts[:, None] + row_of) // devices, 0, bal - 1)
    picked = jnp.where(
        back_valid[:, :, None], mixed[back_slot.reshape(-1)].reshape(devices, bucket, width), 0
    ).astype(jnp.bfloat16)
    returned = lax.all_to_all(picked, "req", split_axis=0, concat_axis=0, tiled=True)
    restored = jnp.roll(jnp.transpose(returned, (1, 0, 2)), -shift, axis=1).reshape(spread, width)
    if spread < total_rows:
        restored = jnp.concatenate(
            [restored, jnp.zeros((total_rows - spread, width), restored.dtype)], axis=0
        )
    is_live = jnp.arange(total_rows, dtype=jnp.int32) < own_count
    return jnp.where(is_live[:, None], restored, jnp.zeros((), jnp.bfloat16))


def solution(mesh):
    placed = (
        P("req", "grp"),
        P("req", "grp"),
        P("req", "grp"),
        P("req", "grp"),
        P("req", "grp"),
        P("req", "grp"),
        P("req"),
        P("req"),
        P("req"),
        P(),
        P("req"),
        P("grp", None),
        P(),
        P(None, "grp"),
        P(None, "grp"),
        P("grp", None),
    )
    return jax.shard_map(
        shards, mesh=mesh, in_specs=placed, out_specs=P("req", "grp"), check_vma=False
    )
```

```python
import jax
import jax.numpy as jnp
from jax import lax
from jax.experimental import pallas as pl
from jax.experimental.pallas import tpu as pltpu
from jax.sharding import PartitionSpec as P

HEADS = 32
KV_HEADS = 8
HEAD_DIM = 64
DEC = 8
REG = 512


MASKED_SCORE = -1e30


SCALE = HEAD_DIM ** (-0.5)
QBLK = 256


def span_kernel(start_ref, q_ref, kp_ref, vp_ref, kf_ref, vf_ref, o_ref):
    span_start = start_ref[0]
    first_kv = (pl.program_id(0) * 2 // (HEADS // KV_HEADS)) % 2 == 0
    half = HEAD_DIM

    def pick(ref, lo, hi):
        return jnp.where(first_kv, ref[lo:hi, 0:half], ref[lo:hi, half : 2 * half])

    rows = q_ref.shape[0]
    prior = kp_ref.shape[0]
    kp = pick(kp_ref, 0, prior)
    vp = pick(vp_ref, 0, prior)
    for blk in range(rows // QBLK):
        lo = blk * QBLK
        hi = lo + QBLK
        kf = pick(kf_ref, 0, hi)
        vf = pick(vf_ref, 0, hi)
        t_p = lax.broadcasted_iota(jnp.int32, (QBLK, prior), 1)
        prior_seen = t_p < span_start
        q_pos = lax.broadcasted_iota(jnp.int32, (QBLK, hi), 0) + lo
        k_pos = lax.broadcasted_iota(jnp.int32, (QBLK, hi), 1)
        seen = (k_pos >= DEC) & (k_pos <= q_pos)
        for hh in range(2):
            q = q_ref[lo:hi, hh * half : (hh + 1) * half]
            s_p = lax.dot_general(
                q, kp, (((1,), (1,)), ((), ())), preferred_element_type=jnp.float32
            ) * SCALE
            s_f = lax.dot_general(
                q, kf, (((1,), (1,)), ((), ())), preferred_element_type=jnp.float32
            ) * SCALE
            s_p = jnp.where(prior_seen, s_p, MASKED_SCORE)
            s_f = jnp.where(seen, s_f, MASKED_SCORE)
            highest = jnp.maximum(
                jnp.max(s_p, axis=1, keepdims=True), jnp.max(s_f, axis=1, keepdims=True)
            )
            e_p = jnp.exp(s_p - highest)
            e_f = jnp.exp(s_f - highest)
            totals = jnp.sum(e_p, axis=1, keepdims=True) + jnp.sum(e_f, axis=1, keepdims=True)
            p_p = (e_p / totals).astype(jnp.bfloat16)
            p_f = (e_f / totals).astype(jnp.bfloat16)
            out = jnp.dot(p_p, vp, preferred_element_type=jnp.float32) + jnp.dot(
                p_f, vf, preferred_element_type=jnp.float32
            )
            o_ref[lo:hi, hh * half : (hh + 1) * half] = out.astype(o_ref.dtype)


def span_attention(queries, pool_keys, pool_values, new_keys, new_values, span_start, cached):
    rows, width = queries.shape
    kv_width = new_keys.shape[1]
    prior = REG
    lanes = 2 * HEAD_DIM
    heads = width // HEAD_DIM
    q_spec = pl.BlockSpec((rows, lanes), lambda c, s: (0, c))
    p_spec = pl.BlockSpec((prior, kv_width), lambda c, s: (cached // prior, 0))
    f_spec = pl.BlockSpec((rows, kv_width), lambda c, s: (0, 0))
    flops = 4 * heads * rows * (prior + rows // 2) * HEAD_DIM
    cost = pl.CostEstimate(
        flops=16 * flops,
        transcendentals=heads * rows * (prior + rows // 2),
        bytes_accessed=2 * (2 * rows * width + 2 * (prior + rows) * kv_width),
    )
    return pl.pallas_call(
        span_kernel,
        out_shape=jax.ShapeDtypeStruct((rows, width), jnp.bfloat16),
        grid_spec=pltpu.PrefetchScalarGridSpec(
            num_scalar_prefetch=1,
            grid=(width // lanes,),
            in_specs=[q_spec, p_spec, p_spec, f_spec, f_spec],
            out_specs=q_spec,
        ),
        cost_estimate=cost,
    )(span_start.reshape(1).astype(jnp.int32), queries, pool_keys, pool_values, new_keys, new_values)


def decode_attention(queries, new_keys, new_values, pool_keys, pool_values, decode_mask):
    kv = new_keys.shape[1] // HEAD_DIM
    per_kv = queries.shape[1] // HEAD_DIM // kv
    cached = DEC * REG
    q = queries[:DEC].reshape(DEC, kv, per_kv, HEAD_DIM)
    kc = pool_keys[:cached].reshape(cached, kv, HEAD_DIM)
    vc = pool_values[:cached].reshape(cached, kv, HEAD_DIM)
    kn = new_keys[:DEC].reshape(DEC, kv, HEAD_DIM)
    vn = new_values[:DEC].reshape(DEC, kv, HEAD_DIM)
    s_c = jnp.einsum("rjhd,tjd->rjht", q, kc, preferred_element_type=jnp.float32) * SCALE
    s_n = jnp.einsum("rjhd,tjd->rjht", q, kn, preferred_element_type=jnp.float32) * SCALE
    s_c = jnp.where(decode_mask[:, None, None, :cached], s_c, MASKED_SCORE)
    s_n = jnp.where(decode_mask[:, None, None, cached:], s_n, MASKED_SCORE)
    highest = jnp.maximum(
        jnp.max(s_c, axis=3, keepdims=True), jnp.max(s_n, axis=3, keepdims=True)
    )
    e_c = jnp.exp(s_c - highest)
    e_n = jnp.exp(s_n - highest)
    totals = jnp.sum(e_c, axis=3, keepdims=True) + jnp.sum(e_n, axis=3, keepdims=True)
    p_c = (e_c / totals).astype(jnp.bfloat16)
    p_n = (e_n / totals).astype(jnp.bfloat16)
    out = jnp.einsum("rjht,tjd->rjhd", p_c, vc, preferred_element_type=jnp.float32) + jnp.einsum(
        "rjht,tjd->rjhd", p_n, vn, preferred_element_type=jnp.float32
    )
    return out.astype(jnp.bfloat16).reshape(DEC, kv * per_kv * HEAD_DIM)


def build_decode_mask(cache_len, prefix_group, prefix_len):
    position = jnp.arange(DEC * REG, dtype=jnp.int32)
    region = position // REG
    offset = position % REG
    request = jnp.arange(DEC, dtype=jnp.int32)
    shared = (region[None, :] == prefix_group[:, None]) & (offset[None, :] < prefix_len[:, None])
    owned = (
        (region[None, :] == request[:, None])
        & (offset[None, :] >= prefix_len[:, None])
        & (offset[None, :] < cache_len[:, None])
    )
    return jnp.concatenate([shared | owned, jnp.eye(DEC, dtype=jnp.bool_)], axis=1)


def attention(queries, new_keys, new_values, pool_keys, pool_values, decode_mask, span_start):
    cached = DEC * REG
    span_rows = span_attention(
        queries, pool_keys, pool_values, new_keys, new_values, span_start, cached
    )
    decode_rows = decode_attention(
        queries, new_keys, new_values, pool_keys, pool_values, decode_mask
    )
    return lax.dynamic_update_slice(span_rows, decode_rows, (0, 0))


def grp_block(x, index, width):
    return lax.dynamic_slice_in_dim(x, index * width, width, 1)


def grp_reduce_scatter(partial):
    parts = lax.axis_size("grp")
    width = partial.shape[1] // parts
    if parts != 4:
        return lax.psum_scatter(partial, "grp", scatter_dimension=1, tiled=True).astype(
            jnp.float32
        )
    me = lax.axis_index("grp")
    near = [(i, i ^ 1) for i in range(parts)]
    far = [(i, i ^ 2) for i in range(parts)]
    outgoing = jnp.stack([grp_block(partial, me ^ 1, width), grp_block(partial, me ^ 3, width)])
    incoming = lax.ppermute(outgoing, "grp", near)
    own = grp_block(partial, me, width).astype(jnp.float32) + incoming[0].astype(jnp.float32)
    other = grp_block(partial, me ^ 2, width).astype(jnp.float32) + incoming[1].astype(
        jnp.float32
    )
    arrived = lax.ppermute(other.astype(jnp.bfloat16), "grp", far)
    return own + arrived.astype(jnp.float32)


def grp_all_gather(block):
    parts = lax.axis_size("grp")
    if parts != 4:
        return lax.all_gather(block, "grp", axis=1, tiled=True)
    me = lax.axis_index("grp")
    near = [(i, i ^ 1) for i in range(parts)]
    far = [(i, i ^ 2) for i in range(parts)]
    across = lax.ppermute(block, "grp", far)
    pair = lax.ppermute(jnp.stack([block, across]), "grp", near)
    held = jnp.stack([block, pair[0], across, pair[1]])
    pieces = [lax.dynamic_index_in_dim(held, k ^ me, 0, keepdims=False) for k in range(parts)]
    return jnp.concatenate(pieces, axis=1)


def finish(attn_rows, resid_rows, out_weight, norm_gain, gate_weight, up_weight, down_weight):
    partial_value = jnp.dot(attn_rows, out_weight, preferred_element_type=jnp.float32)
    proj_cols = grp_reduce_scatter(partial_value.astype(jnp.bfloat16))
    state_cols = (resid_rows.astype(jnp.float32) + proj_cols).astype(jnp.bfloat16)
    state_full = grp_all_gather(state_cols)
    state32 = state_full.astype(jnp.float32)
    normed = (
        state32 * lax.rsqrt(jnp.mean(state32 * state32, axis=1, keepdims=True) + 1e-05) * norm_gain
    ).astype(jnp.bfloat16)
    gate = jnp.dot(normed, gate_weight, preferred_element_type=jnp.float32)
    upval = jnp.dot(normed, up_weight, preferred_element_type=jnp.float32)
    inner = (jax.nn.silu(gate) * upval).astype(jnp.bfloat16)
    down_cols = grp_reduce_scatter(
        jnp.dot(inner, down_weight, preferred_element_type=jnp.float32).astype(jnp.bfloat16)
    )
    return (state_cols.astype(jnp.float32) + down_cols).astype(jnp.bfloat16)


def shards(
    residual,
    queries,
    new_keys,
    new_values,
    pool_keys,
    pool_values,
    cache_len,
    prefix_group,
    prefix_len,
    span_rows,
    span_offset,
    out_weight,
    norm_gain,
    gate_weight,
    up_weight,
    down_weight,
):
    total_rows = residual.shape[0]
    width = residual.shape[1]
    device = lax.axis_index("req")
    devices = lax.axis_size("req")
    bucket = (total_rows - DEC + devices - 1) // devices
    spread = bucket * devices
    bal = total_rows // 2
    counts = DEC + span_rows
    ends = jnp.cumsum(counts)
    firsts = ends - counts
    first = firsts[device]
    own_count = counts[device]
    shift = first % devices

    def outbound(rows):
        grid = rows[:spread].reshape(bucket, devices, rows.shape[1])
        return jnp.transpose(jnp.roll(grid, shift, axis=1), (1, 0, 2))

    send_resid = outbound(residual)
    got_resid = lax.all_to_all(send_resid, "req", split_axis=0, concat_axis=0, tiled=True)
    decode_mask = build_decode_mask(cache_len, prefix_group, prefix_len)
    attn = attention(
        queries, new_keys, new_values, pool_keys, pool_values, decode_mask, span_offset[0]
    )
    got_resid, attn = lax.optimization_barrier((got_resid, attn))
    got_attn = lax.all_to_all(outbound(attn), "req", split_axis=0, concat_axis=0, tiled=True)

    slots = jnp.arange(bal, dtype=jnp.int32)
    wanted = slots * devices + device
    src_dev = jnp.sum((ends[None, :] <= wanted[:, None]).astype(jnp.int32), axis=1)
    src_dev = jnp.minimum(src_dev, devices - 1)
    src_pos = jnp.clip((wanted - firsts[src_dev]) // devices, 0, bucket - 1)
    flat_idx = src_dev * bucket + src_pos
    dense_attn = got_attn.reshape(spread, width)[flat_idx]
    dense_resid = got_resid.reshape(spread, width)[flat_idx]
    mixed = finish(
        dense_attn, dense_resid, out_weight, norm_gain, gate_weight, up_weight, down_weight
    )
    lane = (device - firsts) % devices
    row_of = jnp.arange(bucket, dtype=jnp.int32)[None, :] * devices + lane[:, None]
    back_valid = row_of < counts[:, None]
    back_slot = jnp.clip((firsts[:, None] + row_of) // devices, 0, bal - 1)
    picked = jnp.where(
        back_valid[:, :, None], mixed[back_slot.reshape(-1)].reshape(devices, bucket, width), 0
    ).astype(jnp.bfloat16)
    returned = lax.all_to_all(picked, "req", split_axis=0, concat_axis=0, tiled=True)
    restored = jnp.roll(jnp.transpose(returned, (1, 0, 2)), -shift, axis=1).reshape(spread, width)
    if spread < total_rows:
        restored = jnp.concatenate(
            [restored, jnp.zeros((total_rows - spread, width), restored.dtype)], axis=0
        )
    is_live = jnp.arange(total_rows, dtype=jnp.int32) < own_count
    return jnp.where(is_live[:, None], restored, jnp.zeros((), jnp.bfloat16))


def solution(mesh):
    placed = (
        P("req", "grp"),
        P("req", "grp"),
        P("req", "grp"),
        P("req", "grp"),
        P("req", "grp"),
        P("req", "grp"),
        P("req"),
        P("req"),
        P("req"),
        P(),
        P("req"),
        P("grp", None),
        P(),
        P(None, "grp"),
        P(None, "grp"),
        P("grp", None),
    )
    return jax.shard_map(
        shards, mesh=mesh, in_specs=placed, out_specs=P("req", "grp"), check_vma=False
    )
```

```python
import jax
import jax.numpy as jnp
from jax import lax
from jax.experimental import pallas as pl
from jax.experimental.pallas import tpu as pltpu
from jax.sharding import PartitionSpec as P

HEADS = 32
KV_HEADS = 8
HEAD_DIM = 64
DEC = 8
REG = 512


MASKED_SCORE = -1e30


SCALE = HEAD_DIM ** (-0.5)
QBLK = 256


def span_kernel(start_ref, q_ref, kp_ref, vp_ref, kf_ref, vf_ref, o_ref):
    span_start = start_ref[0]
    first_kv = (pl.program_id(0) * 2 // (HEADS // KV_HEADS)) % 2 == 0
    half = HEAD_DIM

    def pick(ref, lo, hi):
        return jnp.where(first_kv, ref[lo:hi, 0:half], ref[lo:hi, half : 2 * half])

    rows = q_ref.shape[0]
    prior = kp_ref.shape[0]
    kp = pick(kp_ref, 0, prior)
    vp = pick(vp_ref, 0, prior)
    for blk in range(rows // QBLK):
        lo = blk * QBLK
        hi = lo + QBLK
        kf = pick(kf_ref, 0, hi)
        vf = pick(vf_ref, 0, hi)
        t_p = lax.broadcasted_iota(jnp.int32, (QBLK, prior), 1)
        prior_seen = t_p < span_start
        q_pos = lax.broadcasted_iota(jnp.int32, (QBLK, hi), 0) + lo
        k_pos = lax.broadcasted_iota(jnp.int32, (QBLK, hi), 1)
        seen = (k_pos >= DEC) & (k_pos <= q_pos)
        for hh in range(2):
            q = q_ref[lo:hi, hh * half : (hh + 1) * half]
            s_p = lax.dot_general(
                q, kp, (((1,), (1,)), ((), ())), preferred_element_type=jnp.float32
            ) * SCALE
            s_f = lax.dot_general(
                q, kf, (((1,), (1,)), ((), ())), preferred_element_type=jnp.float32
            ) * SCALE
            s_p = jnp.where(prior_seen, s_p, MASKED_SCORE)
            s_f = jnp.where(seen, s_f, MASKED_SCORE)
            highest = jnp.maximum(
                jnp.max(s_p, axis=1, keepdims=True), jnp.max(s_f, axis=1, keepdims=True)
            )
            e_p = jnp.exp(s_p - highest)
            e_f = jnp.exp(s_f - highest)
            totals = jnp.sum(e_p, axis=1, keepdims=True) + jnp.sum(e_f, axis=1, keepdims=True)
            p_p = (e_p / totals).astype(jnp.bfloat16)
            p_f = (e_f / totals).astype(jnp.bfloat16)
            out = jnp.dot(p_p, vp, preferred_element_type=jnp.float32) + jnp.dot(
                p_f, vf, preferred_element_type=jnp.float32
            )
            o_ref[lo:hi, hh * half : (hh + 1) * half] = out.astype(o_ref.dtype)


def span_attention(queries, pool_keys, pool_values, new_keys, new_values, span_start, cached):
    rows, width = queries.shape
    kv_width = new_keys.shape[1]
    prior = REG
    lanes = 2 * HEAD_DIM
    heads = width // HEAD_DIM
    q_spec = pl.BlockSpec((rows, lanes), lambda c, s: (0, c))
    p_spec = pl.BlockSpec((prior, kv_width), lambda c, s: (cached // prior, 0))
    f_spec = pl.BlockSpec((rows, kv_width), lambda c, s: (0, 0))
    flops = 4 * heads * rows * (prior + rows // 2) * HEAD_DIM
    cost = pl.CostEstimate(
        flops=16 * flops,
        transcendentals=heads * rows * (prior + rows // 2),
        bytes_accessed=2 * (2 * rows * width + 2 * (prior + rows) * kv_width),
    )
    return pl.pallas_call(
        span_kernel,
        out_shape=jax.ShapeDtypeStruct((rows, width), jnp.bfloat16),
        grid_spec=pltpu.PrefetchScalarGridSpec(
            num_scalar_prefetch=1,
            grid=(width // lanes,),
            in_specs=[q_spec, p_spec, p_spec, f_spec, f_spec],
            out_specs=q_spec,
        ),
        cost_estimate=cost,
    )(span_start.reshape(1).astype(jnp.int32), queries, pool_keys, pool_values, new_keys, new_values)


def decode_attention(queries, new_keys, new_values, pool_keys, pool_values, decode_mask):
    kv = new_keys.shape[1] // HEAD_DIM
    heads = queries.shape[1] // HEAD_DIM
    per_kv = heads // kv
    cached = DEC * REG
    q = queries[:DEC].reshape(DEC, heads, HEAD_DIM)
    owner = jnp.arange(heads, dtype=jnp.int32) // per_kv
    lanes = [
        jnp.where((owner == j)[None, :, None], q, jnp.zeros((), q.dtype)) for j in range(kv)
    ]
    q_ext = jnp.concatenate(lanes, axis=2)
    s_c = jnp.einsum("rhc,tc->rht", q_ext, pool_keys[:cached], preferred_element_type=jnp.float32)
    s_n = jnp.einsum("rhc,tc->rht", q_ext, new_keys[:DEC], preferred_element_type=jnp.float32)
    s_c = jnp.where(decode_mask[:, None, :cached], s_c * SCALE, MASKED_SCORE)
    s_n = jnp.where(decode_mask[:, None, cached:], s_n * SCALE, MASKED_SCORE)
    highest = jnp.maximum(
        jnp.max(s_c, axis=2, keepdims=True), jnp.max(s_n, axis=2, keepdims=True)
    )
    e_c = jnp.exp(s_c - highest)
    e_n = jnp.exp(s_n - highest)
    totals = jnp.sum(e_c, axis=2, keepdims=True) + jnp.sum(e_n, axis=2, keepdims=True)
    p_c = (e_c / totals).astype(jnp.bfloat16)
    p_n = (e_n / totals).astype(jnp.bfloat16)
    full = jnp.einsum(
        "rht,tc->rhc", p_c, pool_values[:cached], preferred_element_type=jnp.float32
    ) + jnp.einsum("rht,tc->rhc", p_n, new_values[:DEC], preferred_element_type=jnp.float32)
    out = full[:, :, 0:HEAD_DIM]
    for j in range(1, kv):
        out = jnp.where(
            (owner == j)[None, :, None], full[:, :, j * HEAD_DIM : (j + 1) * HEAD_DIM], out
        )
    return out.astype(jnp.bfloat16).reshape(DEC, heads * HEAD_DIM)


def build_decode_mask(cache_len, prefix_group, prefix_len):
    position = jnp.arange(DEC * REG, dtype=jnp.int32)
    region = position // REG
    offset = position % REG
    request = jnp.arange(DEC, dtype=jnp.int32)
    shared = (region[None, :] == prefix_group[:, None]) & (offset[None, :] < prefix_len[:, None])
    owned = (
        (region[None, :] == request[:, None])
        & (offset[None, :] >= prefix_len[:, None])
        & (offset[None, :] < cache_len[:, None])
    )
    return jnp.concatenate([shared | owned, jnp.eye(DEC, dtype=jnp.bool_)], axis=1)


def attention(queries, new_keys, new_values, pool_keys, pool_values, decode_mask, span_start):
    cached = DEC * REG
    span_rows = span_attention(
        queries, pool_keys, pool_values, new_keys, new_values, span_start, cached
    )
    decode_rows = decode_attention(
        queries, new_keys, new_values, pool_keys, pool_values, decode_mask
    )
    return lax.dynamic_update_slice(span_rows, decode_rows, (0, 0))


def grp_block(x, index, width):
    return lax.dynamic_slice_in_dim(x, index * width, width, 1)


def grp_reduce_scatter(partial):
    parts = lax.axis_size("grp")
    width = partial.shape[1] // parts
    if parts != 4:
        return lax.psum_scatter(partial, "grp", scatter_dimension=1, tiled=True).astype(
            jnp.float32
        )
    me = lax.axis_index("grp")
    near = [(i, i ^ 1) for i in range(parts)]
    far = [(i, i ^ 2) for i in range(parts)]
    outgoing = jnp.stack([grp_block(partial, me ^ 1, width), grp_block(partial, me ^ 3, width)])
    incoming = lax.ppermute(outgoing, "grp", near)
    own = grp_block(partial, me, width).astype(jnp.float32) + incoming[0].astype(jnp.float32)
    other = grp_block(partial, me ^ 2, width).astype(jnp.float32) + incoming[1].astype(
        jnp.float32
    )
    arrived = lax.ppermute(other.astype(jnp.bfloat16), "grp", far)
    return own + arrived.astype(jnp.float32)


def grp_all_gather(block):
    parts = lax.axis_size("grp")
    if parts != 4:
        return lax.all_gather(block, "grp", axis=1, tiled=True)
    me = lax.axis_index("grp")
    near = [(i, i ^ 1) for i in range(parts)]
    far = [(i, i ^ 2) for i in range(parts)]
    across = lax.ppermute(block, "grp", far)
    pair = lax.ppermute(jnp.stack([block, across]), "grp", near)
    held = jnp.stack([block, pair[0], across, pair[1]])
    pieces = [lax.dynamic_index_in_dim(held, k ^ me, 0, keepdims=False) for k in range(parts)]
    return jnp.concatenate(pieces, axis=1)


def finish(attn_rows, resid_rows, out_weight, norm_gain, gate_weight, up_weight, down_weight):
    partial_value = jnp.dot(attn_rows, out_weight, preferred_element_type=jnp.float32)
    proj_cols = grp_reduce_scatter(partial_value.astype(jnp.bfloat16))
    state_cols = (resid_rows.astype(jnp.float32) + proj_cols).astype(jnp.bfloat16)
    state_full = grp_all_gather(state_cols)
    state32 = state_full.astype(jnp.float32)
    normed = (
        state32 * lax.rsqrt(jnp.mean(state32 * state32, axis=1, keepdims=True) + 1e-05) * norm_gain
    ).astype(jnp.bfloat16)
    gate = jnp.dot(normed, gate_weight, preferred_element_type=jnp.float32)
    upval = jnp.dot(normed, up_weight, preferred_element_type=jnp.float32)
    inner = (jax.nn.silu(gate) * upval).astype(jnp.bfloat16)
    down_cols = grp_reduce_scatter(
        jnp.dot(inner, down_weight, preferred_element_type=jnp.float32).astype(jnp.bfloat16)
    )
    return (state_cols.astype(jnp.float32) + down_cols).astype(jnp.bfloat16)


def shards(
    residual,
    queries,
    new_keys,
    new_values,
    pool_keys,
    pool_values,
    cache_len,
    prefix_group,
    prefix_len,
    span_rows,
    span_offset,
    out_weight,
    norm_gain,
    gate_weight,
    up_weight,
    down_weight,
):
    total_rows = residual.shape[0]
    width = residual.shape[1]
    device = lax.axis_index("req")
    devices = lax.axis_size("req")
    bucket = (total_rows - DEC + devices - 1) // devices
    spread = bucket * devices
    bal = total_rows // 2
    counts = DEC + span_rows
    ends = jnp.cumsum(counts)
    firsts = ends - counts
    first = firsts[device]
    own_count = counts[device]
    shift = first % devices

    def outbound(rows):
        grid = rows[:spread].reshape(bucket, devices, rows.shape[1])
        return jnp.transpose(jnp.roll(grid, shift, axis=1), (1, 0, 2))

    send_resid = outbound(residual)
    got_resid = lax.all_to_all(send_resid, "req", split_axis=0, concat_axis=0, tiled=True)
    decode_mask = build_decode_mask(cache_len, prefix_group, prefix_len)
    attn = attention(
        queries, new_keys, new_values, pool_keys, pool_values, decode_mask, span_offset[0]
    )
    got_resid, attn = lax.optimization_barrier((got_resid, attn))
    got_attn = lax.all_to_all(outbound(attn), "req", split_axis=0, concat_axis=0, tiled=True)

    slots = jnp.arange(bal, dtype=jnp.int32)
    wanted = slots * devices + device
    src_dev = jnp.sum((ends[None, :] <= wanted[:, None]).astype(jnp.int32), axis=1)
    src_dev = jnp.minimum(src_dev, devices - 1)
    src_pos = jnp.clip((wanted - firsts[src_dev]) // devices, 0, bucket - 1)
    flat_idx = src_dev * bucket + src_pos
    dense_attn = got_attn.reshape(spread, width)[flat_idx]
    dense_resid = got_resid.reshape(spread, width)[flat_idx]
    half = bal // 2
    mixed = jnp.concatenate(
        [
            finish(
                dense_attn[lo : lo + half],
                dense_resid[lo : lo + half],
                out_weight,
                norm_gain,
                gate_weight,
                up_weight,
                down_weight,
            )
            for lo in (0, half)
        ],
        axis=0,
    )
    lane = (device - firsts) % devices
    row_of = jnp.arange(bucket, dtype=jnp.int32)[None, :] * devices + lane[:, None]
    back_valid = row_of < counts[:, None]
    back_slot = jnp.clip((firsts[:, None] + row_of) // devices, 0, bal - 1)
    picked = jnp.where(
        back_valid[:, :, None], mixed[back_slot.reshape(-1)].reshape(devices, bucket, width), 0
    ).astype(jnp.bfloat16)
    returned = lax.all_to_all(picked, "req", split_axis=0, concat_axis=0, tiled=True)
    restored = jnp.roll(jnp.transpose(returned, (1, 0, 2)), -shift, axis=1).reshape(spread, width)
    if spread < total_rows:
        restored = jnp.concatenate(
            [restored, jnp.zeros((total_rows - spread, width), restored.dtype)], axis=0
        )
    is_live = jnp.arange(total_rows, dtype=jnp.int32) < own_count
    return jnp.where(is_live[:, None], restored, jnp.zeros((), jnp.bfloat16))


def solution(mesh):
    placed = (
        P("req", "grp"),
        P("req", "grp"),
        P("req", "grp"),
        P("req", "grp"),
        P("req", "grp"),
        P("req", "grp"),
        P("req"),
        P("req"),
        P("req"),
        P(),
        P("req"),
        P("grp", None),
        P(),
        P(None, "grp"),
        P(None, "grp"),
        P("grp", None),
    )
    return jax.shard_map(
        shards, mesh=mesh, in_specs=placed, out_specs=P("req", "grp"), check_vma=False
    )
```

```python
import functools

import jax
import jax.numpy as jnp
from jax import lax
from jax.experimental import pallas as pl
from jax.experimental.pallas import tpu as pltpu
from jax.sharding import PartitionSpec as P

HEADS = 32
KV_HEADS = 8
HEAD_DIM = 64
DEC = 8
REG = 512


MASKED_SCORE = -1e30


SCALE = HEAD_DIM ** (-0.5)
QBLK = 256


def span_kernel(kv_index, start_ref, q_ref, kp_ref, vp_ref, kf_ref, vf_ref, o_ref):
    span_start = start_ref[0]
    half = HEAD_DIM

    def pick(ref, lo, hi):
        return ref[lo:hi, kv_index * half : (kv_index + 1) * half]

    rows = q_ref.shape[0]
    prior = kp_ref.shape[0]
    kp = pick(kp_ref, 0, prior)
    vp = pick(vp_ref, 0, prior)
    for blk in range(rows // QBLK):
        lo = blk * QBLK
        hi = lo + QBLK
        kf = pick(kf_ref, 0, hi)
        vf = pick(vf_ref, 0, hi)
        t_p = lax.broadcasted_iota(jnp.int32, (QBLK, prior), 1)
        prior_seen = t_p < span_start
        q_pos = lax.broadcasted_iota(jnp.int32, (QBLK, hi), 0) + lo
        k_pos = lax.broadcasted_iota(jnp.int32, (QBLK, hi), 1)
        seen = (k_pos >= DEC) & (k_pos <= q_pos)
        for hh in range(2):
            q = q_ref[lo:hi, hh * half : (hh + 1) * half]
            s_p = lax.dot_general(
                q, kp, (((1,), (1,)), ((), ())), preferred_element_type=jnp.float32
            ) * SCALE
            s_f = lax.dot_general(
                q, kf, (((1,), (1,)), ((), ())), preferred_element_type=jnp.float32
            ) * SCALE
            s_p = jnp.where(prior_seen, s_p, MASKED_SCORE)
            s_f = jnp.where(seen, s_f, MASKED_SCORE)
            highest = jnp.maximum(
                jnp.max(s_p, axis=1, keepdims=True), jnp.max(s_f, axis=1, keepdims=True)
            )
            e_p = jnp.exp(s_p - highest)
            e_f = jnp.exp(s_f - highest)
            totals = jnp.sum(e_p, axis=1, keepdims=True) + jnp.sum(e_f, axis=1, keepdims=True)
            p_p = (e_p / totals).astype(jnp.bfloat16)
            p_f = (e_f / totals).astype(jnp.bfloat16)
            out = jnp.dot(p_p, vp, preferred_element_type=jnp.float32) + jnp.dot(
                p_f, vf, preferred_element_type=jnp.float32
            )
            o_ref[lo:hi, hh * half : (hh + 1) * half] = out.astype(o_ref.dtype)


def span_attention(queries, pool_keys, pool_values, new_keys, new_values, span_start, cached, kv_index):
    rows, width = queries.shape
    kv_width = new_keys.shape[1]
    prior = REG
    lanes = 2 * HEAD_DIM
    heads = width // HEAD_DIM
    kv = kv_width // HEAD_DIM
    steps = width // lanes // kv
    base = kv_index * steps
    q_spec = pl.BlockSpec((rows, lanes), lambda c, s: (0, base + c))
    o_spec = pl.BlockSpec((rows, lanes), lambda c, s: (0, c))
    p_spec = pl.BlockSpec((prior, kv_width), lambda c, s: (cached // prior, 0))
    f_spec = pl.BlockSpec((rows, kv_width), lambda c, s: (0, 0))
    flops = 4 * (heads // kv) * rows * (prior + rows // 2) * HEAD_DIM
    cost = pl.CostEstimate(
        flops=16 * flops,
        transcendentals=(heads // kv) * rows * (prior + rows // 2),
        bytes_accessed=2 * (2 * rows * width // kv + 2 * (prior + rows) * kv_width),
    )
    return pl.pallas_call(
        functools.partial(span_kernel, kv_index),
        out_shape=jax.ShapeDtypeStruct((rows, steps * lanes), jnp.bfloat16),
        grid_spec=pltpu.PrefetchScalarGridSpec(
            num_scalar_prefetch=1,
            grid=(steps,),
            in_specs=[q_spec, p_spec, p_spec, f_spec, f_spec],
            out_specs=o_spec,
        ),
        cost_estimate=cost,
    )(span_start.reshape(1).astype(jnp.int32), queries, pool_keys, pool_values, new_keys, new_values)


def decode_attention(queries, new_keys, new_values, pool_keys, pool_values, decode_mask):
    kv = new_keys.shape[1] // HEAD_DIM
    heads = queries.shape[1] // HEAD_DIM
    per_kv = heads // kv
    cached = DEC * REG
    q = queries[:DEC].reshape(DEC, heads, HEAD_DIM)
    owner = jnp.arange(heads, dtype=jnp.int32) // per_kv
    lanes = [
        jnp.where((owner == j)[None, :, None], q, jnp.zeros((), q.dtype)) for j in range(kv)
    ]
    q_ext = jnp.concatenate(lanes, axis=2)
    s_c = jnp.einsum("rhc,tc->rht", q_ext, pool_keys[:cached], preferred_element_type=jnp.float32)
    s_n = jnp.einsum("rhc,tc->rht", q_ext, new_keys[:DEC], preferred_element_type=jnp.float32)
    s_c = jnp.where(decode_mask[:, None, :cached], s_c * SCALE, MASKED_SCORE)
    s_n = jnp.where(decode_mask[:, None, cached:], s_n * SCALE, MASKED_SCORE)
    highest = jnp.maximum(
        jnp.max(s_c, axis=2, keepdims=True), jnp.max(s_n, axis=2, keepdims=True)
    )
    e_c = jnp.exp(s_c - highest)
    e_n = jnp.exp(s_n - highest)
    totals = jnp.sum(e_c, axis=2, keepdims=True) + jnp.sum(e_n, axis=2, keepdims=True)
    p_c = (e_c / totals).astype(jnp.bfloat16)
    p_n = (e_n / totals).astype(jnp.bfloat16)
    full = jnp.einsum(
        "rht,tc->rhc", p_c, pool_values[:cached], preferred_element_type=jnp.float32
    ) + jnp.einsum("rht,tc->rhc", p_n, new_values[:DEC], preferred_element_type=jnp.float32)
    out = full[:, :, 0:HEAD_DIM]
    for j in range(1, kv):
        out = jnp.where(
            (owner == j)[None, :, None], full[:, :, j * HEAD_DIM : (j + 1) * HEAD_DIM], out
        )
    return out.astype(jnp.bfloat16).reshape(DEC, heads * HEAD_DIM)


def build_decode_mask(cache_len, prefix_group, prefix_len):
    position = jnp.arange(DEC * REG, dtype=jnp.int32)
    region = position // REG
    offset = position % REG
    request = jnp.arange(DEC, dtype=jnp.int32)
    shared = (region[None, :] == prefix_group[:, None]) & (offset[None, :] < prefix_len[:, None])
    owned = (
        (region[None, :] == request[:, None])
        & (offset[None, :] >= prefix_len[:, None])
        & (offset[None, :] < cache_len[:, None])
    )
    return jnp.concatenate([shared | owned, jnp.eye(DEC, dtype=jnp.bool_)], axis=1)


def attention_parts(queries, new_keys, new_values, pool_keys, pool_values, decode_mask, span_start, send):
    cached = DEC * REG
    kv = new_keys.shape[1] // HEAD_DIM
    part_width = queries.shape[1] // kv
    decode_rows = decode_attention(
        queries, new_keys, new_values, pool_keys, pool_values, decode_mask
    )
    sent = []
    for j in range(kv):
        span_rows = span_attention(
            queries, pool_keys, pool_values, new_keys, new_values, span_start, cached, j
        )
        mine = decode_rows[:, j * part_width : (j + 1) * part_width]
        outgoing = send(lax.dynamic_update_slice(span_rows, mine, (0, 0)))
        if j + 1 < kv:
            outgoing, queries = lax.optimization_barrier((outgoing, queries))
        sent.append(outgoing)
    return sent


def grp_block(x, index, width):
    return lax.dynamic_slice_in_dim(x, index * width, width, 1)


def grp_reduce_scatter(partial):
    parts = lax.axis_size("grp")
    width = partial.shape[1] // parts
    if parts != 4:
        return lax.psum_scatter(partial, "grp", scatter_dimension=1, tiled=True).astype(
            jnp.float32
        )
    me = lax.axis_index("grp")
    near = [(i, i ^ 1) for i in range(parts)]
    far = [(i, i ^ 2) for i in range(parts)]
    outgoing = jnp.stack([grp_block(partial, me ^ 1, width), grp_block(partial, me ^ 3, width)])
    incoming = lax.ppermute(outgoing, "grp", near)
    own = grp_block(partial, me, width).astype(jnp.float32) + incoming[0].astype(jnp.float32)
    other = grp_block(partial, me ^ 2, width).astype(jnp.float32) + incoming[1].astype(
        jnp.float32
    )
    arrived = lax.ppermute(other.astype(jnp.bfloat16), "grp", far)
    return own + arrived.astype(jnp.float32)


def grp_all_gather(block):
    parts = lax.axis_size("grp")
    if parts != 4:
        return lax.all_gather(block, "grp", axis=1, tiled=True)
    me = lax.axis_index("grp")
    near = [(i, i ^ 1) for i in range(parts)]
    far = [(i, i ^ 2) for i in range(parts)]
    across = lax.ppermute(block, "grp", far)
    pair = lax.ppermute(jnp.stack([block, across]), "grp", near)
    held = jnp.stack([block, pair[0], across, pair[1]])
    pieces = [lax.dynamic_index_in_dim(held, k ^ me, 0, keepdims=False) for k in range(parts)]
    return jnp.concatenate(pieces, axis=1)


def finish(attn_rows, resid_rows, out_weight, norm_gain, gate_weight, up_weight, down_weight):
    partial_value = jnp.dot(attn_rows, out_weight, preferred_element_type=jnp.float32)
    proj_cols = grp_reduce_scatter(partial_value.astype(jnp.bfloat16))
    state_cols = (resid_rows.astype(jnp.float32) + proj_cols).astype(jnp.bfloat16)
    state_full = grp_all_gather(state_cols)
    state32 = state_full.astype(jnp.float32)
    normed = (
        state32 * lax.rsqrt(jnp.mean(state32 * state32, axis=1, keepdims=True) + 1e-05) * norm_gain
    ).astype(jnp.bfloat16)
    gate = jnp.dot(normed, gate_weight, preferred_element_type=jnp.float32)
    upval = jnp.dot(normed, up_weight, preferred_element_type=jnp.float32)
    inner = (jax.nn.silu(gate) * upval).astype(jnp.bfloat16)
    down_cols = grp_reduce_scatter(
        jnp.dot(inner, down_weight, preferred_element_type=jnp.float32).astype(jnp.bfloat16)
    )
    return (state_cols.astype(jnp.float32) + down_cols).astype(jnp.bfloat16)


def shards(
    residual,
    queries,
    new_keys,
    new_values,
    pool_keys,
    pool_values,
    cache_len,
    prefix_group,
    prefix_len,
    span_rows,
    span_offset,
    out_weight,
    norm_gain,
    gate_weight,
    up_weight,
    down_weight,
):
    total_rows = residual.shape[0]
    width = residual.shape[1]
    device = lax.axis_index("req")
    devices = lax.axis_size("req")
    bucket = (total_rows - DEC + devices - 1) // devices
    spread = bucket * devices
    bal = total_rows // 2
    counts = DEC + span_rows
    ends = jnp.cumsum(counts)
    firsts = ends - counts
    first = firsts[device]
    own_count = counts[device]
    shift = first % devices

    def outbound(rows):
        grid = rows[:spread].reshape(bucket, devices, rows.shape[1])
        return jnp.transpose(jnp.roll(grid, shift, axis=1), (1, 0, 2))

    send_resid = outbound(residual)
    got_resid = lax.all_to_all(send_resid, "req", split_axis=0, concat_axis=0, tiled=True)
    decode_mask = build_decode_mask(cache_len, prefix_group, prefix_len)
    sent_parts = attention_parts(
        queries, new_keys, new_values, pool_keys, pool_values, decode_mask, span_offset[0], outbound
    )
    got_resid, sent_parts[-1] = lax.optimization_barrier((got_resid, sent_parts[-1]))
    got_parts = [
        lax.all_to_all(part, "req", split_axis=0, concat_axis=0, tiled=True)
        for part in sent_parts
    ]

    slots = jnp.arange(bal, dtype=jnp.int32)
    wanted = slots * devices + device
    src_dev = jnp.sum((ends[None, :] <= wanted[:, None]).astype(jnp.int32), axis=1)
    src_dev = jnp.minimum(src_dev, devices - 1)
    src_pos = jnp.clip((wanted - firsts[src_dev]) // devices, 0, bucket - 1)
    flat_idx = src_dev * bucket + src_pos
    dense_attn = jnp.concatenate(
        [got.reshape(spread, got.shape[2])[flat_idx] for got in got_parts], axis=1
    )
    dense_resid = got_resid.reshape(spread, width)[flat_idx]
    mixed = finish(
        dense_attn, dense_resid, out_weight, norm_gain, gate_weight, up_weight, down_weight
    )
    lane = (device - firsts) % devices
    row_of = jnp.arange(bucket, dtype=jnp.int32)[None, :] * devices + lane[:, None]
    back_valid = row_of < counts[:, None]
    back_slot = jnp.clip((firsts[:, None] + row_of) // devices, 0, bal - 1)
    picked = jnp.where(
        back_valid[:, :, None], mixed[back_slot.reshape(-1)].reshape(devices, bucket, width), 0
    ).astype(jnp.bfloat16)
    returned = lax.all_to_all(picked, "req", split_axis=0, concat_axis=0, tiled=True)
    restored = jnp.roll(jnp.transpose(returned, (1, 0, 2)), -shift, axis=1).reshape(spread, width)
    if spread < total_rows:
        restored = jnp.concatenate(
            [restored, jnp.zeros((total_rows - spread, width), restored.dtype)], axis=0
        )
    is_live = jnp.arange(total_rows, dtype=jnp.int32) < own_count
    return jnp.where(is_live[:, None], restored, jnp.zeros((), jnp.bfloat16))


def solution(mesh):
    placed = (
        P("req", "grp"),
        P("req", "grp"),
        P("req", "grp"),
        P("req", "grp"),
        P("req", "grp"),
        P("req", "grp"),
        P("req"),
        P("req"),
        P("req"),
        P(),
        P("req"),
        P("grp", None),
        P(),
        P(None, "grp"),
        P(None, "grp"),
        P("grp", None),
    )
    return jax.shard_map(
        shards, mesh=mesh, in_specs=placed, out_specs=P("req", "grp"), check_vma=False
    )
```

```python
import functools

import jax
import jax.numpy as jnp
from jax import lax
from jax.experimental import pallas as pl
from jax.experimental.pallas import tpu as pltpu
from jax.sharding import PartitionSpec as P

HEADS = 32
KV_HEADS = 8
HEAD_DIM = 64
DEC = 8
REG = 512


MASKED_SCORE = -1e30


SCALE = HEAD_DIM ** (-0.5)
QBLK = 256


def span_kernel(kv_index, start_ref, q_ref, kp_ref, vp_ref, kf_ref, vf_ref, o_ref):
    span_start = start_ref[0]
    half = HEAD_DIM

    def pick(ref, lo, hi):
        return ref[lo:hi, kv_index * half : (kv_index + 1) * half]

    rows = q_ref.shape[0]
    prior = kp_ref.shape[0]
    kp = pick(kp_ref, 0, prior)
    vp = pick(vp_ref, 0, prior)
    for blk in range(rows // QBLK):
        lo = blk * QBLK
        hi = lo + QBLK
        kf = pick(kf_ref, 0, hi)
        vf = pick(vf_ref, 0, hi)
        t_p = lax.broadcasted_iota(jnp.int32, (QBLK, prior), 1)
        prior_seen = t_p < span_start
        q_pos = lax.broadcasted_iota(jnp.int32, (QBLK, hi), 0) + lo
        k_pos = lax.broadcasted_iota(jnp.int32, (QBLK, hi), 1)
        seen = (k_pos >= DEC) & (k_pos <= q_pos)
        for hh in range(2):
            q = q_ref[lo:hi, hh * half : (hh + 1) * half]
            s_p = lax.dot_general(
                q, kp, (((1,), (1,)), ((), ())), preferred_element_type=jnp.float32
            ) * SCALE
            s_f = lax.dot_general(
                q, kf, (((1,), (1,)), ((), ())), preferred_element_type=jnp.float32
            ) * SCALE
            s_p = jnp.where(prior_seen, s_p, MASKED_SCORE)
            s_f = jnp.where(seen, s_f, MASKED_SCORE)
            highest = jnp.maximum(
                jnp.max(s_p, axis=1, keepdims=True), jnp.max(s_f, axis=1, keepdims=True)
            )
            e_p = jnp.exp(s_p - highest)
            e_f = jnp.exp(s_f - highest)
            totals = jnp.sum(e_p, axis=1, keepdims=True) + jnp.sum(e_f, axis=1, keepdims=True)
            p_p = (e_p / totals).astype(jnp.bfloat16)
            p_f = (e_f / totals).astype(jnp.bfloat16)
            out = jnp.dot(p_p, vp, preferred_element_type=jnp.float32) + jnp.dot(
                p_f, vf, preferred_element_type=jnp.float32
            )
            o_ref[lo:hi, hh * half : (hh + 1) * half] = out.astype(o_ref.dtype)


def span_attention(queries, pool_keys, pool_values, new_keys, new_values, span_start, cached, kv_index):
    rows, width = queries.shape
    kv_width = new_keys.shape[1]
    prior = REG
    lanes = 2 * HEAD_DIM
    heads = width // HEAD_DIM
    kv = kv_width // HEAD_DIM
    steps = width // lanes // kv
    base = kv_index * steps
    q_spec = pl.BlockSpec((rows, lanes), lambda c, s: (0, base + c))
    o_spec = pl.BlockSpec((rows, lanes), lambda c, s: (0, c))
    p_spec = pl.BlockSpec((prior, kv_width), lambda c, s: (cached // prior, 0))
    f_spec = pl.BlockSpec((rows, kv_width), lambda c, s: (0, 0))
    flops = 4 * (heads // kv) * rows * (prior + rows // 2) * HEAD_DIM
    cost = pl.CostEstimate(
        flops=16 * flops,
        transcendentals=(heads // kv) * rows * (prior + rows // 2),
        bytes_accessed=2 * (2 * rows * width // kv + 2 * (prior + rows) * kv_width),
    )
    return pl.pallas_call(
        functools.partial(span_kernel, kv_index),
        out_shape=jax.ShapeDtypeStruct((rows, steps * lanes), jnp.bfloat16),
        grid_spec=pltpu.PrefetchScalarGridSpec(
            num_scalar_prefetch=1,
            grid=(steps,),
            in_specs=[q_spec, p_spec, p_spec, f_spec, f_spec],
            out_specs=o_spec,
        ),
        cost_estimate=cost,
    )(span_start.reshape(1).astype(jnp.int32), queries, pool_keys, pool_values, new_keys, new_values)


def decode_attention(queries, new_keys, new_values, pool_keys, pool_values, decode_mask):
    kv = new_keys.shape[1] // HEAD_DIM
    heads = queries.shape[1] // HEAD_DIM
    per_kv = heads // kv
    cached = DEC * REG
    q = queries[:DEC].reshape(DEC, heads, HEAD_DIM)
    owner = jnp.arange(heads, dtype=jnp.int32) // per_kv
    lanes = [
        jnp.where((owner == j)[None, :, None], q, jnp.zeros((), q.dtype)) for j in range(kv)
    ]
    q_ext = jnp.concatenate(lanes, axis=2)
    s_c = jnp.einsum("rhc,tc->rht", q_ext, pool_keys[:cached], preferred_element_type=jnp.float32)
    s_n = jnp.einsum("rhc,tc->rht", q_ext, new_keys[:DEC], preferred_element_type=jnp.float32)
    s_c = jnp.where(decode_mask[:, None, :cached], s_c * SCALE, MASKED_SCORE)
    s_n = jnp.where(decode_mask[:, None, cached:], s_n * SCALE, MASKED_SCORE)
    highest = jnp.maximum(
        jnp.max(s_c, axis=2, keepdims=True), jnp.max(s_n, axis=2, keepdims=True)
    )
    e_c = jnp.exp(s_c - highest)
    e_n = jnp.exp(s_n - highest)
    totals = jnp.sum(e_c, axis=2, keepdims=True) + jnp.sum(e_n, axis=2, keepdims=True)
    p_c = (e_c / totals).astype(jnp.bfloat16)
    p_n = (e_n / totals).astype(jnp.bfloat16)
    full = jnp.einsum(
        "rht,tc->rhc", p_c, pool_values[:cached], preferred_element_type=jnp.float32
    ) + jnp.einsum("rht,tc->rhc", p_n, new_values[:DEC], preferred_element_type=jnp.float32)
    out = full[:, :, 0:HEAD_DIM]
    for j in range(1, kv):
        out = jnp.where(
            (owner == j)[None, :, None], full[:, :, j * HEAD_DIM : (j + 1) * HEAD_DIM], out
        )
    return out.astype(jnp.bfloat16).reshape(DEC, heads * HEAD_DIM)


def build_decode_mask(cache_len, prefix_group, prefix_len):
    position = jnp.arange(DEC * REG, dtype=jnp.int32)
    region = position // REG
    offset = position % REG
    request = jnp.arange(DEC, dtype=jnp.int32)
    shared = (region[None, :] == prefix_group[:, None]) & (offset[None, :] < prefix_len[:, None])
    owned = (
        (region[None, :] == request[:, None])
        & (offset[None, :] >= prefix_len[:, None])
        & (offset[None, :] < cache_len[:, None])
    )
    return jnp.concatenate([shared | owned, jnp.eye(DEC, dtype=jnp.bool_)], axis=1)


def attention_parts(queries, new_keys, new_values, pool_keys, pool_values, decode_mask, span_start, send):
    cached = DEC * REG
    kv = new_keys.shape[1] // HEAD_DIM
    part_width = queries.shape[1] // kv
    decode_rows = decode_attention(
        queries, new_keys, new_values, pool_keys, pool_values, decode_mask
    )
    sent = []
    for j in range(kv):
        span_rows = span_attention(
            queries, pool_keys, pool_values, new_keys, new_values, span_start, cached, j
        )
        mine = decode_rows[:, j * part_width : (j + 1) * part_width]
        outgoing = send(lax.dynamic_update_slice(span_rows, mine, (0, 0)))
        if j + 1 < kv:
            outgoing, queries = lax.optimization_barrier((outgoing, queries))
        sent.append(outgoing)
    return sent


def grp_block(x, index, width):
    return lax.dynamic_slice_in_dim(x, index * width, width, 1)


def grp_reduce_scatter(partial, tie=None):
    parts = lax.axis_size("grp")
    width = partial.shape[1] // parts
    if parts != 4:
        summed = lax.psum_scatter(partial, "grp", scatter_dimension=1, tiled=True)
        return summed.astype(jnp.float32) if tie is None else (summed.astype(jnp.float32), tie)
    me = lax.axis_index("grp")
    near = [(i, i ^ 1) for i in range(parts)]
    far = [(i, i ^ 2) for i in range(parts)]
    outgoing = jnp.stack([grp_block(partial, me ^ 1, width), grp_block(partial, me ^ 3, width)])
    incoming = lax.ppermute(outgoing, "grp", near)
    own = grp_block(partial, me, width).astype(jnp.float32) + incoming[0].astype(jnp.float32)
    other = grp_block(partial, me ^ 2, width).astype(jnp.float32) + incoming[1].astype(
        jnp.float32
    )
    leaving = other.astype(jnp.bfloat16)
    if tie is not None:
        leaving, tie = lax.optimization_barrier((leaving, tie))
    arrived = lax.ppermute(leaving, "grp", far)
    if tie is None:
        return own + arrived.astype(jnp.float32)
    return own + arrived.astype(jnp.float32), tie


def grp_all_gather(block):
    parts = lax.axis_size("grp")
    if parts != 4:
        return lax.all_gather(block, "grp", axis=1, tiled=True)
    me = lax.axis_index("grp")
    near = [(i, i ^ 1) for i in range(parts)]
    far = [(i, i ^ 2) for i in range(parts)]
    across = lax.ppermute(block, "grp", far)
    pair = lax.ppermute(jnp.stack([block, across]), "grp", near)
    held = jnp.stack([block, pair[0], across, pair[1]])
    pieces = [lax.dynamic_index_in_dim(held, k ^ me, 0, keepdims=False) for k in range(parts)]
    return jnp.concatenate(pieces, axis=1)


def finish(attn_rows, resid_rows, out_weight, norm_gain, gate_weight, up_weight, down_weight):
    partial_value = jnp.dot(attn_rows, out_weight, preferred_element_type=jnp.float32)
    proj_cols = grp_reduce_scatter(partial_value.astype(jnp.bfloat16))
    state_cols = (resid_rows.astype(jnp.float32) + proj_cols).astype(jnp.bfloat16)
    state_full = grp_all_gather(state_cols)
    state32 = state_full.astype(jnp.float32)
    normed = (
        state32 * lax.rsqrt(jnp.mean(state32 * state32, axis=1, keepdims=True) + 1e-05) * norm_gain
    ).astype(jnp.bfloat16)
    gate = jnp.dot(normed, gate_weight, preferred_element_type=jnp.float32)
    upval = jnp.dot(normed, up_weight, preferred_element_type=jnp.float32)
    inner = (jax.nn.silu(gate) * upval).astype(jnp.bfloat16)
    down_partial = jnp.dot(inner, down_weight, preferred_element_type=jnp.float32).astype(
        jnp.bfloat16
    )
    return state_cols, down_partial


def shards(
    residual,
    queries,
    new_keys,
    new_values,
    pool_keys,
    pool_values,
    cache_len,
    prefix_group,
    prefix_len,
    span_rows,
    span_offset,
    out_weight,
    norm_gain,
    gate_weight,
    up_weight,
    down_weight,
):
    total_rows = residual.shape[0]
    width = residual.shape[1]
    device = lax.axis_index("req")
    devices = lax.axis_size("req")
    bucket = (total_rows - DEC + devices - 1) // devices
    spread = bucket * devices
    bal = total_rows // 2
    counts = DEC + span_rows
    ends = jnp.cumsum(counts)
    firsts = ends - counts
    first = firsts[device]
    own_count = counts[device]
    shift = first % devices

    def outbound(rows):
        grid = rows[:spread].reshape(bucket, devices, rows.shape[1])
        return jnp.transpose(jnp.roll(grid, shift, axis=1), (1, 0, 2))

    send_resid = outbound(residual)
    got_resid = lax.all_to_all(send_resid, "req", split_axis=0, concat_axis=0, tiled=True)
    decode_mask = build_decode_mask(cache_len, prefix_group, prefix_len)
    sent_parts = attention_parts(
        queries, new_keys, new_values, pool_keys, pool_values, decode_mask, span_offset[0], outbound
    )
    got_resid, sent_parts[-1] = lax.optimization_barrier((got_resid, sent_parts[-1]))
    got_parts = [
        lax.all_to_all(part, "req", split_axis=0, concat_axis=0, tiled=True)
        for part in sent_parts
    ]

    slots = jnp.arange(bal, dtype=jnp.int32)
    wanted = slots * devices + device
    src_dev = jnp.sum((ends[None, :] <= wanted[:, None]).astype(jnp.int32), axis=1)
    src_dev = jnp.minimum(src_dev, devices - 1)
    src_pos = jnp.clip((wanted - firsts[src_dev]) // devices, 0, bucket - 1)
    flat_idx = src_dev * bucket + src_pos
    dense_attn = jnp.concatenate(
        [got.reshape(spread, got.shape[2])[flat_idx] for got in got_parts], axis=1
    )
    dense_resid = got_resid.reshape(spread, width)[flat_idx]
    mixed = finish(
        dense_attn, dense_resid, out_weight, norm_gain, gate_weight, up_weight, down_weight
    )
    lane = (device - firsts) % devices
    row_of = jnp.arange(bucket, dtype=jnp.int32)[None, :] * devices + lane[:, None]
    back_valid = row_of < counts[:, None]
    back_slot = jnp.clip((firsts[:, None] + row_of) // devices, 0, bal - 1)
    state_cols, down_partial = mixed
    rows = down_partial.shape[0]
    parts = lax.axis_size("grp")
    piece = down_partial.shape[1] // parts // 2
    quads = down_partial.reshape(rows, parts, 2, piece)

    def pick_back(k, down_cols):
        own = state_cols[:, k * piece : (k + 1) * piece].astype(jnp.float32)
        half_rows = (own + down_cols).astype(jnp.bfloat16)
        return jnp.where(
            back_valid[:, :, None],
            half_rows[back_slot.reshape(-1)].reshape(devices, bucket, piece),
            0,
        ).astype(jnp.bfloat16)

    picked_a = pick_back(0, grp_reduce_scatter(quads[:, :, 0, :].reshape(rows, parts * piece)))
    down_b, picked_a = grp_reduce_scatter(
        quads[:, :, 1, :].reshape(rows, parts * piece), tie=picked_a
    )
    picked_b = pick_back(1, down_b)
    restored_halves = []
    for picked in (picked_a, picked_b):
        returned = lax.all_to_all(picked, "req", split_axis=0, concat_axis=0, tiled=True)
        restored_halves.append(
            jnp.roll(jnp.transpose(returned, (1, 0, 2)), -shift, axis=1).reshape(spread, piece)
        )
    restored = jnp.concatenate(restored_halves, axis=1)
    if spread < total_rows:
        restored = jnp.concatenate(
            [restored, jnp.zeros((total_rows - spread, width), restored.dtype)], axis=0
        )
    is_live = jnp.arange(total_rows, dtype=jnp.int32) < own_count
    return jnp.where(is_live[:, None], restored, jnp.zeros((), jnp.bfloat16))


def solution(mesh):
    placed = (
        P("req", "grp"),
        P("req", "grp"),
        P("req", "grp"),
        P("req", "grp"),
        P("req", "grp"),
        P("req", "grp"),
        P("req"),
        P("req"),
        P("req"),
        P(),
        P("req"),
        P("grp", None),
        P(),
        P(None, "grp"),
        P(None, "grp"),
        P("grp", None),
    )
    return jax.shard_map(
        shards, mesh=mesh, in_specs=placed, out_specs=P("req", "grp"), check_vma=False
    )
```

```python
import functools

import jax
import jax.numpy as jnp
from jax import lax
from jax.experimental import pallas as pl
from jax.experimental.pallas import tpu as pltpu
from jax.sharding import PartitionSpec as P

HEADS = 32
KV_HEADS = 8
HEAD_DIM = 64
DEC = 8
REG = 512


MASKED_SCORE = -1e30


SCALE = HEAD_DIM ** (-0.5)
QBLK = 256


def span_kernel(kv_index, start_ref, q_ref, kp_ref, vp_ref, kf_ref, vf_ref, o_ref):
    span_start = start_ref[0]
    half = HEAD_DIM

    def pick(ref, lo, hi):
        return ref[lo:hi, kv_index * half : (kv_index + 1) * half]

    rows = q_ref.shape[0]
    prior = kp_ref.shape[0]
    kp = pick(kp_ref, 0, prior)
    vp = pick(vp_ref, 0, prior)
    for blk in range(rows // QBLK):
        lo = blk * QBLK
        hi = lo + QBLK
        kf = pick(kf_ref, 0, hi)
        vf = pick(vf_ref, 0, hi)
        t_p = lax.broadcasted_iota(jnp.int32, (QBLK, prior), 1)
        prior_seen = t_p < span_start
        q_pos = lax.broadcasted_iota(jnp.int32, (QBLK, hi), 0) + lo
        k_pos = lax.broadcasted_iota(jnp.int32, (QBLK, hi), 1)
        seen = (k_pos >= DEC) & (k_pos <= q_pos)
        for hh in range(2):
            q = q_ref[lo:hi, hh * half : (hh + 1) * half]
            s_p = lax.dot_general(
                q, kp, (((1,), (1,)), ((), ())), preferred_element_type=jnp.float32
            ) * SCALE
            s_f = lax.dot_general(
                q, kf, (((1,), (1,)), ((), ())), preferred_element_type=jnp.float32
            ) * SCALE
            s_p = jnp.where(prior_seen, s_p, MASKED_SCORE)
            s_f = jnp.where(seen, s_f, MASKED_SCORE)
            highest = jnp.maximum(
                jnp.max(s_p, axis=1, keepdims=True), jnp.max(s_f, axis=1, keepdims=True)
            )
            e_p = jnp.exp(s_p - highest)
            e_f = jnp.exp(s_f - highest)
            totals = jnp.sum(e_p, axis=1, keepdims=True) + jnp.sum(e_f, axis=1, keepdims=True)
            inverse = 1.0 / totals
            p_p = (e_p * inverse).astype(jnp.bfloat16)
            p_f = (e_f * inverse).astype(jnp.bfloat16)
            out = jnp.dot(p_p, vp, preferred_element_type=jnp.float32) + jnp.dot(
                p_f, vf, preferred_element_type=jnp.float32
            )
            o_ref[lo:hi, hh * half : (hh + 1) * half] = out.astype(o_ref.dtype)


def span_attention(queries, pool_keys, pool_values, new_keys, new_values, span_start, cached, kv_index):
    rows, width = queries.shape
    kv_width = new_keys.shape[1]
    prior = REG
    lanes = 2 * HEAD_DIM
    heads = width // HEAD_DIM
    kv = kv_width // HEAD_DIM
    steps = width // lanes // kv
    base = kv_index * steps
    q_spec = pl.BlockSpec((rows, lanes), lambda c, s: (0, base + c))
    o_spec = pl.BlockSpec((rows, lanes), lambda c, s: (0, c))
    p_spec = pl.BlockSpec((prior, kv_width), lambda c, s: (cached // prior, 0))
    f_spec = pl.BlockSpec((rows, kv_width), lambda c, s: (0, 0))
    flops = 4 * (heads // kv) * rows * (prior + rows // 2) * HEAD_DIM
    cost = pl.CostEstimate(
        flops=16 * flops,
        transcendentals=(heads // kv) * rows * (prior + rows // 2),
        bytes_accessed=2 * (2 * rows * width // kv + 2 * (prior + rows) * kv_width),
    )
    return pl.pallas_call(
        functools.partial(span_kernel, kv_index),
        out_shape=jax.ShapeDtypeStruct((rows, steps * lanes), jnp.bfloat16),
        grid_spec=pltpu.PrefetchScalarGridSpec(
            num_scalar_prefetch=1,
            grid=(steps,),
            in_specs=[q_spec, p_spec, p_spec, f_spec, f_spec],
            out_specs=o_spec,
        ),
        cost_estimate=cost,
    )(span_start.reshape(1).astype(jnp.int32), queries, pool_keys, pool_values, new_keys, new_values)


def decode_attention(queries, new_keys, new_values, pool_keys, pool_values, decode_mask):
    kv = new_keys.shape[1] // HEAD_DIM
    heads = queries.shape[1] // HEAD_DIM
    per_kv = heads // kv
    cached = DEC * REG
    q = queries[:DEC].reshape(DEC, heads, HEAD_DIM)
    owner = jnp.arange(heads, dtype=jnp.int32) // per_kv
    lanes = [
        jnp.where((owner == j)[None, :, None], q, jnp.zeros((), q.dtype)) for j in range(kv)
    ]
    q_ext = jnp.concatenate(lanes, axis=2)
    s_c = jnp.einsum("rhc,tc->rht", q_ext, pool_keys[:cached], preferred_element_type=jnp.float32)
    s_n = jnp.einsum("rhc,tc->rht", q_ext, new_keys[:DEC], preferred_element_type=jnp.float32)
    s_c = jnp.where(decode_mask[:, None, :cached], s_c * SCALE, MASKED_SCORE)
    s_n = jnp.where(decode_mask[:, None, cached:], s_n * SCALE, MASKED_SCORE)
    highest = jnp.maximum(
        jnp.max(s_c, axis=2, keepdims=True), jnp.max(s_n, axis=2, keepdims=True)
    )
    e_c = jnp.exp(s_c - highest)
    e_n = jnp.exp(s_n - highest)
    totals = jnp.sum(e_c, axis=2, keepdims=True) + jnp.sum(e_n, axis=2, keepdims=True)
    p_c = (e_c / totals).astype(jnp.bfloat16)
    p_n = (e_n / totals).astype(jnp.bfloat16)
    full = jnp.einsum(
        "rht,tc->rhc", p_c, pool_values[:cached], preferred_element_type=jnp.float32
    ) + jnp.einsum("rht,tc->rhc", p_n, new_values[:DEC], preferred_element_type=jnp.float32)
    out = full[:, :, 0:HEAD_DIM]
    for j in range(1, kv):
        out = jnp.where(
            (owner == j)[None, :, None], full[:, :, j * HEAD_DIM : (j + 1) * HEAD_DIM], out
        )
    return out.astype(jnp.bfloat16).reshape(DEC, heads * HEAD_DIM)


def build_decode_mask(cache_len, prefix_group, prefix_len):
    position = jnp.arange(DEC * REG, dtype=jnp.int32)
    region = position // REG
    offset = position % REG
    request = jnp.arange(DEC, dtype=jnp.int32)
    shared = (region[None, :] == prefix_group[:, None]) & (offset[None, :] < prefix_len[:, None])
    owned = (
        (region[None, :] == request[:, None])
        & (offset[None, :] >= prefix_len[:, None])
        & (offset[None, :] < cache_len[:, None])
    )
    return jnp.concatenate([shared | owned, jnp.eye(DEC, dtype=jnp.bool_)], axis=1)


def attention_parts(queries, new_keys, new_values, pool_keys, pool_values, decode_mask, span_start, send):
    cached = DEC * REG
    kv = new_keys.shape[1] // HEAD_DIM
    part_width = queries.shape[1] // kv
    decode_rows = decode_attention(
        queries, new_keys, new_values, pool_keys, pool_values, decode_mask
    )
    sent = []
    for j in range(kv):
        span_rows = span_attention(
            queries, pool_keys, pool_values, new_keys, new_values, span_start, cached, j
        )
        mine = decode_rows[:, j * part_width : (j + 1) * part_width]
        outgoing = send(lax.dynamic_update_slice(span_rows, mine, (0, 0)))
        if j + 1 < kv:
            outgoing, queries = lax.optimization_barrier((outgoing, queries))
        sent.append(outgoing)
    return sent


def grp_block(x, index, width):
    return lax.dynamic_slice_in_dim(x, index * width, width, 1)


def grp_reduce_scatter(partial):
    parts = lax.axis_size("grp")
    width = partial.shape[1] // parts
    if parts != 4:
        return lax.psum_scatter(partial, "grp", scatter_dimension=1, tiled=True).astype(
            jnp.float32
        )
    me = lax.axis_index("grp")
    near = [(i, i ^ 1) for i in range(parts)]
    far = [(i, i ^ 2) for i in range(parts)]
    outgoing = jnp.stack([grp_block(partial, me ^ 1, width), grp_block(partial, me ^ 3, width)])
    incoming = lax.ppermute(outgoing, "grp", near)
    own = grp_block(partial, me, width).astype(jnp.float32) + incoming[0].astype(jnp.float32)
    other = grp_block(partial, me ^ 2, width).astype(jnp.float32) + incoming[1].astype(
        jnp.float32
    )
    arrived = lax.ppermute(other.astype(jnp.bfloat16), "grp", far)
    return own + arrived.astype(jnp.float32)


def grp_all_gather(block):
    parts = lax.axis_size("grp")
    if parts != 4:
        return lax.all_gather(block, "grp", axis=1, tiled=True)
    me = lax.axis_index("grp")
    near = [(i, i ^ 1) for i in range(parts)]
    far = [(i, i ^ 2) for i in range(parts)]
    across = lax.ppermute(block, "grp", far)
    pair = lax.ppermute(jnp.stack([block, across]), "grp", near)
    held = jnp.stack([block, pair[0], across, pair[1]])
    pieces = [lax.dynamic_index_in_dim(held, k ^ me, 0, keepdims=False) for k in range(parts)]
    return jnp.concatenate(pieces, axis=1)


def finish(attn_rows, resid_rows, out_weight, norm_gain, gate_weight, up_weight, down_weight):
    partial_value = jnp.dot(attn_rows, out_weight, preferred_element_type=jnp.float32)
    proj_cols = grp_reduce_scatter(partial_value.astype(jnp.bfloat16))
    state_cols = (resid_rows.astype(jnp.float32) + proj_cols).astype(jnp.bfloat16)
    state_full = grp_all_gather(state_cols)
    state32 = state_full.astype(jnp.float32)
    normed = (
        state32 * lax.rsqrt(jnp.mean(state32 * state32, axis=1, keepdims=True) + 1e-05) * norm_gain
    ).astype(jnp.bfloat16)
    gate = jnp.dot(normed, gate_weight, preferred_element_type=jnp.float32)
    upval = jnp.dot(normed, up_weight, preferred_element_type=jnp.float32)
    inner = (jax.nn.silu(gate) * upval).astype(jnp.bfloat16)
    down_cols = grp_reduce_scatter(
        jnp.dot(inner, down_weight, preferred_element_type=jnp.float32).astype(jnp.bfloat16)
    )
    return (state_cols.astype(jnp.float32) + down_cols).astype(jnp.bfloat16)


def shards(
    residual,
    queries,
    new_keys,
    new_values,
    pool_keys,
    pool_values,
    cache_len,
    prefix_group,
    prefix_len,
    span_rows,
    span_offset,
    out_weight,
    norm_gain,
    gate_weight,
    up_weight,
    down_weight,
):
    total_rows = residual.shape[0]
    width = residual.shape[1]
    device = lax.axis_index("req")
    devices = lax.axis_size("req")
    bucket = (total_rows - DEC + devices - 1) // devices
    spread = bucket * devices
    bal = total_rows // 2
    counts = DEC + span_rows
    ends = jnp.cumsum(counts)
    firsts = ends - counts
    first = firsts[device]
    own_count = counts[device]
    shift = first % devices

    def outbound(rows):
        grid = rows[:spread].reshape(bucket, devices, rows.shape[1])
        return jnp.transpose(jnp.roll(grid, shift, axis=1), (1, 0, 2))

    send_resid = outbound(residual)
    got_resid = lax.all_to_all(send_resid, "req", split_axis=0, concat_axis=0, tiled=True)
    decode_mask = build_decode_mask(cache_len, prefix_group, prefix_len)
    sent_parts = attention_parts(
        queries, new_keys, new_values, pool_keys, pool_values, decode_mask, span_offset[0], outbound
    )
    got_resid, sent_parts[-1] = lax.optimization_barrier((got_resid, sent_parts[-1]))
    got_parts = [
        lax.all_to_all(part, "req", split_axis=0, concat_axis=0, tiled=True)
        for part in sent_parts
    ]

    slots = jnp.arange(bal, dtype=jnp.int32)
    wanted = slots * devices + device
    src_dev = jnp.sum((ends[None, :] <= wanted[:, None]).astype(jnp.int32), axis=1)
    src_dev = jnp.minimum(src_dev, devices - 1)
    src_pos = jnp.clip((wanted - firsts[src_dev]) // devices, 0, bucket - 1)
    flat_idx = src_dev * bucket + src_pos
    dense_attn = jnp.concatenate(
        [got.reshape(spread, got.shape[2])[flat_idx] for got in got_parts], axis=1
    )
    dense_resid = got_resid.reshape(spread, width)[flat_idx]
    mixed = finish(
        dense_attn, dense_resid, out_weight, norm_gain, gate_weight, up_weight, down_weight
    )
    lane = (device - firsts) % devices
    row_of = jnp.arange(bucket, dtype=jnp.int32)[None, :] * devices + lane[:, None]
    back_valid = row_of < counts[:, None]
    back_start = (firsts + lane) // devices
    padded = jnp.concatenate([mixed, jnp.zeros((bucket, width), mixed.dtype)], axis=0)
    slabs = jnp.stack(
        [lax.dynamic_slice_in_dim(padded, back_start[k], bucket, 0) for k in range(devices)]
    )
    picked = jnp.where(back_valid[:, :, None], slabs, jnp.zeros((), slabs.dtype))
    returned = lax.all_to_all(picked, "req", split_axis=0, concat_axis=0, tiled=True)
    restored = jnp.roll(jnp.transpose(returned, (1, 0, 2)), -shift, axis=1).reshape(spread, width)
    if spread < total_rows:
        restored = jnp.concatenate(
            [restored, jnp.zeros((total_rows - spread, width), restored.dtype)], axis=0
        )
    is_live = jnp.arange(total_rows, dtype=jnp.int32) < own_count
    return jnp.where(is_live[:, None], restored, jnp.zeros((), jnp.bfloat16))


def solution(mesh):
    placed = (
        P("req", "grp"),
        P("req", "grp"),
        P("req", "grp"),
        P("req", "grp"),
        P("req", "grp"),
        P("req", "grp"),
        P("req"),
        P("req"),
        P("req"),
        P(),
        P("req"),
        P("grp", None),
        P(),
        P(None, "grp"),
        P(None, "grp"),
        P("grp", None),
    )
    return jax.shard_map(
        shards, mesh=mesh, in_specs=placed, out_specs=P("req", "grp"), check_vma=False
    )
```

```python
import functools

import jax
import jax.numpy as jnp
from jax import lax
from jax.experimental import pallas as pl
from jax.experimental.pallas import tpu as pltpu
from jax.sharding import PartitionSpec as P

HEADS = 32
KV_HEADS = 8
HEAD_DIM = 64
DEC = 8
REG = 512


MASKED_SCORE = -1e30


SCALE = HEAD_DIM ** (-0.5)
QBLK = 256


def span_kernel(kv_index, start_ref, q_ref, kp_ref, vp_ref, kf_ref, vf_ref, o_ref):
    span_start = start_ref[0]
    half = HEAD_DIM

    def pick(ref, lo, hi):
        return ref[lo:hi, kv_index * half : (kv_index + 1) * half]

    rows = q_ref.shape[0]
    prior = kp_ref.shape[0]
    kp = pick(kp_ref, 0, prior)
    vp = pick(vp_ref, 0, prior)
    for blk in range(rows // QBLK):
        lo = blk * QBLK
        hi = lo + QBLK
        kf = pick(kf_ref, 0, hi)
        vf = pick(vf_ref, 0, hi)
        t_p = lax.broadcasted_iota(jnp.int32, (QBLK, prior), 1)
        prior_seen = t_p < span_start
        q_pos = lax.broadcasted_iota(jnp.int32, (QBLK, hi), 0) + lo
        k_pos = lax.broadcasted_iota(jnp.int32, (QBLK, hi), 1)
        seen = (k_pos >= DEC) & (k_pos <= q_pos)
        for hh in range(2):
            q = q_ref[lo:hi, hh * half : (hh + 1) * half] * jnp.asarray(SCALE, q_ref.dtype)
            s_p = lax.dot_general(
                q, kp, (((1,), (1,)), ((), ())), preferred_element_type=jnp.float32
            )
            s_f = lax.dot_general(
                q, kf, (((1,), (1,)), ((), ())), preferred_element_type=jnp.float32
            )
            s_p = jnp.where(prior_seen, s_p, MASKED_SCORE)
            s_f = jnp.where(seen, s_f, MASKED_SCORE)
            highest = jnp.maximum(
                jnp.max(s_p, axis=1, keepdims=True), jnp.max(s_f, axis=1, keepdims=True)
            )
            e_p = jnp.exp(s_p - highest)
            e_f = jnp.exp(s_f - highest)
            totals = jnp.sum(e_p, axis=1, keepdims=True) + jnp.sum(e_f, axis=1, keepdims=True)
            inverse = 1.0 / totals
            p_p = (e_p * inverse).astype(jnp.bfloat16)
            p_f = (e_f * inverse).astype(jnp.bfloat16)
            out = jnp.dot(p_p, vp, preferred_element_type=jnp.float32) + jnp.dot(
                p_f, vf, preferred_element_type=jnp.float32
            )
            o_ref[lo:hi, hh * half : (hh + 1) * half] = out.astype(o_ref.dtype)


def span_attention(queries, pool_keys, pool_values, new_keys, new_values, span_start, cached, kv_index):
    rows, width = queries.shape
    kv_width = new_keys.shape[1]
    prior = REG
    lanes = 2 * HEAD_DIM
    heads = width // HEAD_DIM
    kv = kv_width // HEAD_DIM
    steps = width // lanes // kv
    base = kv_index * steps
    q_spec = pl.BlockSpec((rows, lanes), lambda c, s: (0, base + c))
    o_spec = pl.BlockSpec((rows, lanes), lambda c, s: (0, c))
    p_spec = pl.BlockSpec((prior, kv_width), lambda c, s: (cached // prior, 0))
    f_spec = pl.BlockSpec((rows, kv_width), lambda c, s: (0, 0))
    flops = 4 * (heads // kv) * rows * (prior + rows // 2) * HEAD_DIM
    cost = pl.CostEstimate(
        flops=16 * flops,
        transcendentals=(heads // kv) * rows * (prior + rows // 2),
        bytes_accessed=2 * (2 * rows * width // kv + 2 * (prior + rows) * kv_width),
    )
    return pl.pallas_call(
        functools.partial(span_kernel, kv_index),
        out_shape=jax.ShapeDtypeStruct((rows, steps * lanes), jnp.bfloat16),
        grid_spec=pltpu.PrefetchScalarGridSpec(
            num_scalar_prefetch=1,
            grid=(steps,),
            in_specs=[q_spec, p_spec, p_spec, f_spec, f_spec],
            out_specs=o_spec,
        ),
        cost_estimate=cost,
    )(span_start.reshape(1).astype(jnp.int32), queries, pool_keys, pool_values, new_keys, new_values)


def decode_attention(queries, new_keys, new_values, pool_keys, pool_values, decode_mask):
    kv = new_keys.shape[1] // HEAD_DIM
    heads = queries.shape[1] // HEAD_DIM
    per_kv = heads // kv
    cached = DEC * REG
    q = queries[:DEC].reshape(DEC, heads, HEAD_DIM)
    owner = jnp.arange(heads, dtype=jnp.int32) // per_kv
    lanes = [
        jnp.where((owner == j)[None, :, None], q, jnp.zeros((), q.dtype)) for j in range(kv)
    ]
    q_ext = jnp.concatenate(lanes, axis=2)
    s_c = jnp.einsum("rhc,tc->rht", q_ext, pool_keys[:cached], preferred_element_type=jnp.float32)
    s_n = jnp.einsum("rhc,tc->rht", q_ext, new_keys[:DEC], preferred_element_type=jnp.float32)
    s_c = jnp.where(decode_mask[:, None, :cached], s_c * SCALE, MASKED_SCORE)
    s_n = jnp.where(decode_mask[:, None, cached:], s_n * SCALE, MASKED_SCORE)
    highest = jnp.maximum(
        jnp.max(s_c, axis=2, keepdims=True), jnp.max(s_n, axis=2, keepdims=True)
    )
    e_c = jnp.exp(s_c - highest)
    e_n = jnp.exp(s_n - highest)
    totals = jnp.sum(e_c, axis=2, keepdims=True) + jnp.sum(e_n, axis=2, keepdims=True)
    p_c = (e_c / totals).astype(jnp.bfloat16)
    p_n = (e_n / totals).astype(jnp.bfloat16)
    full = jnp.einsum(
        "rht,tc->rhc", p_c, pool_values[:cached], preferred_element_type=jnp.float32
    ) + jnp.einsum("rht,tc->rhc", p_n, new_values[:DEC], preferred_element_type=jnp.float32)
    out = full[:, :, 0:HEAD_DIM]
    for j in range(1, kv):
        out = jnp.where(
            (owner == j)[None, :, None], full[:, :, j * HEAD_DIM : (j + 1) * HEAD_DIM], out
        )
    return out.astype(jnp.bfloat16).reshape(DEC, heads * HEAD_DIM)


def build_decode_mask(cache_len, prefix_group, prefix_len):
    position = jnp.arange(DEC * REG, dtype=jnp.int32)
    region = position // REG
    offset = position % REG
    request = jnp.arange(DEC, dtype=jnp.int32)
    shared = (region[None, :] == prefix_group[:, None]) & (offset[None, :] < prefix_len[:, None])
    owned = (
        (region[None, :] == request[:, None])
        & (offset[None, :] >= prefix_len[:, None])
        & (offset[None, :] < cache_len[:, None])
    )
    return jnp.concatenate([shared | owned, jnp.eye(DEC, dtype=jnp.bool_)], axis=1)


def attention_parts(queries, new_keys, new_values, pool_keys, pool_values, decode_mask, span_start, send):
    cached = DEC * REG
    kv = new_keys.shape[1] // HEAD_DIM
    part_width = queries.shape[1] // kv
    decode_rows = decode_attention(
        queries, new_keys, new_values, pool_keys, pool_values, decode_mask
    )
    sent = []
    for j in range(kv):
        span_rows = span_attention(
            queries, pool_keys, pool_values, new_keys, new_values, span_start, cached, j
        )
        mine = decode_rows[:, j * part_width : (j + 1) * part_width]
        outgoing = send(lax.dynamic_update_slice(span_rows, mine, (0, 0)))
        if j + 1 < kv:
            outgoing, queries = lax.optimization_barrier((outgoing, queries))
        sent.append(outgoing)
    return sent


def grp_block(x, index, width):
    return lax.dynamic_slice_in_dim(x, index * width, width, 1)


def grp_reduce_scatter(partial):
    parts = lax.axis_size("grp")
    width = partial.shape[1] // parts
    if parts != 4:
        return lax.psum_scatter(partial, "grp", scatter_dimension=1, tiled=True).astype(
            jnp.float32
        )
    me = lax.axis_index("grp")
    near = [(i, i ^ 1) for i in range(parts)]
    far = [(i, i ^ 2) for i in range(parts)]
    outgoing = jnp.stack([grp_block(partial, me ^ 1, width), grp_block(partial, me ^ 3, width)])
    incoming = lax.ppermute(outgoing, "grp", near)
    own = grp_block(partial, me, width).astype(jnp.float32) + incoming[0].astype(jnp.float32)
    other = grp_block(partial, me ^ 2, width).astype(jnp.float32) + incoming[1].astype(
        jnp.float32
    )
    arrived = lax.ppermute(other.astype(jnp.bfloat16), "grp", far)
    return own + arrived.astype(jnp.float32)


def grp_reduce_scatter_blocks(block_of, total):
    parts = lax.axis_size("grp")
    width = total // parts
    if parts != 4:
        whole = jnp.concatenate([block_of(k, width) for k in range(parts)], axis=1)
        return grp_reduce_scatter(whole)
    me = lax.axis_index("grp")
    near = [(i, i ^ 1) for i in range(parts)]
    far = [(i, i ^ 2) for i in range(parts)]
    outgoing = jnp.stack([block_of(me ^ 1, width), block_of(me ^ 3, width)])
    incoming = lax.ppermute(outgoing, "grp", near)
    other = block_of(me ^ 2, width).astype(jnp.float32) + incoming[1].astype(jnp.float32)
    arrived = lax.ppermute(other.astype(jnp.bfloat16), "grp", far)
    own = block_of(me, width).astype(jnp.float32) + incoming[0].astype(jnp.float32)
    return own + arrived.astype(jnp.float32)


def grp_all_gather(block):
    parts = lax.axis_size("grp")
    if parts != 4:
        return lax.all_gather(block, "grp", axis=1, tiled=True)
    me = lax.axis_index("grp")
    near = [(i, i ^ 1) for i in range(parts)]
    far = [(i, i ^ 2) for i in range(parts)]
    across = lax.ppermute(block, "grp", far)
    pair = lax.ppermute(jnp.stack([block, across]), "grp", near)
    held = jnp.stack([block, pair[0], across, pair[1]])
    pieces = [lax.dynamic_index_in_dim(held, k ^ me, 0, keepdims=False) for k in range(parts)]
    return jnp.concatenate(pieces, axis=1)


def finish(attn_rows, resid_rows, out_weight, norm_gain, gate_weight, up_weight, down_weight):
    partial_value = jnp.dot(attn_rows, out_weight, preferred_element_type=jnp.float32)
    proj_cols = grp_reduce_scatter(partial_value.astype(jnp.bfloat16))
    state_cols = (resid_rows.astype(jnp.float32) + proj_cols).astype(jnp.bfloat16)
    state_full = grp_all_gather(state_cols)
    state32 = state_full.astype(jnp.float32)
    normed = (
        state32 * lax.rsqrt(jnp.mean(state32 * state32, axis=1, keepdims=True) + 1e-05) * norm_gain
    ).astype(jnp.bfloat16)
    gate = jnp.dot(normed, gate_weight, preferred_element_type=jnp.float32)
    upval = jnp.dot(normed, up_weight, preferred_element_type=jnp.float32)
    inner = (jax.nn.silu(gate) * upval).astype(jnp.bfloat16)
    down_cols = grp_reduce_scatter_blocks(
        lambda index, width: jnp.dot(
            inner, grp_block(down_weight, index, width), preferred_element_type=jnp.float32
        ).astype(jnp.bfloat16),
        down_weight.shape[1],
    )
    return (state_cols.astype(jnp.float32) + down_cols).astype(jnp.bfloat16)


def shards(
    residual,
    queries,
    new_keys,
    new_values,
    pool_keys,
    pool_values,
    cache_len,
    prefix_group,
    prefix_len,
    span_rows,
    span_offset,
    out_weight,
    norm_gain,
    gate_weight,
    up_weight,
    down_weight,
):
    total_rows = residual.shape[0]
    width = residual.shape[1]
    device = lax.axis_index("req")
    devices = lax.axis_size("req")
    bucket = (total_rows - DEC + devices - 1) // devices
    spread = bucket * devices
    bal = total_rows // 2
    counts = DEC + span_rows
    ends = jnp.cumsum(counts)
    firsts = ends - counts
    first = firsts[device]
    own_count = counts[device]
    shift = first % devices

    def outbound(rows):
        grid = rows[:spread].reshape(bucket, devices, rows.shape[1])
        return jnp.transpose(jnp.roll(grid, shift, axis=1), (1, 0, 2))

    send_resid = outbound(residual)
    got_resid = lax.all_to_all(send_resid, "req", split_axis=0, concat_axis=0, tiled=True)
    decode_mask = build_decode_mask(cache_len, prefix_group, prefix_len)
    sent_parts = attention_parts(
        queries, new_keys, new_values, pool_keys, pool_values, decode_mask, span_offset[0], outbound
    )
    got_resid, sent_parts[-1] = lax.optimization_barrier((got_resid, sent_parts[-1]))
    got_parts = [
        lax.all_to_all(part, "req", split_axis=0, concat_axis=0, tiled=True)
        for part in sent_parts
    ]

    slots = jnp.arange(bal, dtype=jnp.int32)
    wanted = slots * devices + device
    src_dev = jnp.sum((ends[None, :] <= wanted[:, None]).astype(jnp.int32), axis=1)
    src_dev = jnp.minimum(src_dev, devices - 1)
    src_pos = jnp.clip((wanted - firsts[src_dev]) // devices, 0, bucket - 1)
    flat_idx = src_dev * bucket + src_pos
    dense_attn = jnp.concatenate(
        [got.reshape(spread, got.shape[2])[flat_idx] for got in got_parts], axis=1
    )
    dense_resid = got_resid.reshape(spread, width)[flat_idx]
    mixed = finish(
        dense_attn, dense_resid, out_weight, norm_gain, gate_weight, up_weight, down_weight
    )
    lane = (device - firsts) % devices
    row_of = jnp.arange(bucket, dtype=jnp.int32)[None, :] * devices + lane[:, None]
    back_valid = row_of < counts[:, None]
    back_start = (firsts + lane) // devices
    padded = jnp.concatenate([mixed, jnp.zeros((bucket, width), mixed.dtype)], axis=0)
    slabs = jnp.stack(
        [lax.dynamic_slice_in_dim(padded, back_start[k], bucket, 0) for k in range(devices)]
    )
    picked = jnp.where(back_valid[:, :, None], slabs, jnp.zeros((), slabs.dtype))
    returned = lax.all_to_all(picked, "req", split_axis=0, concat_axis=0, tiled=True)
    restored = jnp.roll(jnp.transpose(returned, (1, 0, 2)), -shift, axis=1).reshape(spread, width)
    if spread < total_rows:
        restored = jnp.concatenate(
            [restored, jnp.zeros((total_rows - spread, width), restored.dtype)], axis=0
        )
    is_live = jnp.arange(total_rows, dtype=jnp.int32) < own_count
    return jnp.where(is_live[:, None], restored, jnp.zeros((), jnp.bfloat16))


def solution(mesh):
    placed = (
        P("req", "grp"),
        P("req", "grp"),
        P("req", "grp"),
        P("req", "grp"),
        P("req", "grp"),
        P("req", "grp"),
        P("req"),
        P("req"),
        P("req"),
        P(),
        P("req"),
        P("grp", None),
        P(),
        P(None, "grp"),
        P(None, "grp"),
        P("grp", None),
    )
    return jax.shard_map(
        shards, mesh=mesh, in_specs=placed, out_specs=P("req", "grp"), check_vma=False
    )
```

```python
import functools

import jax
import jax.numpy as jnp
from jax import lax
from jax.experimental import pallas as pl
from jax.experimental.pallas import tpu as pltpu
from jax.sharding import PartitionSpec as P

HEADS = 32
KV_HEADS = 8
HEAD_DIM = 64
DEC = 8
REG = 512


MASKED_SCORE = -1e30


SCALE = HEAD_DIM ** (-0.5)
QBLK = 256


def span_kernel(kv_index, start_ref, q_ref, kp_ref, vp_ref, kf_ref, vf_ref, o_ref):
    span_start = start_ref[0]
    half = HEAD_DIM

    def pick(ref, lo, hi):
        return ref[lo:hi, kv_index * half : (kv_index + 1) * half]

    rows = q_ref.shape[0]
    prior = kp_ref.shape[0]
    kp = pick(kp_ref, 0, prior)
    vp = pick(vp_ref, 0, prior)
    for blk in range(rows // QBLK):
        lo = blk * QBLK
        hi = lo + QBLK
        kf = pick(kf_ref, 0, hi)
        vf = pick(vf_ref, 0, hi)
        t_p = lax.broadcasted_iota(jnp.int32, (QBLK, prior), 1)
        prior_seen = t_p < span_start
        q_pos = lax.broadcasted_iota(jnp.int32, (QBLK, hi), 0) + lo
        k_pos = lax.broadcasted_iota(jnp.int32, (QBLK, hi), 1)
        seen = (k_pos >= DEC) & (k_pos <= q_pos)
        for hh in range(2):
            q = q_ref[lo:hi, hh * half : (hh + 1) * half] * jnp.asarray(SCALE, q_ref.dtype)
            s_p = lax.dot_general(
                q, kp, (((1,), (1,)), ((), ())), preferred_element_type=jnp.float32
            )
            s_f = lax.dot_general(
                q, kf, (((1,), (1,)), ((), ())), preferred_element_type=jnp.float32
            )
            s_p = jnp.where(prior_seen, s_p, MASKED_SCORE)
            s_f = jnp.where(seen, s_f, MASKED_SCORE)
            highest = jnp.maximum(
                jnp.max(s_p, axis=1, keepdims=True), jnp.max(s_f, axis=1, keepdims=True)
            )
            e_p = jnp.exp(s_p - highest)
            e_f = jnp.exp(s_f - highest)
            totals = jnp.sum(e_p, axis=1, keepdims=True) + jnp.sum(e_f, axis=1, keepdims=True)
            inverse = 1.0 / totals
            p_p = (e_p * inverse).astype(jnp.bfloat16)
            p_f = (e_f * inverse).astype(jnp.bfloat16)
            out = jnp.dot(p_p, vp, preferred_element_type=jnp.float32) + jnp.dot(
                p_f, vf, preferred_element_type=jnp.float32
            )
            o_ref[lo:hi, hh * half : (hh + 1) * half] = out.astype(o_ref.dtype)


def span_attention(queries, pool_keys, pool_values, new_keys, new_values, span_start, cached, kv_index):
    rows, width = queries.shape
    kv_width = new_keys.shape[1]
    prior = REG
    lanes = 2 * HEAD_DIM
    heads = width // HEAD_DIM
    kv = kv_width // HEAD_DIM
    steps = width // lanes // kv
    base = kv_index * steps
    q_spec = pl.BlockSpec((rows, lanes), lambda c, s: (0, base + c))
    o_spec = pl.BlockSpec((rows, lanes), lambda c, s: (0, c))
    p_spec = pl.BlockSpec((prior, kv_width), lambda c, s: (cached // prior, 0))
    f_spec = pl.BlockSpec((rows, kv_width), lambda c, s: (0, 0))
    flops = 4 * (heads // kv) * rows * (prior + rows // 2) * HEAD_DIM
    cost = pl.CostEstimate(
        flops=16 * flops,
        transcendentals=(heads // kv) * rows * (prior + rows // 2),
        bytes_accessed=2 * (2 * rows * width // kv + 2 * (prior + rows) * kv_width),
    )
    return pl.pallas_call(
        functools.partial(span_kernel, kv_index),
        out_shape=jax.ShapeDtypeStruct((rows, steps * lanes), jnp.bfloat16),
        grid_spec=pltpu.PrefetchScalarGridSpec(
            num_scalar_prefetch=1,
            grid=(steps,),
            in_specs=[q_spec, p_spec, p_spec, f_spec, f_spec],
            out_specs=o_spec,
        ),
        cost_estimate=cost,
    )(span_start.reshape(1).astype(jnp.int32), queries, pool_keys, pool_values, new_keys, new_values)


def decode_attention(queries, new_keys, new_values, pool_keys, pool_values, decode_mask):
    kv = new_keys.shape[1] // HEAD_DIM
    heads = queries.shape[1] // HEAD_DIM
    per_kv = heads // kv
    cached = DEC * REG
    q = queries[:DEC].reshape(DEC, heads, HEAD_DIM)
    owner = jnp.arange(heads, dtype=jnp.int32) // per_kv
    lanes = [
        jnp.where((owner == j)[None, :, None], q, jnp.zeros((), q.dtype)) for j in range(kv)
    ]
    q_ext = jnp.concatenate(lanes, axis=2)
    s_c = jnp.einsum("rhc,tc->rht", q_ext, pool_keys[:cached], preferred_element_type=jnp.float32)
    s_n = jnp.einsum("rhc,tc->rht", q_ext, new_keys[:DEC], preferred_element_type=jnp.float32)
    s_c = jnp.where(decode_mask[:, None, :cached], s_c * SCALE, MASKED_SCORE)
    s_n = jnp.where(decode_mask[:, None, cached:], s_n * SCALE, MASKED_SCORE)
    highest = jnp.maximum(
        jnp.max(s_c, axis=2, keepdims=True), jnp.max(s_n, axis=2, keepdims=True)
    )
    e_c = jnp.exp(s_c - highest)
    e_n = jnp.exp(s_n - highest)
    totals = jnp.sum(e_c, axis=2, keepdims=True) + jnp.sum(e_n, axis=2, keepdims=True)
    p_c = (e_c / totals).astype(jnp.bfloat16)
    p_n = (e_n / totals).astype(jnp.bfloat16)
    full = jnp.einsum(
        "rht,tc->rhc", p_c, pool_values[:cached], preferred_element_type=jnp.float32
    ) + jnp.einsum("rht,tc->rhc", p_n, new_values[:DEC], preferred_element_type=jnp.float32)
    out = full[:, :, 0:HEAD_DIM]
    for j in range(1, kv):
        out = jnp.where(
            (owner == j)[None, :, None], full[:, :, j * HEAD_DIM : (j + 1) * HEAD_DIM], out
        )
    return out.astype(jnp.bfloat16).reshape(DEC, heads * HEAD_DIM)


def build_decode_mask(cache_len, prefix_group, prefix_len):
    position = jnp.arange(DEC * REG, dtype=jnp.int32)
    region = position // REG
    offset = position % REG
    request = jnp.arange(DEC, dtype=jnp.int32)
    shared = (region[None, :] == prefix_group[:, None]) & (offset[None, :] < prefix_len[:, None])
    owned = (
        (region[None, :] == request[:, None])
        & (offset[None, :] >= prefix_len[:, None])
        & (offset[None, :] < cache_len[:, None])
    )
    return jnp.concatenate([shared | owned, jnp.eye(DEC, dtype=jnp.bool_)], axis=1)


def attention_parts(queries, new_keys, new_values, pool_keys, pool_values, decode_mask, span_start, send):
    cached = DEC * REG
    kv = new_keys.shape[1] // HEAD_DIM
    part_width = queries.shape[1] // kv
    decode_rows = decode_attention(
        queries, new_keys, new_values, pool_keys, pool_values, decode_mask
    )
    sent = []
    for j in range(kv):
        span_rows = span_attention(
            queries, pool_keys, pool_values, new_keys, new_values, span_start, cached, j
        )
        mine = decode_rows[:, j * part_width : (j + 1) * part_width]
        outgoing = send(lax.dynamic_update_slice(span_rows, mine, (0, 0)))
        if j + 1 < kv:
            outgoing, queries = lax.optimization_barrier((outgoing, queries))
        sent.append(outgoing)
    return sent


def grp_block(x, index, width):
    return lax.dynamic_slice_in_dim(x, index * width, width, 1)


def grp_reduce_scatter(partial):
    parts = lax.axis_size("grp")
    width = partial.shape[1] // parts
    if parts != 4:
        return lax.psum_scatter(partial, "grp", scatter_dimension=1, tiled=True).astype(
            jnp.float32
        )
    me = lax.axis_index("grp")
    near = [(i, i ^ 1) for i in range(parts)]
    far = [(i, i ^ 2) for i in range(parts)]
    outgoing = jnp.stack([grp_block(partial, me ^ 1, width), grp_block(partial, me ^ 3, width)])
    incoming = lax.ppermute(outgoing, "grp", near)
    own = grp_block(partial, me, width).astype(jnp.float32) + incoming[0].astype(jnp.float32)
    other = grp_block(partial, me ^ 2, width).astype(jnp.float32) + incoming[1].astype(
        jnp.float32
    )
    arrived = lax.ppermute(other.astype(jnp.bfloat16), "grp", far)
    return own + arrived.astype(jnp.float32)


def grp_reduce_scatter_blocks(block_of, total):
    parts = lax.axis_size("grp")
    width = total // parts
    if parts != 4:
        whole = jnp.concatenate([block_of(k, width) for k in range(parts)], axis=1)
        return grp_reduce_scatter(whole)
    me = lax.axis_index("grp")
    near = [(i, i ^ 1) for i in range(parts)]
    far = [(i, i ^ 2) for i in range(parts)]
    outgoing = jnp.stack([block_of(me ^ 1, width), block_of(me ^ 3, width)])
    incoming = lax.ppermute(outgoing, "grp", near)
    other = block_of(me ^ 2, width).astype(jnp.float32) + incoming[1].astype(jnp.float32)
    arrived = lax.ppermute(other.astype(jnp.bfloat16), "grp", far)
    own = block_of(me, width).astype(jnp.float32) + incoming[0].astype(jnp.float32)
    return own + arrived.astype(jnp.float32)


def grp_all_gather(block):
    parts = lax.axis_size("grp")
    if parts != 4:
        return lax.all_gather(block, "grp", axis=1, tiled=True)
    me = lax.axis_index("grp")
    near = [(i, i ^ 1) for i in range(parts)]
    far = [(i, i ^ 2) for i in range(parts)]
    beside = lax.ppermute(block, "grp", near)
    across = lax.ppermute(block, "grp", far)
    diagonal = lax.ppermute(across, "grp", near)
    held = jnp.stack([block, beside, across, diagonal])
    pieces = [lax.dynamic_index_in_dim(held, k ^ me, 0, keepdims=False) for k in range(parts)]
    return jnp.concatenate(pieces, axis=1)


def finish(attn_rows, resid_rows, out_weight, norm_gain, gate_weight, up_weight, down_weight):
    proj_cols = grp_reduce_scatter_blocks(
        lambda index, width: jnp.dot(
            attn_rows, grp_block(out_weight, index, width), preferred_element_type=jnp.float32
        ).astype(jnp.bfloat16),
        out_weight.shape[1],
    )
    state_cols = (resid_rows.astype(jnp.float32) + proj_cols).astype(jnp.bfloat16)
    state_full = grp_all_gather(state_cols)
    state32 = state_full.astype(jnp.float32)
    normed = (
        state32 * lax.rsqrt(jnp.mean(state32 * state32, axis=1, keepdims=True) + 1e-05) * norm_gain
    ).astype(jnp.bfloat16)
    gate = jnp.dot(normed, gate_weight, preferred_element_type=jnp.float32)
    upval = jnp.dot(normed, up_weight, preferred_element_type=jnp.float32)
    inner = (jax.nn.silu(gate) * upval).astype(jnp.bfloat16)
    down_cols = grp_reduce_scatter_blocks(
        lambda index, width: jnp.dot(
            inner, grp_block(down_weight, index, width), preferred_element_type=jnp.float32
        ).astype(jnp.bfloat16),
        down_weight.shape[1],
    )
    return (state_cols.astype(jnp.float32) + down_cols).astype(jnp.bfloat16)


def shards(
    residual,
    queries,
    new_keys,
    new_values,
    pool_keys,
    pool_values,
    cache_len,
    prefix_group,
    prefix_len,
    span_rows,
    span_offset,
    out_weight,
    norm_gain,
    gate_weight,
    up_weight,
    down_weight,
):
    total_rows = residual.shape[0]
    width = residual.shape[1]
    device = lax.axis_index("req")
    devices = lax.axis_size("req")
    bucket = (total_rows - DEC + devices - 1) // devices
    spread = bucket * devices
    bal = total_rows // 2
    counts = DEC + span_rows
    ends = jnp.cumsum(counts)
    firsts = ends - counts
    first = firsts[device]
    own_count = counts[device]
    shift = first % devices

    def outbound(rows):
        grid = rows[:spread].reshape(bucket, devices, rows.shape[1])
        return jnp.transpose(jnp.roll(grid, shift, axis=1), (1, 0, 2))

    send_resid = outbound(residual)
    got_resid = lax.all_to_all(send_resid, "req", split_axis=0, concat_axis=0, tiled=True)
    decode_mask = build_decode_mask(cache_len, prefix_group, prefix_len)
    sent_parts = attention_parts(
        queries, new_keys, new_values, pool_keys, pool_values, decode_mask, span_offset[0], outbound
    )
    got_resid, sent_parts[-1] = lax.optimization_barrier((got_resid, sent_parts[-1]))
    got_parts = [
        lax.all_to_all(part, "req", split_axis=0, concat_axis=0, tiled=True)
        for part in sent_parts
    ]

    slots = jnp.arange(bal, dtype=jnp.int32)
    wanted = slots * devices + device
    src_dev = jnp.sum((ends[None, :] <= wanted[:, None]).astype(jnp.int32), axis=1)
    src_dev = jnp.minimum(src_dev, devices - 1)
    src_pos = jnp.clip((wanted - firsts[src_dev]) // devices, 0, bucket - 1)
    flat_idx = src_dev * bucket + src_pos
    dense_attn = jnp.concatenate(
        [got.reshape(spread, got.shape[2])[flat_idx] for got in got_parts], axis=1
    )
    dense_resid = got_resid.reshape(spread, width)[flat_idx]
    mixed = finish(
        dense_attn, dense_resid, out_weight, norm_gain, gate_weight, up_weight, down_weight
    )
    lane = (device - firsts) % devices
    row_of = jnp.arange(bucket, dtype=jnp.int32)[None, :] * devices + lane[:, None]
    back_valid = row_of < counts[:, None]
    back_start = (firsts + lane) // devices
    padded = jnp.concatenate([mixed, jnp.zeros((bucket, width), mixed.dtype)], axis=0)
    slabs = jnp.stack(
        [lax.dynamic_slice_in_dim(padded, back_start[k], bucket, 0) for k in range(devices)]
    )
    picked = jnp.where(back_valid[:, :, None], slabs, jnp.zeros((), slabs.dtype))
    returned = lax.all_to_all(picked, "req", split_axis=0, concat_axis=0, tiled=True)
    restored = jnp.roll(jnp.transpose(returned, (1, 0, 2)), -shift, axis=1).reshape(spread, width)
    if spread < total_rows:
        restored = jnp.concatenate(
            [restored, jnp.zeros((total_rows - spread, width), restored.dtype)], axis=0
        )
    is_live = jnp.arange(total_rows, dtype=jnp.int32) < own_count
    return jnp.where(is_live[:, None], restored, jnp.zeros((), jnp.bfloat16))


def solution(mesh):
    placed = (
        P("req", "grp"),
        P("req", "grp"),
        P("req", "grp"),
        P("req", "grp"),
        P("req", "grp"),
        P("req", "grp"),
        P("req"),
        P("req"),
        P("req"),
        P(),
        P("req"),
        P("grp", None),
        P(),
        P(None, "grp"),
        P(None, "grp"),
        P("grp", None),
    )
    return jax.shard_map(
        shards, mesh=mesh, in_specs=placed, out_specs=P("req", "grp"), check_vma=False
    )
```

```python
import functools

import jax
import jax.numpy as jnp
from jax import lax
from jax.experimental import pallas as pl
from jax.experimental.pallas import tpu as pltpu
from jax.sharding import PartitionSpec as P

HEADS = 32
KV_HEADS = 8
HEAD_DIM = 64
DEC = 8
REG = 512


MASKED_SCORE = -1e30


SCALE = HEAD_DIM ** (-0.5)
QBLK = 256


def span_kernel(kv_index, start_ref, q_ref, kp_ref, vp_ref, kf_ref, vf_ref, o_ref):
    span_start = start_ref[0]
    half = HEAD_DIM

    def pick(ref, lo, hi):
        return ref[lo:hi, kv_index * half : (kv_index + 1) * half]

    rows = q_ref.shape[0]
    prior = kp_ref.shape[0]
    kp = pick(kp_ref, 0, prior)
    vp = pick(vp_ref, 0, prior)
    for blk in range(rows // QBLK):
        lo = blk * QBLK
        hi = lo + QBLK
        kf = pick(kf_ref, 0, hi)
        vf = pick(vf_ref, 0, hi)
        t_p = lax.broadcasted_iota(jnp.int32, (QBLK, prior), 1)
        prior_seen = t_p < span_start
        q_pos = lax.broadcasted_iota(jnp.int32, (QBLK, hi), 0) + lo
        k_pos = lax.broadcasted_iota(jnp.int32, (QBLK, hi), 1)
        seen = (k_pos >= DEC) & (k_pos <= q_pos)
        for hh in range(2):
            q = q_ref[lo:hi, hh * half : (hh + 1) * half] * jnp.asarray(SCALE, q_ref.dtype)
            s_p = lax.dot_general(
                q, kp, (((1,), (1,)), ((), ())), preferred_element_type=jnp.float32
            )
            s_f = lax.dot_general(
                q, kf, (((1,), (1,)), ((), ())), preferred_element_type=jnp.float32
            )
            s_p = jnp.where(prior_seen, s_p, MASKED_SCORE)
            s_f = jnp.where(seen, s_f, MASKED_SCORE)
            highest = jnp.maximum(
                jnp.max(s_p, axis=1, keepdims=True), jnp.max(s_f, axis=1, keepdims=True)
            )
            e_p = jnp.exp(s_p - highest)
            e_f = jnp.exp(s_f - highest)
            totals = jnp.sum(e_p, axis=1, keepdims=True) + jnp.sum(e_f, axis=1, keepdims=True)
            inverse = 1.0 / totals
            p_p = (e_p * inverse).astype(jnp.bfloat16)
            p_f = (e_f * inverse).astype(jnp.bfloat16)
            out = jnp.dot(p_p, vp, preferred_element_type=jnp.float32) + jnp.dot(
                p_f, vf, preferred_element_type=jnp.float32
            )
            o_ref[lo:hi, hh * half : (hh + 1) * half] = out.astype(o_ref.dtype)


def span_attention(queries, pool_keys, pool_values, new_keys, new_values, span_start, cached, kv_index):
    rows, width = queries.shape
    kv_width = new_keys.shape[1]
    prior = REG
    lanes = 2 * HEAD_DIM
    heads = width // HEAD_DIM
    kv = kv_width // HEAD_DIM
    steps = width // lanes // kv
    base = kv_index * steps
    q_spec = pl.BlockSpec((rows, lanes), lambda c, s: (0, base + c))
    o_spec = pl.BlockSpec((rows, lanes), lambda c, s: (0, c))
    p_spec = pl.BlockSpec((prior, kv_width), lambda c, s: (cached // prior, 0))
    f_spec = pl.BlockSpec((rows, kv_width), lambda c, s: (0, 0))
    flops = 4 * (heads // kv) * rows * (prior + rows // 2) * HEAD_DIM
    cost = pl.CostEstimate(
        flops=16 * flops,
        transcendentals=(heads // kv) * rows * (prior + rows // 2),
        bytes_accessed=2 * (2 * rows * width // kv + 2 * (prior + rows) * kv_width),
    )
    return pl.pallas_call(
        functools.partial(span_kernel, kv_index),
        out_shape=jax.ShapeDtypeStruct((rows, steps * lanes), jnp.bfloat16),
        grid_spec=pltpu.PrefetchScalarGridSpec(
            num_scalar_prefetch=1,
            grid=(steps,),
            in_specs=[q_spec, p_spec, p_spec, f_spec, f_spec],
            out_specs=o_spec,
        ),
        cost_estimate=cost,
    )(span_start.reshape(1).astype(jnp.int32), queries, pool_keys, pool_values, new_keys, new_values)


def decode_attention(queries, new_keys, new_values, pool_keys, pool_values, decode_mask):
    kv = new_keys.shape[1] // HEAD_DIM
    heads = queries.shape[1] // HEAD_DIM
    per_kv = heads // kv
    cached = DEC * REG
    q = queries[:DEC].reshape(DEC, heads, HEAD_DIM)
    owner = jnp.arange(heads, dtype=jnp.int32) // per_kv
    lanes = [
        jnp.where((owner == j)[None, :, None], q, jnp.zeros((), q.dtype)) for j in range(kv)
    ]
    q_ext = jnp.concatenate(lanes, axis=2)
    s_c = jnp.einsum("rhc,tc->rht", q_ext, pool_keys[:cached], preferred_element_type=jnp.float32)
    s_n = jnp.einsum("rhc,tc->rht", q_ext, new_keys[:DEC], preferred_element_type=jnp.float32)
    s_c = jnp.where(decode_mask[:, None, :cached], s_c * SCALE, MASKED_SCORE)
    s_n = jnp.where(decode_mask[:, None, cached:], s_n * SCALE, MASKED_SCORE)
    highest = jnp.maximum(
        jnp.max(s_c, axis=2, keepdims=True), jnp.max(s_n, axis=2, keepdims=True)
    )
    e_c = jnp.exp(s_c - highest)
    e_n = jnp.exp(s_n - highest)
    totals = jnp.sum(e_c, axis=2, keepdims=True) + jnp.sum(e_n, axis=2, keepdims=True)
    p_c = (e_c / totals).astype(jnp.bfloat16)
    p_n = (e_n / totals).astype(jnp.bfloat16)
    full = jnp.einsum(
        "rht,tc->rhc", p_c, pool_values[:cached], preferred_element_type=jnp.float32
    ) + jnp.einsum("rht,tc->rhc", p_n, new_values[:DEC], preferred_element_type=jnp.float32)
    out = full[:, :, 0:HEAD_DIM]
    for j in range(1, kv):
        out = jnp.where(
            (owner == j)[None, :, None], full[:, :, j * HEAD_DIM : (j + 1) * HEAD_DIM], out
        )
    return out.astype(jnp.bfloat16).reshape(DEC, heads * HEAD_DIM)


def build_decode_mask(cache_len, prefix_group, prefix_len):
    position = jnp.arange(DEC * REG, dtype=jnp.int32)
    region = position // REG
    offset = position % REG
    request = jnp.arange(DEC, dtype=jnp.int32)
    shared = (region[None, :] == prefix_group[:, None]) & (offset[None, :] < prefix_len[:, None])
    owned = (
        (region[None, :] == request[:, None])
        & (offset[None, :] >= prefix_len[:, None])
        & (offset[None, :] < cache_len[:, None])
    )
    return jnp.concatenate([shared | owned, jnp.eye(DEC, dtype=jnp.bool_)], axis=1)


def attention_parts(queries, new_keys, new_values, pool_keys, pool_values, decode_mask, span_start, send):
    cached = DEC * REG
    kv = new_keys.shape[1] // HEAD_DIM
    part_width = queries.shape[1] // kv
    decode_rows = decode_attention(
        queries, new_keys, new_values, pool_keys, pool_values, decode_mask
    )
    sent = []
    for j in range(kv):
        span_rows = span_attention(
            queries, pool_keys, pool_values, new_keys, new_values, span_start, cached, j
        )
        mine = decode_rows[:, j * part_width : (j + 1) * part_width]
        outgoing = send(lax.dynamic_update_slice(span_rows, mine, (0, 0)))
        if j + 1 < kv:
            outgoing, queries = lax.optimization_barrier((outgoing, queries))
        sent.append(outgoing)
    return sent


def grp_block(x, index, width):
    return lax.dynamic_slice_in_dim(x, index * width, width, 1)


def grp_reduce_scatter(partial):
    parts = lax.axis_size("grp")
    width = partial.shape[1] // parts
    if parts != 4:
        return lax.psum_scatter(partial, "grp", scatter_dimension=1, tiled=True).astype(
            jnp.float32
        )
    me = lax.axis_index("grp")
    near = [(i, i ^ 1) for i in range(parts)]
    far = [(i, i ^ 2) for i in range(parts)]
    outgoing = jnp.stack([grp_block(partial, me ^ 1, width), grp_block(partial, me ^ 3, width)])
    incoming = lax.ppermute(outgoing, "grp", near)
    own = grp_block(partial, me, width).astype(jnp.float32) + incoming[0].astype(jnp.float32)
    other = grp_block(partial, me ^ 2, width).astype(jnp.float32) + incoming[1].astype(
        jnp.float32
    )
    arrived = lax.ppermute(other.astype(jnp.bfloat16), "grp", far)
    return own + arrived.astype(jnp.float32)


def grp_reduce_scatter_blocks(block_of, total):
    parts = lax.axis_size("grp")
    width = total // parts
    if parts != 4:
        whole = jnp.concatenate([block_of(k, width) for k in range(parts)], axis=1)
        return grp_reduce_scatter(whole)
    me = lax.axis_index("grp")
    near = [(i, i ^ 1) for i in range(parts)]
    far = [(i, i ^ 2) for i in range(parts)]
    outgoing = jnp.stack([block_of(me ^ 1, width), block_of(me ^ 3, width)])
    incoming = lax.ppermute(outgoing, "grp", near)
    other = block_of(me ^ 2, width).astype(jnp.float32) + incoming[1].astype(jnp.float32)
    arrived = lax.ppermute(other.astype(jnp.bfloat16), "grp", far)
    own = block_of(me, width).astype(jnp.float32) + incoming[0].astype(jnp.float32)
    return own + arrived.astype(jnp.float32)


def grp_all_gather(block):
    parts = lax.axis_size("grp")
    if parts != 4:
        return lax.all_gather(block, "grp", axis=1, tiled=True)
    me = lax.axis_index("grp")
    near = [(i, i ^ 1) for i in range(parts)]
    far = [(i, i ^ 2) for i in range(parts)]
    beside = lax.ppermute(block, "grp", near)
    across = lax.ppermute(block, "grp", far)
    diagonal = lax.ppermute(across, "grp", near)
    held = jnp.stack([block, beside, across, diagonal])
    pieces = [lax.dynamic_index_in_dim(held, k ^ me, 0, keepdims=False) for k in range(parts)]
    return jnp.concatenate(pieces, axis=1)


def finish(attn_rows, resid_rows, out_weight, norm_gain, gate_weight, up_weight, down_weight):
    partial_value = jnp.dot(attn_rows, out_weight, preferred_element_type=jnp.float32)
    proj_cols = grp_reduce_scatter(partial_value.astype(jnp.bfloat16))
    state_cols = (resid_rows.astype(jnp.float32) + proj_cols).astype(jnp.bfloat16)
    state_full = grp_all_gather(state_cols)
    state32 = state_full.astype(jnp.float32)
    normed = (
        state32 * lax.rsqrt(jnp.mean(state32 * state32, axis=1, keepdims=True) + 1e-05) * norm_gain
    ).astype(jnp.bfloat16)
    gate = jnp.dot(normed, gate_weight, preferred_element_type=jnp.float32)
    upval = jnp.dot(normed, up_weight, preferred_element_type=jnp.float32)
    inner = (jax.nn.silu(gate) * upval).astype(jnp.bfloat16)
    down_cols = grp_reduce_scatter_blocks(
        lambda index, width: jnp.dot(
            inner, grp_block(down_weight, index, width), preferred_element_type=jnp.float32
        ).astype(jnp.bfloat16),
        down_weight.shape[1],
    )
    return (state_cols.astype(jnp.float32) + down_cols).astype(jnp.bfloat16)


def shards(
    residual,
    queries,
    new_keys,
    new_values,
    pool_keys,
    pool_values,
    cache_len,
    prefix_group,
    prefix_len,
    span_rows,
    span_offset,
    out_weight,
    norm_gain,
    gate_weight,
    up_weight,
    down_weight,
):
    total_rows = residual.shape[0]
    width = residual.shape[1]
    device = lax.axis_index("req")
    devices = lax.axis_size("req")
    bucket = (total_rows - DEC + devices - 1) // devices
    spread = bucket * devices
    bal = total_rows // 2
    counts = DEC + span_rows
    ends = jnp.cumsum(counts)
    firsts = ends - counts
    first = firsts[device]
    own_count = counts[device]
    shift = first % devices

    def outbound(rows):
        grid = rows[:spread].reshape(bucket, devices, rows.shape[1])
        return jnp.transpose(jnp.roll(grid, shift, axis=1), (1, 0, 2))

    send_resid = outbound(residual)
    got_resid = lax.all_to_all(send_resid, "req", split_axis=0, concat_axis=0, tiled=True)
    decode_mask = build_decode_mask(cache_len, prefix_group, prefix_len)
    sent_parts = attention_parts(
        queries, new_keys, new_values, pool_keys, pool_values, decode_mask, span_offset[0], outbound
    )
    got_resid, sent_parts[-1] = lax.optimization_barrier((got_resid, sent_parts[-1]))
    got_parts = [
        lax.all_to_all(part, "req", split_axis=0, concat_axis=0, tiled=True)
        for part in sent_parts
    ]

    slots = jnp.arange(bal, dtype=jnp.int32)
    wanted = slots * devices + device
    src_dev = jnp.sum((ends[None, :] <= wanted[:, None]).astype(jnp.int32), axis=1)
    src_dev = jnp.minimum(src_dev, devices - 1)
    src_pos = jnp.clip((wanted - firsts[src_dev]) // devices, 0, bucket - 1)
    flat_idx = src_dev * bucket + src_pos
    dense_attn = jnp.concatenate(
        [got.reshape(spread, got.shape[2])[flat_idx] for got in got_parts], axis=1
    )
    dense_resid = got_resid.reshape(spread, width)[flat_idx]
    mixed = finish(
        dense_attn, dense_resid, out_weight, norm_gain, gate_weight, up_weight, down_weight
    )
    lane = (device - firsts) % devices
    row_of = jnp.arange(bucket, dtype=jnp.int32)[None, :] * devices + lane[:, None]
    back_valid = row_of < counts[:, None]
    back_start = (firsts + lane) // devices
    padded = jnp.concatenate([mixed, jnp.zeros((bucket, width), mixed.dtype)], axis=0)
    slabs = jnp.stack(
        [lax.dynamic_slice_in_dim(padded, back_start[k], bucket, 0) for k in range(devices)]
    )
    picked = jnp.where(back_valid[:, :, None], slabs, jnp.zeros((), slabs.dtype))
    returned = lax.all_to_all(picked, "req", split_axis=0, concat_axis=0, tiled=True)
    restored = jnp.roll(jnp.transpose(returned, (1, 0, 2)), -shift, axis=1).reshape(spread, width)
    if spread < total_rows:
        restored = jnp.concatenate(
            [restored, jnp.zeros((total_rows - spread, width), restored.dtype)], axis=0
        )
    is_live = jnp.arange(total_rows, dtype=jnp.int32) < own_count
    return jnp.where(is_live[:, None], restored, jnp.zeros((), jnp.bfloat16))


def solution(mesh):
    placed = (
        P("req", "grp"),
        P("req", "grp"),
        P("req", "grp"),
        P("req", "grp"),
        P("req", "grp"),
        P("req", "grp"),
        P("req"),
        P("req"),
        P("req"),
        P(),
        P("req"),
        P("grp", None),
        P(),
        P(None, "grp"),
        P(None, "grp"),
        P("grp", None),
    )
    return jax.shard_map(
        shards, mesh=mesh, in_specs=placed, out_specs=P("req", "grp"), check_vma=False
    )
```

```python
import functools

import jax
import jax.numpy as jnp
from jax import lax
from jax.experimental import pallas as pl
from jax.experimental.pallas import tpu as pltpu
from jax.sharding import PartitionSpec as P

HEADS = 32
KV_HEADS = 8
HEAD_DIM = 64
DEC = 8
REG = 512


MASKED_SCORE = -1e30


SCALE = HEAD_DIM ** (-0.5)
QBLK = 128


def span_kernel(kv_index, start_ref, q_ref, kp_ref, vp_ref, kf_ref, vf_ref, o_ref):
    span_start = start_ref[0]
    half = HEAD_DIM

    def pick(ref, lo, hi):
        return ref[lo:hi, kv_index * half : (kv_index + 1) * half]

    rows = q_ref.shape[0]
    prior = kp_ref.shape[0]
    kp = pick(kp_ref, 0, prior)
    vp = pick(vp_ref, 0, prior)
    for blk in range(rows // QBLK):
        lo = blk * QBLK
        hi = lo + QBLK
        kf = pick(kf_ref, 0, hi)
        vf = pick(vf_ref, 0, hi)
        t_p = lax.broadcasted_iota(jnp.int32, (QBLK, prior), 1)
        prior_seen = t_p < span_start
        q_pos = lax.broadcasted_iota(jnp.int32, (QBLK, hi), 0) + lo
        k_pos = lax.broadcasted_iota(jnp.int32, (QBLK, hi), 1)
        seen = (k_pos >= DEC) & (k_pos <= q_pos)
        for hh in range(2):
            q = q_ref[lo:hi, hh * half : (hh + 1) * half] * jnp.asarray(SCALE, q_ref.dtype)
            s_p = lax.dot_general(
                q, kp, (((1,), (1,)), ((), ())), preferred_element_type=jnp.float32
            )
            s_f = lax.dot_general(
                q, kf, (((1,), (1,)), ((), ())), preferred_element_type=jnp.float32
            )
            s_p = jnp.where(prior_seen, s_p, MASKED_SCORE)
            s_f = jnp.where(seen, s_f, MASKED_SCORE)
            highest = jnp.maximum(
                jnp.max(s_p, axis=1, keepdims=True), jnp.max(s_f, axis=1, keepdims=True)
            )
            e_p = jnp.exp(s_p - highest)
            e_f = jnp.exp(s_f - highest)
            totals = jnp.sum(e_p, axis=1, keepdims=True) + jnp.sum(e_f, axis=1, keepdims=True)
            inverse = 1.0 / totals
            p_p = (e_p * inverse).astype(jnp.bfloat16)
            p_f = (e_f * inverse).astype(jnp.bfloat16)
            out = jnp.dot(p_p, vp, preferred_element_type=jnp.float32) + jnp.dot(
                p_f, vf, preferred_element_type=jnp.float32
            )
            o_ref[lo:hi, hh * half : (hh + 1) * half] = out.astype(o_ref.dtype)


def span_attention(queries, pool_keys, pool_values, new_keys, new_values, span_start, cached, kv_index):
    rows, width = queries.shape
    kv_width = new_keys.shape[1]
    prior = REG
    lanes = 2 * HEAD_DIM
    heads = width // HEAD_DIM
    kv = kv_width // HEAD_DIM
    steps = width // lanes // kv
    base = kv_index * steps
    q_spec = pl.BlockSpec((rows, lanes), lambda c, s: (0, base + c))
    o_spec = pl.BlockSpec((rows, lanes), lambda c, s: (0, c))
    p_spec = pl.BlockSpec((prior, kv_width), lambda c, s: (cached // prior, 0))
    f_spec = pl.BlockSpec((rows, kv_width), lambda c, s: (0, 0))
    flops = 4 * (heads // kv) * rows * (prior + rows // 2) * HEAD_DIM
    cost = pl.CostEstimate(
        flops=16 * flops,
        transcendentals=(heads // kv) * rows * (prior + rows // 2),
        bytes_accessed=2 * (2 * rows * width // kv + 2 * (prior + rows) * kv_width),
    )
    return pl.pallas_call(
        functools.partial(span_kernel, kv_index),
        out_shape=jax.ShapeDtypeStruct((rows, steps * lanes), jnp.bfloat16),
        grid_spec=pltpu.PrefetchScalarGridSpec(
            num_scalar_prefetch=1,
            grid=(steps,),
            in_specs=[q_spec, p_spec, p_spec, f_spec, f_spec],
            out_specs=o_spec,
        ),
        cost_estimate=cost,
    )(span_start.reshape(1).astype(jnp.int32), queries, pool_keys, pool_values, new_keys, new_values)


def decode_attention(queries, new_keys, new_values, pool_keys, pool_values, decode_mask):
    kv = new_keys.shape[1] // HEAD_DIM
    heads = queries.shape[1] // HEAD_DIM
    per_kv = heads // kv
    cached = DEC * REG
    q = queries[:DEC].reshape(DEC, heads, HEAD_DIM)
    owner = jnp.arange(heads, dtype=jnp.int32) // per_kv
    lanes = [
        jnp.where((owner == j)[None, :, None], q, jnp.zeros((), q.dtype)) for j in range(kv)
    ]
    q_ext = jnp.concatenate(lanes, axis=2)
    s_c = jnp.einsum("rhc,tc->rht", q_ext, pool_keys[:cached], preferred_element_type=jnp.float32)
    s_n = jnp.einsum("rhc,tc->rht", q_ext, new_keys[:DEC], preferred_element_type=jnp.float32)
    s_c = jnp.where(decode_mask[:, None, :cached], s_c * SCALE, MASKED_SCORE)
    s_n = jnp.where(decode_mask[:, None, cached:], s_n * SCALE, MASKED_SCORE)
    highest = jnp.maximum(
        jnp.max(s_c, axis=2, keepdims=True), jnp.max(s_n, axis=2, keepdims=True)
    )
    e_c = jnp.exp(s_c - highest)
    e_n = jnp.exp(s_n - highest)
    totals = jnp.sum(e_c, axis=2, keepdims=True) + jnp.sum(e_n, axis=2, keepdims=True)
    p_c = (e_c / totals).astype(jnp.bfloat16)
    p_n = (e_n / totals).astype(jnp.bfloat16)
    full = jnp.einsum(
        "rht,tc->rhc", p_c, pool_values[:cached], preferred_element_type=jnp.float32
    ) + jnp.einsum("rht,tc->rhc", p_n, new_values[:DEC], preferred_element_type=jnp.float32)
    out = full[:, :, 0:HEAD_DIM]
    for j in range(1, kv):
        out = jnp.where(
            (owner == j)[None, :, None], full[:, :, j * HEAD_DIM : (j + 1) * HEAD_DIM], out
        )
    return out.astype(jnp.bfloat16).reshape(DEC, heads * HEAD_DIM)


def build_decode_mask(cache_len, prefix_group, prefix_len):
    position = jnp.arange(DEC * REG, dtype=jnp.int32)
    region = position // REG
    offset = position % REG
    request = jnp.arange(DEC, dtype=jnp.int32)
    shared = (region[None, :] == prefix_group[:, None]) & (offset[None, :] < prefix_len[:, None])
    owned = (
        (region[None, :] == request[:, None])
        & (offset[None, :] >= prefix_len[:, None])
        & (offset[None, :] < cache_len[:, None])
    )
    return jnp.concatenate([shared | owned, jnp.eye(DEC, dtype=jnp.bool_)], axis=1)


def attention_parts(queries, new_keys, new_values, pool_keys, pool_values, decode_mask, span_start, send):
    cached = DEC * REG
    kv = new_keys.shape[1] // HEAD_DIM
    part_width = queries.shape[1] // kv
    decode_rows = decode_attention(
        queries, new_keys, new_values, pool_keys, pool_values, decode_mask
    )
    sent = []
    for j in range(kv):
        span_rows = span_attention(
            queries, pool_keys, pool_values, new_keys, new_values, span_start, cached, j
        )
        mine = decode_rows[:, j * part_width : (j + 1) * part_width]
        outgoing = send(lax.dynamic_update_slice(span_rows, mine, (0, 0)))
        if j + 1 < kv:
            outgoing, queries = lax.optimization_barrier((outgoing, queries))
        sent.append(outgoing)
    return sent


def grp_block(x, index, width):
    return lax.dynamic_slice_in_dim(x, index * width, width, 1)


def grp_reduce_scatter(partial):
    parts = lax.axis_size("grp")
    width = partial.shape[1] // parts
    if parts != 4:
        return lax.psum_scatter(partial, "grp", scatter_dimension=1, tiled=True).astype(
            jnp.float32
        )
    me = lax.axis_index("grp")
    near = [(i, i ^ 1) for i in range(parts)]
    far = [(i, i ^ 2) for i in range(parts)]
    outgoing = jnp.stack([grp_block(partial, me ^ 1, width), grp_block(partial, me ^ 3, width)])
    incoming = lax.ppermute(outgoing, "grp", near)
    own = grp_block(partial, me, width).astype(jnp.float32) + incoming[0].astype(jnp.float32)
    other = grp_block(partial, me ^ 2, width).astype(jnp.float32) + incoming[1].astype(
        jnp.float32
    )
    arrived = lax.ppermute(other.astype(jnp.bfloat16), "grp", far)
    return own + arrived.astype(jnp.float32)


def grp_reduce_scatter_blocks(block_of, total):
    parts = lax.axis_size("grp")
    width = total // parts
    if parts != 4:
        whole = jnp.concatenate([block_of(k, width) for k in range(parts)], axis=1)
        return grp_reduce_scatter(whole)
    me = lax.axis_index("grp")
    near = [(i, i ^ 1) for i in range(parts)]
    far = [(i, i ^ 2) for i in range(parts)]
    outgoing = jnp.stack([block_of(me ^ 1, width), block_of(me ^ 3, width)])
    incoming = lax.ppermute(outgoing, "grp", near)
    other = block_of(me ^ 2, width).astype(jnp.float32) + incoming[1].astype(jnp.float32)
    arrived = lax.ppermute(other.astype(jnp.bfloat16), "grp", far)
    own = block_of(me, width).astype(jnp.float32) + incoming[0].astype(jnp.float32)
    return own + arrived.astype(jnp.float32)


def grp_all_gather(block):
    parts = lax.axis_size("grp")
    if parts != 4:
        return lax.all_gather(block, "grp", axis=1, tiled=True)
    me = lax.axis_index("grp")
    near = [(i, i ^ 1) for i in range(parts)]
    far = [(i, i ^ 2) for i in range(parts)]
    beside = lax.ppermute(block, "grp", near)
    across = lax.ppermute(block, "grp", far)
    diagonal = lax.ppermute(across, "grp", near)
    held = jnp.stack([block, beside, across, diagonal])
    pieces = [lax.dynamic_index_in_dim(held, k ^ me, 0, keepdims=False) for k in range(parts)]
    return jnp.concatenate(pieces, axis=1)


def finish(attn_rows, resid_rows, out_weight, norm_gain, gate_weight, up_weight, down_weight):
    partial_value = jnp.dot(attn_rows, out_weight, preferred_element_type=jnp.float32)
    proj_cols = grp_reduce_scatter(partial_value.astype(jnp.bfloat16))
    state_cols = (resid_rows.astype(jnp.float32) + proj_cols).astype(jnp.bfloat16)
    state_full = grp_all_gather(state_cols)
    state32 = state_full.astype(jnp.float32)
    normed = (
        state32 * lax.rsqrt(jnp.mean(state32 * state32, axis=1, keepdims=True) + 1e-05) * norm_gain
    ).astype(jnp.bfloat16)
    gate = jnp.dot(normed, gate_weight, preferred_element_type=jnp.float32)
    upval = jnp.dot(normed, up_weight, preferred_element_type=jnp.float32)
    inner = (jax.nn.silu(gate) * upval).astype(jnp.bfloat16)
    down_cols = grp_reduce_scatter_blocks(
        lambda index, width: jnp.dot(
            inner, grp_block(down_weight, index, width), preferred_element_type=jnp.float32
        ).astype(jnp.bfloat16),
        down_weight.shape[1],
    )
    return (state_cols.astype(jnp.float32) + down_cols).astype(jnp.bfloat16)


def shards(
    residual,
    queries,
    new_keys,
    new_values,
    pool_keys,
    pool_values,
    cache_len,
    prefix_group,
    prefix_len,
    span_rows,
    span_offset,
    out_weight,
    norm_gain,
    gate_weight,
    up_weight,
    down_weight,
):
    total_rows = residual.shape[0]
    width = residual.shape[1]
    device = lax.axis_index("req")
    devices = lax.axis_size("req")
    bucket = (total_rows - DEC + devices - 1) // devices
    spread = bucket * devices
    bal = total_rows // 2
    counts = DEC + span_rows
    ends = jnp.cumsum(counts)
    firsts = ends - counts
    first = firsts[device]
    own_count = counts[device]
    shift = first % devices

    def outbound(rows):
        grid = rows[:spread].reshape(bucket, devices, rows.shape[1])
        return jnp.transpose(jnp.roll(grid, shift, axis=1), (1, 0, 2))

    send_resid = outbound(residual)
    got_resid = lax.all_to_all(send_resid, "req", split_axis=0, concat_axis=0, tiled=True)
    decode_mask = build_decode_mask(cache_len, prefix_group, prefix_len)
    sent_parts = attention_parts(
        queries, new_keys, new_values, pool_keys, pool_values, decode_mask, span_offset[0], outbound
    )
    got_resid, sent_parts[-1] = lax.optimization_barrier((got_resid, sent_parts[-1]))
    got_parts = [
        lax.all_to_all(part, "req", split_axis=0, concat_axis=0, tiled=True)
        for part in sent_parts
    ]

    slots = jnp.arange(bal, dtype=jnp.int32)
    wanted = slots * devices + device
    src_dev = jnp.sum((ends[None, :] <= wanted[:, None]).astype(jnp.int32), axis=1)
    src_dev = jnp.minimum(src_dev, devices - 1)
    src_pos = jnp.clip((wanted - firsts[src_dev]) // devices, 0, bucket - 1)
    flat_idx = src_dev * bucket + src_pos
    dense_attn = jnp.concatenate(
        [got.reshape(spread, got.shape[2])[flat_idx] for got in got_parts], axis=1
    )
    dense_resid = got_resid.reshape(spread, width)[flat_idx]
    mixed = finish(
        dense_attn, dense_resid, out_weight, norm_gain, gate_weight, up_weight, down_weight
    )
    lane = (device - firsts) % devices
    row_of = jnp.arange(bucket, dtype=jnp.int32)[None, :] * devices + lane[:, None]
    back_valid = row_of < counts[:, None]
    back_start = (firsts + lane) // devices
    padded = jnp.concatenate([mixed, jnp.zeros((bucket, width), mixed.dtype)], axis=0)
    slabs = jnp.stack(
        [lax.dynamic_slice_in_dim(padded, back_start[k], bucket, 0) for k in range(devices)]
    )
    picked = jnp.where(back_valid[:, :, None], slabs, jnp.zeros((), slabs.dtype))
    returned = lax.all_to_all(picked, "req", split_axis=0, concat_axis=0, tiled=True)
    restored = jnp.roll(jnp.transpose(returned, (1, 0, 2)), -shift, axis=1).reshape(spread, width)
    if spread < total_rows:
        restored = jnp.concatenate(
            [restored, jnp.zeros((total_rows - spread, width), restored.dtype)], axis=0
        )
    is_live = jnp.arange(total_rows, dtype=jnp.int32) < own_count
    return jnp.where(is_live[:, None], restored, jnp.zeros((), jnp.bfloat16))


def solution(mesh):
    placed = (
        P("req", "grp"),
        P("req", "grp"),
        P("req", "grp"),
        P("req", "grp"),
        P("req", "grp"),
        P("req", "grp"),
        P("req"),
        P("req"),
        P("req"),
        P(),
        P("req"),
        P("grp", None),
        P(),
        P(None, "grp"),
        P(None, "grp"),
        P("grp", None),
    )
    return jax.shard_map(
        shards, mesh=mesh, in_specs=placed, out_specs=P("req", "grp"), check_vma=False
    )
```

```python
import functools

import jax
import jax.numpy as jnp
from jax import lax
from jax.experimental import pallas as pl
from jax.experimental.pallas import tpu as pltpu
from jax.sharding import PartitionSpec as P

HEADS = 32
KV_HEADS = 8
HEAD_DIM = 64
DEC = 8
REG = 512


MASKED_SCORE = -1e30


SCALE = HEAD_DIM ** (-0.5)
QBLK = 512


def span_kernel(kv_index, start_ref, q_ref, kp_ref, vp_ref, kf_ref, vf_ref, o_ref):
    span_start = start_ref[0]
    half = HEAD_DIM

    def pick(ref, lo, hi):
        return ref[lo:hi, kv_index * half : (kv_index + 1) * half]

    rows = q_ref.shape[0]
    prior = kp_ref.shape[0]
    kp = pick(kp_ref, 0, prior)
    vp = pick(vp_ref, 0, prior)
    for blk in range(rows // QBLK):
        lo = blk * QBLK
        hi = lo + QBLK
        kf = pick(kf_ref, 0, hi)
        vf = pick(vf_ref, 0, hi)
        t_p = lax.broadcasted_iota(jnp.int32, (QBLK, prior), 1)
        prior_seen = t_p < span_start
        q_pos = lax.broadcasted_iota(jnp.int32, (QBLK, hi), 0) + lo
        k_pos = lax.broadcasted_iota(jnp.int32, (QBLK, hi), 1)
        seen = (k_pos >= DEC) & (k_pos <= q_pos)
        for hh in range(2):
            q = q_ref[lo:hi, hh * half : (hh + 1) * half] * jnp.asarray(SCALE, q_ref.dtype)
            s_p = lax.dot_general(
                q, kp, (((1,), (1,)), ((), ())), preferred_element_type=jnp.float32
            )
            s_f = lax.dot_general(
                q, kf, (((1,), (1,)), ((), ())), preferred_element_type=jnp.float32
            )
            s_p = jnp.where(prior_seen, s_p, MASKED_SCORE)
            s_f = jnp.where(seen, s_f, MASKED_SCORE)
            highest = jnp.maximum(
                jnp.max(s_p, axis=1, keepdims=True), jnp.max(s_f, axis=1, keepdims=True)
            )
            e_p = jnp.exp(s_p - highest)
            e_f = jnp.exp(s_f - highest)
            totals = jnp.sum(e_p, axis=1, keepdims=True) + jnp.sum(e_f, axis=1, keepdims=True)
            inverse = 1.0 / totals
            p_p = (e_p * inverse).astype(jnp.bfloat16)
            p_f = (e_f * inverse).astype(jnp.bfloat16)
            out = jnp.dot(p_p, vp, preferred_element_type=jnp.float32) + jnp.dot(
                p_f, vf, preferred_element_type=jnp.float32
            )
            o_ref[lo:hi, hh * half : (hh + 1) * half] = out.astype(o_ref.dtype)


def span_attention(queries, pool_keys, pool_values, new_keys, new_values, span_start, cached, kv_index):
    rows, width = queries.shape
    kv_width = new_keys.shape[1]
    prior = REG
    lanes = 2 * HEAD_DIM
    heads = width // HEAD_DIM
    kv = kv_width // HEAD_DIM
    steps = width // lanes // kv
    base = kv_index * steps
    q_spec = pl.BlockSpec((rows, lanes), lambda c, s: (0, base + c))
    o_spec = pl.BlockSpec((rows, lanes), lambda c, s: (0, c))
    p_spec = pl.BlockSpec((prior, kv_width), lambda c, s: (cached // prior, 0))
    f_spec = pl.BlockSpec((rows, kv_width), lambda c, s: (0, 0))
    flops = 4 * (heads // kv) * rows * (prior + rows // 2) * HEAD_DIM
    cost = pl.CostEstimate(
        flops=16 * flops,
        transcendentals=(heads // kv) * rows * (prior + rows // 2),
        bytes_accessed=2 * (2 * rows * width // kv + 2 * (prior + rows) * kv_width),
    )
    return pl.pallas_call(
        functools.partial(span_kernel, kv_index),
        out_shape=jax.ShapeDtypeStruct((rows, steps * lanes), jnp.bfloat16),
        grid_spec=pltpu.PrefetchScalarGridSpec(
            num_scalar_prefetch=1,
            grid=(steps,),
            in_specs=[q_spec, p_spec, p_spec, f_spec, f_spec],
            out_specs=o_spec,
        ),
        cost_estimate=cost,
    )(span_start.reshape(1).astype(jnp.int32), queries, pool_keys, pool_values, new_keys, new_values)


def decode_attention(queries, new_keys, new_values, pool_keys, pool_values, decode_mask):
    kv = new_keys.shape[1] // HEAD_DIM
    heads = queries.shape[1] // HEAD_DIM
    per_kv = heads // kv
    cached = DEC * REG
    q = queries[:DEC].reshape(DEC, heads, HEAD_DIM)
    owner = jnp.arange(heads, dtype=jnp.int32) // per_kv
    lanes = [
        jnp.where((owner == j)[None, :, None], q, jnp.zeros((), q.dtype)) for j in range(kv)
    ]
    q_ext = jnp.concatenate(lanes, axis=2)
    s_c = jnp.einsum("rhc,tc->rht", q_ext, pool_keys[:cached], preferred_element_type=jnp.float32)
    s_n = jnp.einsum("rhc,tc->rht", q_ext, new_keys[:DEC], preferred_element_type=jnp.float32)
    s_c = jnp.where(decode_mask[:, None, :cached], s_c * SCALE, MASKED_SCORE)
    s_n = jnp.where(decode_mask[:, None, cached:], s_n * SCALE, MASKED_SCORE)
    highest = jnp.maximum(
        jnp.max(s_c, axis=2, keepdims=True), jnp.max(s_n, axis=2, keepdims=True)
    )
    e_c = jnp.exp(s_c - highest)
    e_n = jnp.exp(s_n - highest)
    totals = jnp.sum(e_c, axis=2, keepdims=True) + jnp.sum(e_n, axis=2, keepdims=True)
    p_c = (e_c / totals).astype(jnp.bfloat16)
    p_n = (e_n / totals).astype(jnp.bfloat16)
    full = jnp.einsum(
        "rht,tc->rhc", p_c, pool_values[:cached], preferred_element_type=jnp.float32
    ) + jnp.einsum("rht,tc->rhc", p_n, new_values[:DEC], preferred_element_type=jnp.float32)
    out = full[:, :, 0:HEAD_DIM]
    for j in range(1, kv):
        out = jnp.where(
            (owner == j)[None, :, None], full[:, :, j * HEAD_DIM : (j + 1) * HEAD_DIM], out
        )
    return out.astype(jnp.bfloat16).reshape(DEC, heads * HEAD_DIM)


def build_decode_mask(cache_len, prefix_group, prefix_len):
    position = jnp.arange(DEC * REG, dtype=jnp.int32)
    region = position // REG
    offset = position % REG
    request = jnp.arange(DEC, dtype=jnp.int32)
    shared = (region[None, :] == prefix_group[:, None]) & (offset[None, :] < prefix_len[:, None])
    owned = (
        (region[None, :] == request[:, None])
        & (offset[None, :] >= prefix_len[:, None])
        & (offset[None, :] < cache_len[:, None])
    )
    return jnp.concatenate([shared | owned, jnp.eye(DEC, dtype=jnp.bool_)], axis=1)


def attention_parts(queries, new_keys, new_values, pool_keys, pool_values, decode_mask, span_start, send):
    cached = DEC * REG
    kv = new_keys.shape[1] // HEAD_DIM
    part_width = queries.shape[1] // kv
    decode_rows = decode_attention(
        queries, new_keys, new_values, pool_keys, pool_values, decode_mask
    )
    sent = []
    for j in range(kv):
        span_rows = span_attention(
            queries, pool_keys, pool_values, new_keys, new_values, span_start, cached, j
        )
        mine = decode_rows[:, j * part_width : (j + 1) * part_width]
        outgoing = send(lax.dynamic_update_slice(span_rows, mine, (0, 0)))
        if j + 1 < kv:
            outgoing, queries = lax.optimization_barrier((outgoing, queries))
        sent.append(outgoing)
    return sent


def grp_block(x, index, width):
    return lax.dynamic_slice_in_dim(x, index * width, width, 1)


def grp_reduce_scatter(partial):
    parts = lax.axis_size("grp")
    width = partial.shape[1] // parts
    if parts != 4:
        return lax.psum_scatter(partial, "grp", scatter_dimension=1, tiled=True).astype(
            jnp.float32
        )
    me = lax.axis_index("grp")
    near = [(i, i ^ 1) for i in range(parts)]
    far = [(i, i ^ 2) for i in range(parts)]
    outgoing = jnp.stack([grp_block(partial, me ^ 1, width), grp_block(partial, me ^ 3, width)])
    incoming = lax.ppermute(outgoing, "grp", near)
    own = grp_block(partial, me, width).astype(jnp.float32) + incoming[0].astype(jnp.float32)
    other = grp_block(partial, me ^ 2, width).astype(jnp.float32) + incoming[1].astype(
        jnp.float32
    )
    arrived = lax.ppermute(other.astype(jnp.bfloat16), "grp", far)
    return own + arrived.astype(jnp.float32)


def grp_reduce_scatter_blocks(block_of, total):
    parts = lax.axis_size("grp")
    width = total // parts
    if parts != 4:
        whole = jnp.concatenate([block_of(k, width) for k in range(parts)], axis=1)
        return grp_reduce_scatter(whole)
    me = lax.axis_index("grp")
    near = [(i, i ^ 1) for i in range(parts)]
    far = [(i, i ^ 2) for i in range(parts)]
    outgoing = jnp.stack([block_of(me ^ 1, width), block_of(me ^ 3, width)])
    incoming = lax.ppermute(outgoing, "grp", near)
    other = block_of(me ^ 2, width).astype(jnp.float32) + incoming[1].astype(jnp.float32)
    arrived = lax.ppermute(other.astype(jnp.bfloat16), "grp", far)
    own = block_of(me, width).astype(jnp.float32) + incoming[0].astype(jnp.float32)
    return own + arrived.astype(jnp.float32)


def grp_all_gather(block):
    parts = lax.axis_size("grp")
    if parts != 4:
        return lax.all_gather(block, "grp", axis=1, tiled=True)
    me = lax.axis_index("grp")
    near = [(i, i ^ 1) for i in range(parts)]
    far = [(i, i ^ 2) for i in range(parts)]
    beside = lax.ppermute(block, "grp", near)
    across = lax.ppermute(block, "grp", far)
    diagonal = lax.ppermute(across, "grp", near)
    held = jnp.stack([block, beside, across, diagonal])
    pieces = [lax.dynamic_index_in_dim(held, k ^ me, 0, keepdims=False) for k in range(parts)]
    return jnp.concatenate(pieces, axis=1)


def finish(attn_rows, resid_rows, out_weight, norm_gain, gate_weight, up_weight, down_weight):
    partial_value = jnp.dot(attn_rows, out_weight, preferred_element_type=jnp.float32)
    proj_cols = grp_reduce_scatter(partial_value.astype(jnp.bfloat16))
    state_cols = (resid_rows.astype(jnp.float32) + proj_cols).astype(jnp.bfloat16)
    state_full = grp_all_gather(state_cols)
    state32 = state_full.astype(jnp.float32)
    normed = (
        state32 * lax.rsqrt(jnp.mean(state32 * state32, axis=1, keepdims=True) + 1e-05) * norm_gain
    ).astype(jnp.bfloat16)
    gate = jnp.dot(normed, gate_weight, preferred_element_type=jnp.float32)
    upval = jnp.dot(normed, up_weight, preferred_element_type=jnp.float32)
    inner = (jax.nn.silu(gate) * upval).astype(jnp.bfloat16)
    down_cols = grp_reduce_scatter_blocks(
        lambda index, width: jnp.dot(
            inner, grp_block(down_weight, index, width), preferred_element_type=jnp.float32
        ).astype(jnp.bfloat16),
        down_weight.shape[1],
    )
    return (state_cols.astype(jnp.float32) + down_cols).astype(jnp.bfloat16)


def shards(
    residual,
    queries,
    new_keys,
    new_values,
    pool_keys,
    pool_values,
    cache_len,
    prefix_group,
    prefix_len,
    span_rows,
    span_offset,
    out_weight,
    norm_gain,
    gate_weight,
    up_weight,
    down_weight,
):
    total_rows = residual.shape[0]
    width = residual.shape[1]
    device = lax.axis_index("req")
    devices = lax.axis_size("req")
    bucket = (total_rows - DEC + devices - 1) // devices
    spread = bucket * devices
    bal = total_rows // 2
    counts = DEC + span_rows
    ends = jnp.cumsum(counts)
    firsts = ends - counts
    first = firsts[device]
    own_count = counts[device]
    shift = first % devices

    def outbound(rows):
        grid = rows[:spread].reshape(bucket, devices, rows.shape[1])
        return jnp.transpose(jnp.roll(grid, shift, axis=1), (1, 0, 2))

    send_resid = outbound(residual)
    got_resid = lax.all_to_all(send_resid, "req", split_axis=0, concat_axis=0, tiled=True)
    decode_mask = build_decode_mask(cache_len, prefix_group, prefix_len)
    sent_parts = attention_parts(
        queries, new_keys, new_values, pool_keys, pool_values, decode_mask, span_offset[0], outbound
    )
    got_resid, sent_parts[-1] = lax.optimization_barrier((got_resid, sent_parts[-1]))
    got_parts = [
        lax.all_to_all(part, "req", split_axis=0, concat_axis=0, tiled=True)
        for part in sent_parts
    ]

    slots = jnp.arange(bal, dtype=jnp.int32)
    wanted = slots * devices + device
    src_dev = jnp.sum((ends[None, :] <= wanted[:, None]).astype(jnp.int32), axis=1)
    src_dev = jnp.minimum(src_dev, devices - 1)
    src_pos = jnp.clip((wanted - firsts[src_dev]) // devices, 0, bucket - 1)
    flat_idx = src_dev * bucket + src_pos
    dense_attn = jnp.concatenate(
        [got.reshape(spread, got.shape[2])[flat_idx] for got in got_parts], axis=1
    )
    dense_resid = got_resid.reshape(spread, width)[flat_idx]
    mixed = finish(
        dense_attn, dense_resid, out_weight, norm_gain, gate_weight, up_weight, down_weight
    )
    lane = (device - firsts) % devices
    row_of = jnp.arange(bucket, dtype=jnp.int32)[None, :] * devices + lane[:, None]
    back_valid = row_of < counts[:, None]
    back_start = (firsts + lane) // devices
    padded = jnp.concatenate([mixed, jnp.zeros((bucket, width), mixed.dtype)], axis=0)
    slabs = jnp.stack(
        [lax.dynamic_slice_in_dim(padded, back_start[k], bucket, 0) for k in range(devices)]
    )
    picked = jnp.where(back_valid[:, :, None], slabs, jnp.zeros((), slabs.dtype))
    returned = lax.all_to_all(picked, "req", split_axis=0, concat_axis=0, tiled=True)
    restored = jnp.roll(jnp.transpose(returned, (1, 0, 2)), -shift, axis=1).reshape(spread, width)
    if spread < total_rows:
        restored = jnp.concatenate(
            [restored, jnp.zeros((total_rows - spread, width), restored.dtype)], axis=0
        )
    is_live = jnp.arange(total_rows, dtype=jnp.int32) < own_count
    return jnp.where(is_live[:, None], restored, jnp.zeros((), jnp.bfloat16))


def solution(mesh):
    placed = (
        P("req", "grp"),
        P("req", "grp"),
        P("req", "grp"),
        P("req", "grp"),
        P("req", "grp"),
        P("req", "grp"),
        P("req"),
        P("req"),
        P("req"),
        P(),
        P("req"),
        P("grp", None),
        P(),
        P(None, "grp"),
        P(None, "grp"),
        P("grp", None),
    )
    return jax.shard_map(
        shards, mesh=mesh, in_specs=placed, out_specs=P("req", "grp"), check_vma=False
    )
```

```python
import functools

import jax
import jax.numpy as jnp
from jax import lax
from jax.experimental import pallas as pl
from jax.experimental.pallas import tpu as pltpu
from jax.sharding import PartitionSpec as P

HEADS = 32
KV_HEADS = 8
HEAD_DIM = 64
DEC = 8
REG = 512


MASKED_SCORE = -1e30


SCALE = HEAD_DIM ** (-0.5)
QBLK = 512


def span_kernel(kv_index, start_ref, q_ref, kp_ref, vp_ref, kf_ref, vf_ref, o_ref):
    span_start = start_ref[0]
    half = HEAD_DIM

    def pick(ref, lo, hi):
        return ref[lo:hi, kv_index * half : (kv_index + 1) * half]

    rows = q_ref.shape[0]
    prior = kp_ref.shape[0]
    kp = pick(kp_ref, 0, prior)
    vp = pick(vp_ref, 0, prior)
    for blk in range(rows // QBLK):
        lo = blk * QBLK
        hi = lo + QBLK
        kf = pick(kf_ref, 0, hi)
        vf = pick(vf_ref, 0, hi)
        t_p = lax.broadcasted_iota(jnp.int32, (QBLK, prior), 1)
        prior_seen = t_p < span_start
        q_pos = lax.broadcasted_iota(jnp.int32, (QBLK, hi), 0) + lo
        k_pos = lax.broadcasted_iota(jnp.int32, (QBLK, hi), 1)
        seen = (k_pos >= DEC) & (k_pos <= q_pos)
        for hh in range(2):
            q = q_ref[lo:hi, hh * half : (hh + 1) * half] * jnp.asarray(SCALE, q_ref.dtype)
            s_p = lax.dot_general(
                q, kp, (((1,), (1,)), ((), ())), preferred_element_type=jnp.float32
            )
            s_f = lax.dot_general(
                q, kf, (((1,), (1,)), ((), ())), preferred_element_type=jnp.float32
            )
            s_p = jnp.where(prior_seen, s_p, MASKED_SCORE)
            s_f = jnp.where(seen, s_f, MASKED_SCORE)
            highest = jnp.maximum(
                jnp.max(s_p, axis=1, keepdims=True), jnp.max(s_f, axis=1, keepdims=True)
            )
            e_p = jnp.exp(s_p - highest)
            e_f = jnp.exp(s_f - highest)
            totals = jnp.sum(e_p, axis=1, keepdims=True) + jnp.sum(e_f, axis=1, keepdims=True)
            inverse = 1.0 / totals
            p_p = (e_p * inverse).astype(jnp.bfloat16)
            p_f = (e_f * inverse).astype(jnp.bfloat16)
            out = jnp.dot(p_p, vp, preferred_element_type=jnp.float32) + jnp.dot(
                p_f, vf, preferred_element_type=jnp.float32
            )
            o_ref[lo:hi, hh * half : (hh + 1) * half] = out.astype(o_ref.dtype)


def span_attention(queries, pool_keys, pool_values, new_keys, new_values, span_start, cached, kv_index):
    rows, width = queries.shape
    kv_width = new_keys.shape[1]
    prior = REG
    lanes = 2 * HEAD_DIM
    heads = width // HEAD_DIM
    kv = kv_width // HEAD_DIM
    steps = width // lanes // kv
    base = kv_index * steps
    q_spec = pl.BlockSpec((rows, lanes), lambda c, s: (0, base + c))
    o_spec = pl.BlockSpec((rows, lanes), lambda c, s: (0, c))
    p_spec = pl.BlockSpec((prior, kv_width), lambda c, s: (cached // prior, 0))
    f_spec = pl.BlockSpec((rows, kv_width), lambda c, s: (0, 0))
    flops = 4 * (heads // kv) * rows * (prior + rows // 2) * HEAD_DIM
    cost = pl.CostEstimate(
        flops=16 * flops,
        transcendentals=(heads // kv) * rows * (prior + rows // 2),
        bytes_accessed=2 * (2 * rows * width // kv + 2 * (prior + rows) * kv_width),
    )
    return pl.pallas_call(
        functools.partial(span_kernel, kv_index),
        out_shape=jax.ShapeDtypeStruct((rows, steps * lanes), jnp.bfloat16),
        grid_spec=pltpu.PrefetchScalarGridSpec(
            num_scalar_prefetch=1,
            grid=(steps,),
            in_specs=[q_spec, p_spec, p_spec, f_spec, f_spec],
            out_specs=o_spec,
        ),
        cost_estimate=cost,
    )(span_start.reshape(1).astype(jnp.int32), queries, pool_keys, pool_values, new_keys, new_values)


def decode_attention(queries, new_keys, new_values, pool_keys, pool_values, decode_mask):
    kv = new_keys.shape[1] // HEAD_DIM
    heads = queries.shape[1] // HEAD_DIM
    per_kv = heads // kv
    cached = DEC * REG
    q = queries[:DEC].reshape(DEC, heads, HEAD_DIM)
    owner = jnp.arange(heads, dtype=jnp.int32) // per_kv
    lanes = [
        jnp.where((owner == j)[None, :, None], q, jnp.zeros((), q.dtype)) for j in range(kv)
    ]
    q_ext = jnp.concatenate(lanes, axis=2)
    s_c = jnp.einsum("rhc,tc->rht", q_ext, pool_keys[:cached], preferred_element_type=jnp.float32)
    s_n = jnp.einsum("rhc,tc->rht", q_ext, new_keys[:DEC], preferred_element_type=jnp.float32)
    s_c = jnp.where(decode_mask[:, None, :cached], s_c * SCALE, MASKED_SCORE)
    s_n = jnp.where(decode_mask[:, None, cached:], s_n * SCALE, MASKED_SCORE)
    highest = jnp.maximum(
        jnp.max(s_c, axis=2, keepdims=True), jnp.max(s_n, axis=2, keepdims=True)
    )
    e_c = jnp.exp(s_c - highest)
    e_n = jnp.exp(s_n - highest)
    totals = jnp.sum(e_c, axis=2, keepdims=True) + jnp.sum(e_n, axis=2, keepdims=True)
    p_c = (e_c / totals).astype(jnp.bfloat16)
    p_n = (e_n / totals).astype(jnp.bfloat16)
    full = jnp.einsum(
        "rht,tc->rhc", p_c, pool_values[:cached], preferred_element_type=jnp.float32
    ) + jnp.einsum("rht,tc->rhc", p_n, new_values[:DEC], preferred_element_type=jnp.float32)
    out = full[:, :, 0:HEAD_DIM]
    for j in range(1, kv):
        out = jnp.where(
            (owner == j)[None, :, None], full[:, :, j * HEAD_DIM : (j + 1) * HEAD_DIM], out
        )
    return out.astype(jnp.bfloat16).reshape(DEC, heads * HEAD_DIM)


def build_decode_mask(cache_len, prefix_group, prefix_len):
    position = jnp.arange(DEC * REG, dtype=jnp.int32)
    region = position // REG
    offset = position % REG
    request = jnp.arange(DEC, dtype=jnp.int32)
    shared = (region[None, :] == prefix_group[:, None]) & (offset[None, :] < prefix_len[:, None])
    owned = (
        (region[None, :] == request[:, None])
        & (offset[None, :] >= prefix_len[:, None])
        & (offset[None, :] < cache_len[:, None])
    )
    return jnp.concatenate([shared | owned, jnp.eye(DEC, dtype=jnp.bool_)], axis=1)


def attention_parts(queries, new_keys, new_values, pool_keys, pool_values, decode_mask, span_start, send):
    cached = DEC * REG
    kv = new_keys.shape[1] // HEAD_DIM
    part_width = queries.shape[1] // kv
    decode_rows = decode_attention(
        queries, new_keys, new_values, pool_keys, pool_values, decode_mask
    )
    sent = []
    for j in range(kv):
        span_rows = span_attention(
            queries, pool_keys, pool_values, new_keys, new_values, span_start, cached, j
        )
        mine = decode_rows[:, j * part_width : (j + 1) * part_width]
        outgoing = send(lax.dynamic_update_slice(span_rows, mine, (0, 0)))
        if j + 1 < kv:
            outgoing, queries = lax.optimization_barrier((outgoing, queries))
        sent.append(outgoing)
    return sent


def grp_block(x, index, width):
    return lax.dynamic_slice_in_dim(x, index * width, width, 1)


def grp_reduce_scatter(partial):
    parts = lax.axis_size("grp")
    width = partial.shape[1] // parts
    if parts != 4:
        return lax.psum_scatter(partial, "grp", scatter_dimension=1, tiled=True).astype(
            jnp.float32
        )
    me = lax.axis_index("grp")
    near = [(i, i ^ 1) for i in range(parts)]
    far = [(i, i ^ 2) for i in range(parts)]
    outgoing = jnp.stack([grp_block(partial, me ^ 1, width), grp_block(partial, me ^ 3, width)])
    incoming = lax.ppermute(outgoing, "grp", near)
    own = grp_block(partial, me, width).astype(jnp.float32) + incoming[0].astype(jnp.float32)
    other = grp_block(partial, me ^ 2, width).astype(jnp.float32) + incoming[1].astype(
        jnp.float32
    )
    arrived = lax.ppermute(other.astype(jnp.bfloat16), "grp", far)
    return own + arrived.astype(jnp.float32)


def grp_reduce_scatter_blocks(block_of, total):
    parts = lax.axis_size("grp")
    width = total // parts
    if parts != 4:
        whole = jnp.concatenate([block_of(k, width) for k in range(parts)], axis=1)
        return grp_reduce_scatter(whole)
    me = lax.axis_index("grp")
    near = [(i, i ^ 1) for i in range(parts)]
    far = [(i, i ^ 2) for i in range(parts)]
    outgoing = jnp.stack([block_of(me ^ 1, width), block_of(me ^ 3, width)])
    incoming = lax.ppermute(outgoing, "grp", near)
    other = block_of(me ^ 2, width).astype(jnp.float32) + incoming[1].astype(jnp.float32)
    arrived = lax.ppermute(other.astype(jnp.bfloat16), "grp", far)
    own = block_of(me, width).astype(jnp.float32) + incoming[0].astype(jnp.float32)
    return own + arrived.astype(jnp.float32)


def grp_all_gather(block):
    parts = lax.axis_size("grp")
    if parts != 4:
        return lax.all_gather(block, "grp", axis=1, tiled=True)
    me = lax.axis_index("grp")
    near = [(i, i ^ 1) for i in range(parts)]
    far = [(i, i ^ 2) for i in range(parts)]
    beside = lax.ppermute(block, "grp", near)
    across = lax.ppermute(block, "grp", far)
    diagonal = lax.ppermute(across, "grp", near)
    held = jnp.stack([block, beside, across, diagonal])
    pieces = [lax.dynamic_index_in_dim(held, k ^ me, 0, keepdims=False) for k in range(parts)]
    return jnp.concatenate(pieces, axis=1)


def finish(attn_rows, resid_rows, out_weight, norm_gain, gate_weight, up_weight, down_weight):
    partial_value = jnp.dot(attn_rows, out_weight, preferred_element_type=jnp.float32)
    proj_cols = grp_reduce_scatter(partial_value.astype(jnp.bfloat16))
    state_cols = (resid_rows.astype(jnp.float32) + proj_cols).astype(jnp.bfloat16)
    state_full = grp_all_gather(state_cols)
    state32 = state_full.astype(jnp.float32)
    normed = (
        state32 * lax.rsqrt(jnp.mean(state32 * state32, axis=1, keepdims=True) + 1e-05) * norm_gain
    ).astype(jnp.bfloat16)
    gate = jnp.dot(normed, gate_weight, preferred_element_type=jnp.float32)
    upval = jnp.dot(normed, up_weight, preferred_element_type=jnp.float32)
    inner = (jax.nn.silu(gate) * upval).astype(jnp.bfloat16)
    down_cols = grp_reduce_scatter_blocks(
        lambda index, width: jnp.dot(
            inner, grp_block(down_weight, index, width), preferred_element_type=jnp.float32
        ).astype(jnp.bfloat16),
        down_weight.shape[1],
    )
    return (state_cols.astype(jnp.float32) + down_cols).astype(jnp.bfloat16)


def shards(
    residual,
    queries,
    new_keys,
    new_values,
    pool_keys,
    pool_values,
    cache_len,
    prefix_group,
    prefix_len,
    span_rows,
    span_offset,
    out_weight,
    norm_gain,
    gate_weight,
    up_weight,
    down_weight,
):
    total_rows = residual.shape[0]
    width = residual.shape[1]
    device = lax.axis_index("req")
    devices = lax.axis_size("req")
    bucket = total_rows // devices
    spread = bucket * devices
    bal = total_rows // 2
    counts = DEC + span_rows
    ends = jnp.cumsum(counts)
    firsts = ends - counts
    first = firsts[device]
    own_count = counts[device]
    shift = first % devices

    def outbound(rows):
        grid = rows[:spread].reshape(bucket, devices, rows.shape[1])
        return jnp.transpose(jnp.roll(grid, shift, axis=1), (1, 0, 2))

    send_resid = outbound(residual)
    got_resid = lax.all_to_all(send_resid, "req", split_axis=0, concat_axis=0, tiled=True)
    decode_mask = build_decode_mask(cache_len, prefix_group, prefix_len)
    sent_parts = attention_parts(
        queries, new_keys, new_values, pool_keys, pool_values, decode_mask, span_offset[0], outbound
    )
    got_resid, sent_parts[-1] = lax.optimization_barrier((got_resid, sent_parts[-1]))
    got_parts = [
        lax.all_to_all(part, "req", split_axis=0, concat_axis=0, tiled=True)
        for part in sent_parts
    ]

    slots = jnp.arange(bal, dtype=jnp.int32)
    wanted = slots * devices + device
    src_dev = jnp.sum((ends[None, :] <= wanted[:, None]).astype(jnp.int32), axis=1)
    src_dev = jnp.minimum(src_dev, devices - 1)
    src_pos = jnp.clip((wanted - firsts[src_dev]) // devices, 0, bucket - 1)
    flat_idx = src_dev * bucket + src_pos
    dense_attn = jnp.concatenate(
        [got.reshape(spread, got.shape[2])[flat_idx] for got in got_parts], axis=1
    )
    dense_resid = got_resid.reshape(spread, width)[flat_idx]
    mixed = finish(
        dense_attn, dense_resid, out_weight, norm_gain, gate_weight, up_weight, down_weight
    )
    lane = (device - firsts) % devices
    row_of = jnp.arange(bucket, dtype=jnp.int32)[None, :] * devices + lane[:, None]
    back_valid = row_of < counts[:, None]
    back_start = (firsts + lane) // devices
    padded = jnp.concatenate([mixed, jnp.zeros((bucket, width), mixed.dtype)], axis=0)
    slabs = jnp.stack(
        [lax.dynamic_slice_in_dim(padded, back_start[k], bucket, 0) for k in range(devices)]
    )
    picked = jnp.where(back_valid[:, :, None], slabs, jnp.zeros((), slabs.dtype))
    returned = lax.all_to_all(picked, "req", split_axis=0, concat_axis=0, tiled=True)
    restored = jnp.roll(jnp.transpose(returned, (1, 0, 2)), -shift, axis=1).reshape(spread, width)
    if spread < total_rows:
        restored = jnp.concatenate(
            [restored, jnp.zeros((total_rows - spread, width), restored.dtype)], axis=0
        )
    is_live = jnp.arange(total_rows, dtype=jnp.int32) < own_count
    return jnp.where(is_live[:, None], restored, jnp.zeros((), jnp.bfloat16))


def solution(mesh):
    placed = (
        P("req", "grp"),
        P("req", "grp"),
        P("req", "grp"),
        P("req", "grp"),
        P("req", "grp"),
        P("req", "grp"),
        P("req"),
        P("req"),
        P("req"),
        P(),
        P("req"),
        P("grp", None),
        P(),
        P(None, "grp"),
        P(None, "grp"),
        P("grp", None),
    )
    return jax.shard_map(
        shards, mesh=mesh, in_specs=placed, out_specs=P("req", "grp"), check_vma=False
    )
```

```python
import functools

import jax
import jax.numpy as jnp
from jax import lax
from jax.experimental import pallas as pl
from jax.experimental.pallas import tpu as pltpu
from jax.sharding import PartitionSpec as P

HEADS = 32
KV_HEADS = 8
HEAD_DIM = 64
DEC = 8
REG = 512


MASKED_SCORE = -1e30


SCALE = HEAD_DIM ** (-0.5)
QBLK = 512


def span_kernel(kv_index, start_ref, q_ref, kp_ref, vp_ref, kf_ref, vf_ref, o_ref):
    span_start = start_ref[0]
    half = HEAD_DIM

    def pick(ref, lo, hi):
        return ref[lo:hi, kv_index * half : (kv_index + 1) * half]

    rows = q_ref.shape[0]
    prior = kp_ref.shape[0]
    kp = pick(kp_ref, 0, prior)
    vp = pick(vp_ref, 0, prior)
    for blk in range(rows // QBLK):
        lo = blk * QBLK
        hi = lo + QBLK
        kf = pick(kf_ref, 0, hi)
        vf = pick(vf_ref, 0, hi)
        t_p = lax.broadcasted_iota(jnp.int32, (QBLK, prior), 1)
        prior_seen = t_p < span_start
        q_pos = lax.broadcasted_iota(jnp.int32, (QBLK, hi), 0) + lo
        k_pos = lax.broadcasted_iota(jnp.int32, (QBLK, hi), 1)
        seen = (k_pos >= DEC) & (k_pos <= q_pos)
        for hh in range(2):
            q = q_ref[lo:hi, hh * half : (hh + 1) * half] * jnp.asarray(SCALE, q_ref.dtype)
            s_p = lax.dot_general(
                q, kp, (((1,), (1,)), ((), ())), preferred_element_type=jnp.float32
            )
            s_f = lax.dot_general(
                q, kf, (((1,), (1,)), ((), ())), preferred_element_type=jnp.float32
            )
            s_p = jnp.where(prior_seen, s_p, MASKED_SCORE)
            s_f = jnp.where(seen, s_f, MASKED_SCORE)
            highest = jnp.maximum(
                jnp.max(s_p, axis=1, keepdims=True), jnp.max(s_f, axis=1, keepdims=True)
            )
            e_p = jnp.exp(s_p - highest)
            e_f = jnp.exp(s_f - highest)
            totals = jnp.sum(e_p, axis=1, keepdims=True) + jnp.sum(e_f, axis=1, keepdims=True)
            inverse = 1.0 / totals
            p_p = (e_p * inverse).astype(jnp.bfloat16)
            p_f = (e_f * inverse).astype(jnp.bfloat16)
            out = jnp.dot(p_p, vp, preferred_element_type=jnp.float32) + jnp.dot(
                p_f, vf, preferred_element_type=jnp.float32
            )
            o_ref[lo:hi, hh * half : (hh + 1) * half] = out.astype(o_ref.dtype)


def span_attention(queries, pool_keys, pool_values, new_keys, new_values, span_start, cached, kv_index):
    rows, width = queries.shape
    kv_width = new_keys.shape[1]
    prior = REG
    lanes = 2 * HEAD_DIM
    heads = width // HEAD_DIM
    kv = kv_width // HEAD_DIM
    steps = width // lanes // kv
    base = kv_index * steps
    q_spec = pl.BlockSpec((rows, lanes), lambda c, s: (0, base + c))
    o_spec = pl.BlockSpec((rows, lanes), lambda c, s: (0, c))
    p_spec = pl.BlockSpec((prior, kv_width), lambda c, s: (cached // prior, 0))
    f_spec = pl.BlockSpec((rows, kv_width), lambda c, s: (0, 0))
    flops = 4 * (heads // kv) * rows * (prior + rows // 2) * HEAD_DIM
    cost = pl.CostEstimate(
        flops=16 * flops,
        transcendentals=(heads // kv) * rows * (prior + rows // 2),
        bytes_accessed=2 * (2 * rows * width // kv + 2 * (prior + rows) * kv_width),
    )
    return pl.pallas_call(
        functools.partial(span_kernel, kv_index),
        out_shape=jax.ShapeDtypeStruct((rows, steps * lanes), jnp.bfloat16),
        grid_spec=pltpu.PrefetchScalarGridSpec(
            num_scalar_prefetch=1,
            grid=(steps,),
            in_specs=[q_spec, p_spec, p_spec, f_spec, f_spec],
            out_specs=o_spec,
        ),
        cost_estimate=cost,
    )(span_start.reshape(1).astype(jnp.int32), queries, pool_keys, pool_values, new_keys, new_values)


def decode_attention(queries, new_keys, new_values, pool_keys, pool_values, decode_mask):
    kv = new_keys.shape[1] // HEAD_DIM
    heads = queries.shape[1] // HEAD_DIM
    per_kv = heads // kv
    cached = DEC * REG
    q = queries[:DEC].reshape(DEC, heads, HEAD_DIM)
    owner = jnp.arange(heads, dtype=jnp.int32) // per_kv
    lanes = [
        jnp.where((owner == j)[None, :, None], q, jnp.zeros((), q.dtype)) for j in range(kv)
    ]
    q_ext = jnp.concatenate(lanes, axis=2)
    s_c = jnp.einsum("rhc,tc->rht", q_ext, pool_keys[:cached], preferred_element_type=jnp.float32)
    s_n = jnp.einsum("rhc,tc->rht", q_ext, new_keys[:DEC], preferred_element_type=jnp.float32)
    s_c = jnp.where(decode_mask[:, None, :cached], s_c * SCALE, MASKED_SCORE)
    s_n = jnp.where(decode_mask[:, None, cached:], s_n * SCALE, MASKED_SCORE)
    highest = jnp.maximum(
        jnp.max(s_c, axis=2, keepdims=True), jnp.max(s_n, axis=2, keepdims=True)
    )
    e_c = jnp.exp(s_c - highest)
    e_n = jnp.exp(s_n - highest)
    totals = jnp.sum(e_c, axis=2, keepdims=True) + jnp.sum(e_n, axis=2, keepdims=True)
    p_c = (e_c / totals).astype(jnp.bfloat16)
    p_n = (e_n / totals).astype(jnp.bfloat16)
    full = jnp.einsum(
        "rht,tc->rhc", p_c, pool_values[:cached], preferred_element_type=jnp.float32
    ) + jnp.einsum("rht,tc->rhc", p_n, new_values[:DEC], preferred_element_type=jnp.float32)
    out = full[:, :, 0:HEAD_DIM]
    for j in range(1, kv):
        out = jnp.where(
            (owner == j)[None, :, None], full[:, :, j * HEAD_DIM : (j + 1) * HEAD_DIM], out
        )
    return out.astype(jnp.bfloat16).reshape(DEC, heads * HEAD_DIM)


def build_decode_mask(cache_len, prefix_group, prefix_len):
    position = jnp.arange(DEC * REG, dtype=jnp.int32)
    region = position // REG
    offset = position % REG
    request = jnp.arange(DEC, dtype=jnp.int32)
    shared = (region[None, :] == prefix_group[:, None]) & (offset[None, :] < prefix_len[:, None])
    owned = (
        (region[None, :] == request[:, None])
        & (offset[None, :] >= prefix_len[:, None])
        & (offset[None, :] < cache_len[:, None])
    )
    return jnp.concatenate([shared | owned, jnp.eye(DEC, dtype=jnp.bool_)], axis=1)


def attention_parts(queries, new_keys, new_values, pool_keys, pool_values, decode_mask, span_start, send):
    cached = DEC * REG
    kv = new_keys.shape[1] // HEAD_DIM
    part_width = queries.shape[1] // kv
    decode_rows = decode_attention(
        queries, new_keys, new_values, pool_keys, pool_values, decode_mask
    )
    sent = []
    for j in range(kv):
        span_rows = span_attention(
            queries, pool_keys, pool_values, new_keys, new_values, span_start, cached, j
        )
        mine = decode_rows[:, j * part_width : (j + 1) * part_width]
        outgoing = send(lax.dynamic_update_slice(span_rows, mine, (0, 0)))
        if j + 1 < kv:
            outgoing, queries = lax.optimization_barrier((outgoing, queries))
        sent.append(outgoing)
    return sent


def grp_block(x, index, width):
    return lax.dynamic_slice_in_dim(x, index * width, width, 1)


def grp_reduce_scatter(partial):
    parts = lax.axis_size("grp")
    width = partial.shape[1] // parts
    if parts != 4:
        return lax.psum_scatter(partial, "grp", scatter_dimension=1, tiled=True).astype(
            jnp.float32
        )
    me = lax.axis_index("grp")
    near = [(i, i ^ 1) for i in range(parts)]
    far = [(i, i ^ 2) for i in range(parts)]
    outgoing = jnp.stack([grp_block(partial, me ^ 1, width), grp_block(partial, me ^ 3, width)])
    incoming = lax.ppermute(outgoing, "grp", near)
    own = grp_block(partial, me, width).astype(jnp.float32) + incoming[0].astype(jnp.float32)
    other = grp_block(partial, me ^ 2, width).astype(jnp.float32) + incoming[1].astype(
        jnp.float32
    )
    arrived = lax.ppermute(other.astype(jnp.bfloat16), "grp", far)
    return own + arrived.astype(jnp.float32)


def grp_reduce_scatter_blocks(block_of, total):
    parts = lax.axis_size("grp")
    width = total // parts
    if parts != 4:
        whole = jnp.concatenate([block_of(k, width) for k in range(parts)], axis=1)
        return grp_reduce_scatter(whole)
    me = lax.axis_index("grp")
    near = [(i, i ^ 1) for i in range(parts)]
    far = [(i, i ^ 2) for i in range(parts)]
    outgoing = jnp.stack([block_of(me ^ 1, width), block_of(me ^ 3, width)])
    incoming = lax.ppermute(outgoing, "grp", near)
    other = block_of(me ^ 2, width).astype(jnp.float32) + incoming[1].astype(jnp.float32)
    arrived = lax.ppermute(other.astype(jnp.bfloat16), "grp", far)
    own = block_of(me, width).astype(jnp.float32) + incoming[0].astype(jnp.float32)
    return own + arrived.astype(jnp.float32)


def grp_all_gather(block):
    parts = lax.axis_size("grp")
    if parts != 4:
        return lax.all_gather(block, "grp", axis=1, tiled=True)
    me = lax.axis_index("grp")
    near = [(i, i ^ 1) for i in range(parts)]
    far = [(i, i ^ 2) for i in range(parts)]
    beside = lax.ppermute(block, "grp", near)
    across = lax.ppermute(block, "grp", far)
    diagonal = lax.ppermute(across, "grp", near)
    held = jnp.stack([block, beside, across, diagonal])
    pieces = [lax.dynamic_index_in_dim(held, k ^ me, 0, keepdims=False) for k in range(parts)]
    return jnp.concatenate(pieces, axis=1)


def finish(attn_rows, resid_rows, out_weight, norm_gain, gate_weight, up_weight, down_weight):
    partial_value = jnp.dot(attn_rows, out_weight, preferred_element_type=jnp.float32)
    proj_cols = grp_reduce_scatter(partial_value.astype(jnp.bfloat16))
    state_cols = (resid_rows.astype(jnp.float32) + proj_cols).astype(jnp.bfloat16)
    state_full = grp_all_gather(state_cols)
    state32 = state_full.astype(jnp.float32)
    normed = (
        state32 * lax.rsqrt(jnp.mean(state32 * state32, axis=1, keepdims=True) + 1e-05) * norm_gain
    ).astype(jnp.bfloat16)
    gate = jnp.dot(normed, gate_weight, preferred_element_type=jnp.float32)
    upval = jnp.dot(normed, up_weight, preferred_element_type=jnp.float32)
    inner = (jax.nn.silu(gate) * upval).astype(jnp.bfloat16)
    down_cols = grp_reduce_scatter_blocks(
        lambda index, width: jnp.dot(
            inner, grp_block(down_weight, index, width), preferred_element_type=jnp.float32
        ).astype(jnp.bfloat16),
        down_weight.shape[1],
    )
    return (state_cols.astype(jnp.float32) + down_cols).astype(jnp.bfloat16)


def shards(
    residual,
    queries,
    new_keys,
    new_values,
    pool_keys,
    pool_values,
    cache_len,
    prefix_group,
    prefix_len,
    span_rows,
    span_offset,
    out_weight,
    norm_gain,
    gate_weight,
    up_weight,
    down_weight,
):
    total_rows = residual.shape[0]
    width = residual.shape[1]
    device = lax.axis_index("req")
    devices = lax.axis_size("req")
    bucket = (total_rows - DEC + devices - 1) // devices
    spread = bucket * devices
    bal = total_rows // 2
    counts = DEC + span_rows
    ends = jnp.cumsum(counts)
    firsts = ends - counts
    first = firsts[device]
    own_count = counts[device]
    shift = first % devices

    def outbound(rows):
        grid = rows[:spread].reshape(bucket, devices, rows.shape[1])
        return jnp.transpose(jnp.roll(grid, shift, axis=1), (1, 0, 2))

    send_resid = outbound(residual)
    got_resid = lax.all_to_all(send_resid, "req", split_axis=0, concat_axis=0, tiled=True)
    decode_mask = build_decode_mask(cache_len, prefix_group, prefix_len)
    sent_parts = attention_parts(
        queries, new_keys, new_values, pool_keys, pool_values, decode_mask, span_offset[0], outbound
    )
    got_resid, sent_parts[-1] = lax.optimization_barrier((got_resid, sent_parts[-1]))
    got_parts = [
        lax.all_to_all(part, "req", split_axis=0, concat_axis=0, tiled=True)
        for part in sent_parts
    ]

    slots = jnp.arange(bal, dtype=jnp.int32)
    wanted = slots * devices + device
    src_dev = jnp.sum((ends[None, :] <= wanted[:, None]).astype(jnp.int32), axis=1)
    src_dev = jnp.minimum(src_dev, devices - 1)
    src_pos = jnp.clip((wanted - firsts[src_dev]) // devices, 0, bucket - 1)
    flat_idx = src_dev * bucket + src_pos
    dense_attn = jnp.concatenate(
        [got.reshape(spread, got.shape[2])[flat_idx] for got in got_parts], axis=1
    )
    dense_resid = got_resid.reshape(spread, width)[flat_idx]
    mixed = finish(
        dense_attn, dense_resid, out_weight, norm_gain, gate_weight, up_weight, down_weight
    )
    lane = (device - firsts) % devices
    row_of = jnp.arange(bucket, dtype=jnp.int32)[None, :] * devices + lane[:, None]
    back_valid = row_of < counts[:, None]
    back_start = (firsts + lane) // devices
    padded = jnp.concatenate([mixed, jnp.zeros((bucket, width), mixed.dtype)], axis=0)
    slabs = jnp.stack(
        [lax.dynamic_slice_in_dim(padded, back_start[k], bucket, 0) for k in range(devices)]
    )
    picked = jnp.where(back_valid[:, :, None], slabs, jnp.zeros((), slabs.dtype))
    returned = lax.all_to_all(picked, "req", split_axis=0, concat_axis=0, tiled=True)
    restored = jnp.roll(jnp.transpose(returned, (1, 0, 2)), -shift, axis=1).reshape(spread, width)
    if spread < total_rows:
        restored = jnp.concatenate(
            [restored, jnp.zeros((total_rows - spread, width), restored.dtype)], axis=0
        )
    return restored


def solution(mesh):
    placed = (
        P("req", "grp"),
        P("req", "grp"),
        P("req", "grp"),
        P("req", "grp"),
        P("req", "grp"),
        P("req", "grp"),
        P("req"),
        P("req"),
        P("req"),
        P(),
        P("req"),
        P("grp", None),
        P(),
        P(None, "grp"),
        P(None, "grp"),
        P("grp", None),
    )
    return jax.shard_map(
        shards, mesh=mesh, in_specs=placed, out_specs=P("req", "grp"), check_vma=False
    )
```

```python
import functools

import jax
import jax.numpy as jnp
from jax import lax
from jax.experimental import pallas as pl
from jax.experimental.pallas import tpu as pltpu
from jax.sharding import PartitionSpec as P

HEADS = 32
KV_HEADS = 8
HEAD_DIM = 64
DEC = 8
REG = 512


MASKED_SCORE = -1e30


SCALE = HEAD_DIM ** (-0.5)
QBLK = 512


def span_kernel(kv_index, start_ref, q_ref, kp_ref, vp_ref, kf_ref, vf_ref, o_ref):
    span_start = start_ref[0]
    half = HEAD_DIM

    def pick(ref, lo, hi):
        return ref[lo:hi, kv_index * half : (kv_index + 1) * half]

    rows = q_ref.shape[0]
    prior = kp_ref.shape[0]
    kp = pick(kp_ref, 0, prior)
    vp = pick(vp_ref, 0, prior)
    for blk in range(rows // QBLK):
        lo = blk * QBLK
        hi = lo + QBLK
        kf = pick(kf_ref, 0, hi)
        vf = pick(vf_ref, 0, hi)
        t_p = lax.broadcasted_iota(jnp.int32, (QBLK, prior), 1)
        prior_seen = t_p < span_start
        q_pos = lax.broadcasted_iota(jnp.int32, (QBLK, hi), 0) + lo
        k_pos = lax.broadcasted_iota(jnp.int32, (QBLK, hi), 1)
        seen = (k_pos >= DEC) & (k_pos <= q_pos)
        for hh in range(2):
            q = q_ref[lo:hi, hh * half : (hh + 1) * half] * jnp.asarray(SCALE, q_ref.dtype)
            s_p = lax.dot_general(
                q, kp, (((1,), (1,)), ((), ())), preferred_element_type=jnp.float32
            )
            s_f = lax.dot_general(
                q, kf, (((1,), (1,)), ((), ())), preferred_element_type=jnp.float32
            )
            s_p = jnp.where(prior_seen, s_p, MASKED_SCORE)
            s_f = jnp.where(seen, s_f, MASKED_SCORE)
            highest = jnp.maximum(
                jnp.max(s_p, axis=1, keepdims=True), jnp.max(s_f, axis=1, keepdims=True)
            )
            e_p = jnp.exp(s_p - highest)
            e_f = jnp.exp(s_f - highest)
            totals = jnp.sum(e_p, axis=1, keepdims=True) + jnp.sum(e_f, axis=1, keepdims=True)
            inverse = 1.0 / totals
            p_p = (e_p * inverse).astype(jnp.bfloat16)
            p_f = (e_f * inverse).astype(jnp.bfloat16)
            out = jnp.dot(p_p, vp, preferred_element_type=jnp.float32) + jnp.dot(
                p_f, vf, preferred_element_type=jnp.float32
            )
            o_ref[lo:hi, hh * half : (hh + 1) * half] = out.astype(o_ref.dtype)


def span_attention(queries, pool_keys, pool_values, new_keys, new_values, span_start, cached, kv_index):
    rows, width = queries.shape
    kv_width = new_keys.shape[1]
    prior = REG
    lanes = 2 * HEAD_DIM
    heads = width // HEAD_DIM
    kv = kv_width // HEAD_DIM
    steps = width // lanes // kv
    base = kv_index * steps
    q_spec = pl.BlockSpec((rows, lanes), lambda c, s: (0, base + c))
    o_spec = pl.BlockSpec((rows, lanes), lambda c, s: (0, c))
    p_spec = pl.BlockSpec((prior, kv_width), lambda c, s: (cached // prior, 0))
    f_spec = pl.BlockSpec((rows, kv_width), lambda c, s: (0, 0))
    flops = 4 * (heads // kv) * rows * (prior + rows // 2) * HEAD_DIM
    cost = pl.CostEstimate(
        flops=16 * flops,
        transcendentals=(heads // kv) * rows * (prior + rows // 2),
        bytes_accessed=2 * (2 * rows * width // kv + 2 * (prior + rows) * kv_width),
    )
    return pl.pallas_call(
        functools.partial(span_kernel, kv_index),
        out_shape=jax.ShapeDtypeStruct((rows, steps * lanes), jnp.bfloat16),
        grid_spec=pltpu.PrefetchScalarGridSpec(
            num_scalar_prefetch=1,
            grid=(steps,),
            in_specs=[q_spec, p_spec, p_spec, f_spec, f_spec],
            out_specs=o_spec,
        ),
        cost_estimate=cost,
    )(span_start.reshape(1).astype(jnp.int32), queries, pool_keys, pool_values, new_keys, new_values)


def decode_attention(queries, new_keys, new_values, pool_keys, pool_values, decode_mask):
    kv = new_keys.shape[1] // HEAD_DIM
    heads = queries.shape[1] // HEAD_DIM
    per_kv = heads // kv
    cached = DEC * REG
    q = queries[:DEC].reshape(DEC, heads, HEAD_DIM)
    owner = jnp.arange(heads, dtype=jnp.int32) // per_kv
    lanes = [
        jnp.where((owner == j)[None, :, None], q, jnp.zeros((), q.dtype)) for j in range(kv)
    ]
    q_ext = jnp.concatenate(lanes, axis=2) * jnp.asarray(SCALE, q.dtype)
    s_c = jnp.einsum("rhc,tc->rht", q_ext, pool_keys[:cached], preferred_element_type=jnp.float32)
    s_n = jnp.einsum("rhc,tc->rht", q_ext, new_keys[:DEC], preferred_element_type=jnp.float32)
    s_c = jnp.where(decode_mask[:, None, :cached], s_c, MASKED_SCORE)
    s_n = jnp.where(decode_mask[:, None, cached:], s_n, MASKED_SCORE)
    highest = jnp.maximum(
        jnp.max(s_c, axis=2, keepdims=True), jnp.max(s_n, axis=2, keepdims=True)
    )
    e_c = jnp.exp(s_c - highest)
    e_n = jnp.exp(s_n - highest)
    totals = jnp.sum(e_c, axis=2, keepdims=True) + jnp.sum(e_n, axis=2, keepdims=True)
    inverse = 1.0 / totals
    p_c = (e_c * inverse).astype(jnp.bfloat16)
    p_n = (e_n * inverse).astype(jnp.bfloat16)
    full = jnp.einsum(
        "rht,tc->rhc", p_c, pool_values[:cached], preferred_element_type=jnp.float32
    ) + jnp.einsum("rht,tc->rhc", p_n, new_values[:DEC], preferred_element_type=jnp.float32)
    out = full[:, :, 0:HEAD_DIM]
    for j in range(1, kv):
        out = jnp.where(
            (owner == j)[None, :, None], full[:, :, j * HEAD_DIM : (j + 1) * HEAD_DIM], out
        )
    return out.astype(jnp.bfloat16).reshape(DEC, heads * HEAD_DIM)


def build_decode_mask(cache_len, prefix_group, prefix_len):
    position = jnp.arange(DEC * REG, dtype=jnp.int32)
    region = position // REG
    offset = position % REG
    request = jnp.arange(DEC, dtype=jnp.int32)
    shared = (region[None, :] == prefix_group[:, None]) & (offset[None, :] < prefix_len[:, None])
    owned = (
        (region[None, :] == request[:, None])
        & (offset[None, :] >= prefix_len[:, None])
        & (offset[None, :] < cache_len[:, None])
    )
    return jnp.concatenate([shared | owned, jnp.eye(DEC, dtype=jnp.bool_)], axis=1)


def attention_parts(queries, new_keys, new_values, pool_keys, pool_values, decode_mask, span_start, send):
    cached = DEC * REG
    kv = new_keys.shape[1] // HEAD_DIM
    part_width = queries.shape[1] // kv
    decode_rows = decode_attention(
        queries, new_keys, new_values, pool_keys, pool_values, decode_mask
    )
    sent = []
    for j in range(kv):
        span_rows = span_attention(
            queries, pool_keys, pool_values, new_keys, new_values, span_start, cached, j
        )
        mine = decode_rows[:, j * part_width : (j + 1) * part_width]
        outgoing = send(lax.dynamic_update_slice(span_rows, mine, (0, 0)))
        if j + 1 < kv:
            outgoing, queries = lax.optimization_barrier((outgoing, queries))
        sent.append(outgoing)
    return sent


def grp_block(x, index, width):
    return lax.dynamic_slice_in_dim(x, index * width, width, 1)


def grp_reduce_scatter(partial):
    parts = lax.axis_size("grp")
    width = partial.shape[1] // parts
    if parts != 4:
        return lax.psum_scatter(partial, "grp", scatter_dimension=1, tiled=True).astype(
            jnp.float32
        )
    me = lax.axis_index("grp")
    near = [(i, i ^ 1) for i in range(parts)]
    far = [(i, i ^ 2) for i in range(parts)]
    outgoing = jnp.stack([grp_block(partial, me ^ 1, width), grp_block(partial, me ^ 3, width)])
    incoming = lax.ppermute(outgoing, "grp", near)
    own = grp_block(partial, me, width).astype(jnp.float32) + incoming[0].astype(jnp.float32)
    other = grp_block(partial, me ^ 2, width).astype(jnp.float32) + incoming[1].astype(
        jnp.float32
    )
    arrived = lax.ppermute(other.astype(jnp.bfloat16), "grp", far)
    return own + arrived.astype(jnp.float32)


def grp_reduce_scatter_blocks(block_of, total):
    parts = lax.axis_size("grp")
    width = total // parts
    if parts != 4:
        whole = jnp.concatenate([block_of(k, width) for k in range(parts)], axis=1)
        return grp_reduce_scatter(whole)
    me = lax.axis_index("grp")
    near = [(i, i ^ 1) for i in range(parts)]
    far = [(i, i ^ 2) for i in range(parts)]
    outgoing = jnp.stack([block_of(me ^ 1, width), block_of(me ^ 3, width)])
    incoming = lax.ppermute(outgoing, "grp", near)
    other = block_of(me ^ 2, width).astype(jnp.float32) + incoming[1].astype(jnp.float32)
    arrived = lax.ppermute(other.astype(jnp.bfloat16), "grp", far)
    own = block_of(me, width).astype(jnp.float32) + incoming[0].astype(jnp.float32)
    return own + arrived.astype(jnp.float32)


def grp_all_gather(block):
    parts = lax.axis_size("grp")
    if parts != 4:
        return lax.all_gather(block, "grp", axis=1, tiled=True)
    me = lax.axis_index("grp")
    near = [(i, i ^ 1) for i in range(parts)]
    far = [(i, i ^ 2) for i in range(parts)]
    beside = lax.ppermute(block, "grp", near)
    across = lax.ppermute(block, "grp", far)
    diagonal = lax.ppermute(across, "grp", near)
    held = jnp.stack([block, beside, across, diagonal])
    pieces = [lax.dynamic_index_in_dim(held, k ^ me, 0, keepdims=False) for k in range(parts)]
    return jnp.concatenate(pieces, axis=1)


def finish(attn_rows, resid_rows, out_weight, norm_gain, gate_weight, up_weight, down_weight):
    partial_value = jnp.dot(attn_rows, out_weight, preferred_element_type=jnp.float32)
    proj_cols = grp_reduce_scatter(partial_value.astype(jnp.bfloat16))
    state_cols = (resid_rows.astype(jnp.float32) + proj_cols).astype(jnp.bfloat16)
    state_full = grp_all_gather(state_cols)
    state32 = state_full.astype(jnp.float32)
    normed = (
        state32 * lax.rsqrt(jnp.mean(state32 * state32, axis=1, keepdims=True) + 1e-05) * norm_gain
    ).astype(jnp.bfloat16)
    gate = jnp.dot(normed, gate_weight, preferred_element_type=jnp.float32)
    upval = jnp.dot(normed, up_weight, preferred_element_type=jnp.float32)
    inner = (jax.nn.silu(gate) * upval).astype(jnp.bfloat16)
    down_cols = grp_reduce_scatter_blocks(
        lambda index, width: jnp.dot(
            inner, grp_block(down_weight, index, width), preferred_element_type=jnp.float32
        ).astype(jnp.bfloat16),
        down_weight.shape[1],
    )
    return (state_cols.astype(jnp.float32) + down_cols).astype(jnp.bfloat16)


def shards(
    residual,
    queries,
    new_keys,
    new_values,
    pool_keys,
    pool_values,
    cache_len,
    prefix_group,
    prefix_len,
    span_rows,
    span_offset,
    out_weight,
    norm_gain,
    gate_weight,
    up_weight,
    down_weight,
):
    total_rows = residual.shape[0]
    width = residual.shape[1]
    device = lax.axis_index("req")
    devices = lax.axis_size("req")
    bucket = (total_rows - DEC + devices - 1) // devices
    spread = bucket * devices
    bal = total_rows // 2
    counts = DEC + span_rows
    ends = jnp.cumsum(counts)
    firsts = ends - counts
    first = firsts[device]
    own_count = counts[device]
    shift = first % devices

    def outbound(rows):
        grid = rows[:spread].reshape(bucket, devices, rows.shape[1])
        return jnp.transpose(jnp.roll(grid, shift, axis=1), (1, 0, 2))

    send_resid = outbound(residual)
    got_resid = lax.all_to_all(send_resid, "req", split_axis=0, concat_axis=0, tiled=True)
    decode_mask = build_decode_mask(cache_len, prefix_group, prefix_len)
    sent_parts = attention_parts(
        queries, new_keys, new_values, pool_keys, pool_values, decode_mask, span_offset[0], outbound
    )
    got_resid, sent_parts[-1] = lax.optimization_barrier((got_resid, sent_parts[-1]))
    got_parts = [
        lax.all_to_all(part, "req", split_axis=0, concat_axis=0, tiled=True)
        for part in sent_parts
    ]

    slots = jnp.arange(bal, dtype=jnp.int32)
    wanted = slots * devices + device
    src_dev = jnp.sum((ends[None, :] <= wanted[:, None]).astype(jnp.int32), axis=1)
    src_dev = jnp.minimum(src_dev, devices - 1)
    src_pos = jnp.clip((wanted - firsts[src_dev]) // devices, 0, bucket - 1)
    flat_idx = src_dev * bucket + src_pos
    dense_attn = jnp.concatenate(
        [got.reshape(spread, got.shape[2])[flat_idx] for got in got_parts], axis=1
    )
    dense_resid = got_resid.reshape(spread, width)[flat_idx]
    mixed = finish(
        dense_attn, dense_resid, out_weight, norm_gain, gate_weight, up_weight, down_weight
    )
    lane = (device - firsts) % devices
    row_of = jnp.arange(bucket, dtype=jnp.int32)[None, :] * devices + lane[:, None]
    back_valid = row_of < counts[:, None]
    back_start = (firsts + lane) // devices
    padded = jnp.concatenate([mixed, jnp.zeros((bucket, width), mixed.dtype)], axis=0)
    slabs = jnp.stack(
        [lax.dynamic_slice_in_dim(padded, back_start[k], bucket, 0) for k in range(devices)]
    )
    picked = jnp.where(back_valid[:, :, None], slabs, jnp.zeros((), slabs.dtype))
    returned = lax.all_to_all(picked, "req", split_axis=0, concat_axis=0, tiled=True)
    restored = jnp.roll(jnp.transpose(returned, (1, 0, 2)), -shift, axis=1).reshape(spread, width)
    if spread < total_rows:
        restored = jnp.concatenate(
            [restored, jnp.zeros((total_rows - spread, width), restored.dtype)], axis=0
        )
    return restored


def solution(mesh):
    placed = (
        P("req", "grp"),
        P("req", "grp"),
        P("req", "grp"),
        P("req", "grp"),
        P("req", "grp"),
        P("req", "grp"),
        P("req"),
        P("req"),
        P("req"),
        P(),
        P("req"),
        P("grp", None),
        P(),
        P(None, "grp"),
        P(None, "grp"),
        P("grp", None),
    )
    return jax.shard_map(
        shards, mesh=mesh, in_specs=placed, out_specs=P("req", "grp"), check_vma=False
    )
```
